32 devices in a mesh: dom: 8 (over z, y), rep: 4 (over x, core).
Axes of the slice: x: 2, y: 2, z: 4, core: 2. Of those that a mesh axis runs over, the one named last changes fastest.
Arguments:
- rhs: float32 [256, 32, 128], P(('dom', 'rep')), may hold values from -15 to 15
- precond: float32 [256, 128], P(('dom', 'rep')), may hold values from 0.25 to 1
- diag_tiles: bfloat16 [256, 128, 128], P(('dom', 'rep')), may hold values from -0.08 to 6.08
- off_tiles: bfloat16 [256, 2, 128, 128], P(('dom', 'rep')), may hold values from -0.119628906 to 0.119628906
- off_cols: int32 [256, 2], P(('dom', 'rep')), may hold values from 0 to 7
- link_tiles: bfloat16 [32, 128, 128], P(('dom', 'rep')), may hold values from -0.19921875 to 0.19921875
- contact_tiles: bfloat16 [512, 128, 128], P(('dom', 'rep')), may hold values from -0.29882812 to 0.29882812
- contact_owner: int32 [512, 1], P(('dom', 'rep')), may hold values from 0 to 3; in each aligned block of 16 rows (0 to 15, 16 to 31, ...) at most 8 rows name the same one
- contact_anode: int32 [512], P(('dom', 'rep')), may hold values from 0 to 7
- contact_bnode: int32 [512], P(('dom', 'rep')), may hold values from 0 to 7
Outputs:
- solution: float32 [256, 32, 128], P(('dom', 'rep'))
- residual: float32 [256, 32, 128], P(('dom', 'rep'))
The draws below stay inside these ranges and needn't reach their ends.
Inputs may be any that keep to these rules, and one draw needn't show every extreme that they name: `contact_owner`: among the rows of one device no rep index is named by more than 8 rows.
All inputs are finite; a program needn't handle non-finite values.
Results may differ from the reference program's by a relative error of at most 0.03.
Values may be sent and summed in bfloat16 or wider, within the bound.
No kernel may reach another device: no remote copies, remote signals or barrier semaphores. Data moves between devices by JAX's collectives and lax.ppermute only.
A program may use at most 64 MiB of HBM per device.

```python
import math
import jax
import jax.numpy as jnp
import numpy as np
from jax import lax

B = 128
R = 32
NB = 8
NNZ = 2
TILES = 16
ITERS = 4
CAP = 8
NODES = 256
CONTACTS = 512
N_DOM = 8
N_REP = 4


def draw_rhs(key, part):
    ramp = 1.0 + 2.0 * jnp.arange(NODES, dtype=jnp.float32) / NODES
    base = jnp.clip(jax.random.normal(key, (NODES, R, B), jnp.float32), -5.0, 5.0)
    return base * ramp[:, None, None]


def draw_diag_tiles(key, part):
    noise = 0.02 * jnp.clip(jax.random.normal(key, (NODES, B, B), jnp.float32), -4.0, 4.0)
    symmetric = 0.5 * (noise + jnp.swapaxes(noise, 1, 2))
    level = jax.random.uniform(jax.random.fold_in(key, 3), (NODES, 1, 1), jnp.float32, 3.0, 6.0)
    return (level * jnp.eye(B, dtype=jnp.float32)[None] + symmetric).astype(jnp.bfloat16)


def plant(values, rng, least, largest):
    index_at = [jax.random.randint(jax.random.fold_in(rng, axis), (), 0, length) for axis, length in enumerate(values.shape)]
    widest = values.shape.index(max(values.shape))
    beside = index_at[:widest] + [(index_at[widest] + 1) % values.shape[widest]] + index_at[widest + 1:]
    return values.at[tuple(index_at)].set(least).at[tuple(beside)].set(largest)


def block_levels(stream_key, dims, pieces, least, largest):
    factor_of, own = 1.0, jax.random.fold_in(stream_key, 6)
    for axis_at, blocks in pieces:
        heights = jnp.exp(jax.random.uniform(jax.random.fold_in(own, axis_at), (blocks,), jnp.float32, least / len(pieces), largest / len(pieces)))
        factor_of = factor_of * jnp.repeat(heights, dims[axis_at] // blocks).reshape([-1 if axis == axis_at else 1 for axis in range(len(dims))])
    return factor_of


def routed_block(rng, own, number, rows, count, top, reach, lean):
    order = jax.random.permutation(rng, count)
    heavy_load, ordinary = load_shares(count, rows * top, reach, lean, True), load_shares(count, rows * top, reach, lean, False)
    places = jnp.arange(count)

    def named(lengths, offset_by):
        used = int((lengths > 0).sum())
        fixed = max(1, used // 4)
        shifted = fixed + (places - fixed + offset_by * (used - fixed)) % max(1, count - fixed)
        return jnp.zeros((count,), jnp.int32).at[order[jnp.where(places < fixed, places, shifted)]].set(jnp.asarray(lengths, jnp.int32))

    lengths = jnp.where(number % 4 == 0, named(heavy_load, number // 4), named(ordinary, number - number // 4 - 1))
    mixed = jax.random.permutation(jax.random.fold_in(own, 3), count)
    source_of, taker = mixed[0:count // 2 * 2:2], mixed[1:count // 2 * 2:2]
    room = jnp.minimum(lengths[source_of] - 1, reach - lengths[taker]) // 2
    room = jnp.where((source_of == order[0]) | (taker == order[0]) | (lengths[taker] == 0), 0, jnp.maximum(room, 0))
    shifted = jax.random.randint(jax.random.fold_in(own, 4), (count // 2,), 0, 1 << 20) % (room + 1)
    lengths = lengths.at[source_of].add(-shifted).at[taker].add(shifted)
    labels = jnp.searchsorted(jnp.cumsum(lengths), jnp.arange(rows * top), side="right").astype(jnp.int32)
    table = labels.reshape(top, rows).T
    table = table[jax.random.permutation(jax.random.fold_in(own, 1), rows)]
    offset_by = jax.random.randint(jax.random.fold_in(own, 2), (rows, 1), 0, top)
    return jnp.take_along_axis(table, (jnp.arange(top)[None, :] + offset_by) % top, axis=1)


def load_shares(number_of, total, reach, lean, full):
    weights = [(1 << 20) // math.isqrt(standing ** lean) + 1 for standing in range(1, number_of + 1)]
    largest = reach if full else min(reach, max(-(-total // number_of), total * weights[0] // sum(weights)))
    least = 1 if total - largest >= number_of - 1 else 0
    holding, surplus = [largest] + [least] * (number_of - 1), total - largest - least * (number_of - 1)
    while surplus > 0:
        free = [i for i in range(1, number_of) if holding[i] < largest] or [i for i in range(1, number_of) if holding[i] < reach]
        whole, left = sum([weights[i] for i in free]), surplus
        for i in free:
            addition = min(reach - holding[i], max(1, left * weights[i] // whole), surplus)
            holding[i] = holding[i] + addition
            surplus = surplus - addition
    return np.array(holding)


def normal_values(rng, extent, width, most, pieces=(), kind=jnp.bfloat16):
    factor_of = block_levels(rng, extent, pieces, -0.22, 0.18) if pieces else 1.0
    values = jax.random.normal(rng, extent, jnp.float32) * width * factor_of
    return jnp.minimum(jnp.maximum(values, -most), most).astype(kind)


def setup_inputs(seed: int = 0) -> dict:
    key_list = jax.random.split(jax.random.key(seed), 11)
    rhs = draw_rhs(jax.random.fold_in(key_list[10], 71), 0)
    precond = jnp.clip(jnp.exp(math.log(1.0) - 1.3862944 * jax.random.uniform(key_list[1], (NODES, B), jnp.float32) ** block_levels(key_list[1], (NODES, B), ((0, 32),), -0.2, 0.2)), 0.25, 1.0)
    diag_tiles = draw_diag_tiles(jax.random.fold_in(key_list[10], 71), 0)
    off_tiles = normal_values(key_list[3], (NODES, NNZ, B, B), 0.03, 0.119628906, ((0, 32),))
    off_cols = plant(jax.random.randint(key_list[4], (NODES, NNZ), 0, NB), jax.random.fold_in(key_list[4], 1), 0, NB - 1).astype(jnp.int32)
    link_tiles = normal_values(key_list[5], (N_DOM * N_REP, B, B), 0.05, 0.19921875, ((0, 32),))
    contact_tiles = normal_values(key_list[6], (CONTACTS, B, B), 0.06, 0.29882812, ((0, 32),))
    contact_owner_keys = jax.random.split(jax.random.fold_in(key_list[7], 1), CONTACTS // TILES)
    contact_owner_turns = jax.random.permutation(jax.random.fold_in(key_list[7], 3), CONTACTS // TILES)
    contact_owner = jax.vmap(lambda own, number: routed_block(jax.random.fold_in(key_list[7], 2), own, number, TILES, N_REP, 1, CAP, 2))(contact_owner_keys, contact_owner_turns).reshape((CONTACTS, 1))
    contact_anode = plant(jax.random.randint(key_list[8], (CONTACTS,), 0, NB), jax.random.fold_in(key_list[8], 1), 0, NB - 1).astype(jnp.int32)
    contact_bnode = plant(jax.random.randint(key_list[9], (CONTACTS,), 0, NB), jax.random.fold_in(key_list[9], 1), 0, NB - 1).astype(jnp.int32)
    return dict(rhs=rhs, precond=precond, diag_tiles=diag_tiles, off_tiles=off_tiles, off_cols=off_cols, link_tiles=link_tiles, contact_tiles=contact_tiles, contact_owner=contact_owner, contact_anode=contact_anode, contact_bnode=contact_bnode)


def rounded_back(values):
    return lax.optimization_barrier(values.astype(jnp.bfloat16)).astype(jnp.float32)


def node_stiffness(inputs):
    block, diag_block, off_block, col_block = inputs
    result = jnp.einsum('nrk,nkj->nrj', block, diag_block.astype(jnp.float32))
    off_wide = off_block.astype(jnp.float32)
    picked = block[col_block]
    result = result + jnp.einsum('nmrk,nmkj->nrj', picked, off_wide)
    mirror = jnp.einsum('nrk,nmjk->nmrj', block, off_wide)
    mirror = mirror.reshape(NB * NNZ, R, B)
    return result + jax.ops.segment_sum(mirror, col_block.reshape(-1), num_segments=NB)


def apply_operator(vector, diag_tiles, off_tiles, off_cols, link_tiles, contact_tiles, near_glob, far_glob):
    devs = N_DOM * N_REP
    rounded = rounded_back(vector)
    blocks = rounded.reshape(devs, NB, R, B)
    result = lax.map(node_stiffness, (blocks, diag_tiles.reshape(devs, NB, B, B), off_tiles.reshape(devs, NB, NNZ, B, B), off_cols.reshape(devs, NB, NNZ)))
    grid = blocks.reshape(N_DOM, N_REP, NB, R, B)
    links = link_tiles.astype(jnp.float32).reshape(N_DOM, N_REP, B, B)
    before = jnp.roll(grid[:, :, NB - 1], 1, axis=1)
    first_add = jnp.einsum('dark,dakj->darj', before, links)
    back_term = jnp.einsum('dark,dajk->darj', grid[:, :, 0], links)
    last_add = jnp.roll(back_term, -1, axis=1)
    result = result.reshape(N_DOM, N_REP, NB, R, B)
    result = result.at[:, :, 0].add(first_add)
    result = result.at[:, :, NB - 1].add(last_add)
    result = result.reshape(devs * NB, R, B)
    contact_blocks = contact_tiles.reshape(devs, TILES, B, B)

    def one_device(total, inputs):
        tile_block, near_block, far_block = inputs
        difference = rounded_back(vector[near_block] - vector[far_block])
        wide_tiles = tile_block.astype(jnp.float32)
        multiplier = rounded_back(jnp.einsum('trk,tkj->trj', difference, wide_tiles))
        terms = jnp.einsum('trj,tkj->trk', multiplier, wide_tiles)
        total = total.at[near_block].add(terms)
        total = total.at[far_block].add(-terms)
        return total, None

    result, _ = lax.scan(one_device, result, (contact_blocks, near_glob.reshape(devs, TILES), far_glob.reshape(devs, TILES)))
    return result


def reference(rhs, precond, diag_tiles, off_tiles, off_cols, link_tiles, contact_tiles, contact_owner, contact_anode, contact_bnode):
    count = N_DOM * N_REP * TILES
    source = jnp.arange(count, dtype=jnp.int32) // TILES
    body_dom = source // N_REP
    partner_dom = body_dom + 1 - 2 * (body_dom % 2)
    owner_rep = contact_owner[:, 0].astype(jnp.int32)
    near_glob = ((body_dom * N_REP + owner_rep) * NB + contact_anode).astype(jnp.int32)
    far_glob = ((partner_dom * N_REP + owner_rep) * NB + contact_bnode).astype(jnp.int32)
    scale = precond[:, None, :]
    solution = jnp.zeros_like(rhs)
    residual = rhs
    preconditioned = scale * residual
    direction = preconditioned
    res_dot = jnp.sum(residual * preconditioned, axis=(0, 2))
    for step in range(ITERS):
        image = apply_operator(direction, diag_tiles, off_tiles, off_cols, link_tiles, contact_tiles, near_glob, far_glob)
        alpha = res_dot / jnp.sum(direction * image, axis=(0, 2))
        solution = solution + alpha[None, :, None] * direction
        residual = residual - alpha[None, :, None] * image
        preconditioned = scale * residual
        next_dot = jnp.sum(residual * preconditioned, axis=(0, 2))
        direction = preconditioned + (next_dot / res_dot)[None, :, None] * direction
        res_dot = next_dot
    return solution, residual
```

```python
import jax
import jax.numpy as jnp
from jax import lax
from jax.sharding import PartitionSpec as P

B = 128
ITERS = 4
CAP = 8


def from_behind(value, axis, steps):
    count = lax.axis_size(axis)
    pairs = [(source, (source + steps) % count) for source in range(count)]
    return lax.ppermute(value, axis, pairs)


def partner(value, axis, distance):
    return lax.ppermute(value, axis, [(i, i ^ 1 << distance) for i in range(lax.axis_size(axis))])


def total(value):
    count = lax.axis_size("dom") * lax.axis_size("rep")
    spread = jnp.broadcast_to(value[None], (count,) + value.shape)
    gathered = lax.all_to_all(spread, ("dom", "rep"), 0, 0, tiled=True)
    return jnp.sum(gathered, axis=0)


def local_stiffness(rounded, diag_tiles, off_tiles, off_cols):
    nodes = rounded.shape[0]
    result = jnp.einsum("nrk,nkj->nrj", rounded, diag_tiles, preferred_element_type=jnp.float32)
    picked = rounded[off_cols]
    result = result + jnp.einsum(
        "nmrk,nmkj->nrj", picked, off_tiles, preferred_element_type=jnp.float32
    )
    mirror = jnp.einsum("nrk,nmjk->nmrj", rounded, off_tiles, preferred_element_type=jnp.float32)
    flat_cols = off_cols.reshape(-1)
    onehot = (flat_cols[:, None] == jnp.arange(nodes, dtype=jnp.int32)[None, :]).astype(jnp.float32)
    mirror = mirror.reshape(flat_cols.shape[0], rounded.shape[1], rounded.shape[2])
    return result + jnp.einsum("pn,prj->nrj", onehot, mirror, precision=lax.Precision.HIGHEST)


def contact_pairs(vector, other, near_index, far_index, contact_set):
    difference = (vector[near_index] - other[far_index]).astype(jnp.bfloat16)
    multiplier = jnp.einsum(
        "srk,skj->srj", difference, contact_set, preferred_element_type=jnp.float32
    ).astype(jnp.bfloat16)
    return jnp.einsum("srj,skj->srk", multiplier, contact_set, preferred_element_type=jnp.float32)


def collect(values, index, nodes):
    onehot = (index[:, None] == jnp.arange(nodes, dtype=jnp.int32)[None, :]).astype(jnp.float32)
    return jnp.einsum("sn,srk->nrk", onehot, values, precision=lax.Precision.HIGHEST)


def apply_operator(
    vector, diag_tiles, off_tiles, off_cols, link_tile, contact_set, near_index, far_index
):
    nodes = vector.shape[0]
    rounded = vector.astype(jnp.bfloat16)
    result = local_stiffness(rounded, diag_tiles, off_tiles, off_cols)
    before = from_behind(rounded[nodes - 1], "rep", 1)
    first_add = jnp.dot(before, link_tile, preferred_element_type=jnp.float32)
    back_term = lax.dot_general(
        rounded[0], link_tile, (((1,), (1,)), ((), ())), preferred_element_type=jnp.float32
    )
    after = from_behind(back_term, "rep", -1)
    result = result.at[0].add(first_add)
    result = result.at[nodes - 1].add(after)
    other = partner(vector.astype(jnp.bfloat16), "dom", 0).astype(vector.dtype)
    terms = contact_pairs(vector, other, near_index, far_index, contact_set)
    result = result + collect(terms, near_index, nodes)
    far_terms = partner(collect(terms, far_index, nodes).astype(jnp.bfloat16), "dom", 0).astype(
        jnp.float32
    )
    result = result - far_terms
    return result


def body(
    rhs,
    precond,
    diag_tiles,
    off_tiles,
    off_cols,
    link_tiles,
    contact_tiles,
    contact_owner,
    contact_anode,
    contact_bnode,
):
    groups = lax.axis_size("rep")
    target = contact_owner[:, 0]
    choose = (target[:, None] == jnp.arange(groups, dtype=jnp.int32)[None, :]).astype(jnp.int32)
    rank = jnp.sum((jnp.cumsum(choose, axis=0) - choose) * choose, axis=1)
    send_set = jnp.zeros((groups, CAP, B, B), jnp.bfloat16).at[target, rank].set(contact_tiles)
    labels = jnp.stack([contact_anode, contact_bnode], axis=1)
    send_labels = jnp.zeros((groups, CAP, 2), jnp.int32).at[target, rank].set(labels)
    got_set, got_labels = (
        lax.all_to_all(send_set, "rep", split_axis=0, concat_axis=0, tiled=True),
        lax.all_to_all(send_labels, "rep", split_axis=0, concat_axis=0, tiled=True),
    )
    slots = groups * CAP
    contact_set = got_set.reshape(slots, B, B)
    got_labels = got_labels.reshape(slots, 2)
    near_index = got_labels[:, 0]
    far_index = got_labels[:, 1]
    link_tile = link_tiles[0]
    scale = precond[:, None, :]
    solution = jnp.zeros_like(rhs)
    residual = rhs
    preconditioned = scale * residual
    direction = preconditioned
    res_dot = total(jnp.sum(residual * preconditioned, axis=(0, 2)))
    for step in range(ITERS):
        image = apply_operator(
            direction,
            diag_tiles,
            off_tiles,
            off_cols,
            link_tile,
            contact_set,
            near_index,
            far_index,
        )
        curve = total(jnp.sum(direction * image, axis=(0, 2)))
        alpha = res_dot / curve
        solution = solution + alpha[None, :, None] * direction
        residual = residual - alpha[None, :, None] * image
        preconditioned = scale * residual
        next_dot = total(jnp.sum(residual * preconditioned, axis=(0, 2)))
        direction = preconditioned + (next_dot / res_dot)[None, :, None] * direction
        res_dot = next_dot
    return (solution, residual)


def solution(mesh):
    in_specs = (
        P(("dom", "rep"), None, None),
        P(("dom", "rep"), None),
        P(("dom", "rep"), None, None),
        P(("dom", "rep"), None, None, None),
        P(("dom", "rep"), None),
        P(("dom", "rep"), None, None),
        P(("dom", "rep"), None, None),
        P(("dom", "rep"), None),
        P(("dom", "rep")),
        P(("dom", "rep")),
    )
    out_specs = (P(("dom", "rep"), None, None), P(("dom", "rep"), None, None))
    return jax.shard_map(body, mesh=mesh, in_specs=in_specs, out_specs=out_specs, check_vma=False)
```

```python
import jax
import jax.numpy as jnp
from jax import lax
from jax.sharding import PartitionSpec as P

B = 128
ITERS = 4
CAP = 8


def from_behind(value, axis, steps):
    count = lax.axis_size(axis)
    pairs = [(source, (source + steps) % count) for source in range(count)]
    return lax.ppermute(value, axis, pairs)


def partner(value, axis, distance):
    return lax.ppermute(value, axis, [(i, i ^ 1 << distance) for i in range(lax.axis_size(axis))])


def total(value):
    count = lax.axis_size("dom") * lax.axis_size("rep")
    spread = jnp.broadcast_to(value[None], (count,) + value.shape)
    gathered = lax.all_to_all(spread, ("dom", "rep"), 0, 0, tiled=True)
    return jnp.sum(gathered, axis=0)


def local_stiffness(rounded, diag_tiles, off_tiles, off_cols):
    nodes = rounded.shape[0]
    result = jnp.einsum("nrk,nkj->nrj", rounded, diag_tiles, preferred_element_type=jnp.float32)
    picked = rounded[off_cols]
    result = result + jnp.einsum(
        "nmrk,nmkj->nrj", picked, off_tiles, preferred_element_type=jnp.float32
    )
    mirror = jnp.einsum("nrk,nmjk->nmrj", rounded, off_tiles, preferred_element_type=jnp.float32)
    flat_cols = off_cols.reshape(-1)
    onehot = (flat_cols[:, None] == jnp.arange(nodes, dtype=jnp.int32)[None, :]).astype(jnp.float32)
    mirror = mirror.reshape(flat_cols.shape[0], rounded.shape[1], rounded.shape[2])
    return result + jnp.einsum("pn,prj->nrj", onehot, mirror, precision=lax.Precision.HIGHEST)


def contact_pairs(vector, other, near_index, far_index, contact_set):
    difference = (vector[near_index] - other[far_index]).astype(jnp.bfloat16)
    multiplier = jnp.einsum(
        "srk,skj->srj", difference, contact_set, preferred_element_type=jnp.float32
    ).astype(jnp.bfloat16)
    return jnp.einsum("srj,skj->srk", multiplier, contact_set, preferred_element_type=jnp.float32)


def collect(values, index, nodes):
    onehot = (index[:, None] == jnp.arange(nodes, dtype=jnp.int32)[None, :]).astype(jnp.float32)
    return jnp.einsum("sn,srk->nrk", onehot, values, precision=lax.Precision.HIGHEST)


def apply_operator(
    vector, diag_tiles, off_tiles, off_cols, link_tile, contact_set, near_index, far_index
):
    nodes = vector.shape[0]
    rounded = vector.astype(jnp.bfloat16)
    result = local_stiffness(rounded, diag_tiles, off_tiles, off_cols)
    before = from_behind(rounded[nodes - 1], "rep", 1)
    first_add = jnp.dot(before, link_tile, preferred_element_type=jnp.float32)
    back_term = lax.dot_general(
        rounded[0], link_tile, (((1,), (1,)), ((), ())), preferred_element_type=jnp.float32
    )
    after = from_behind(back_term, "rep", -1)
    result = result.at[0].add(first_add)
    result = result.at[nodes - 1].add(after)
    other = partner(vector.astype(jnp.bfloat16), "dom", 0).astype(vector.dtype)
    terms = contact_pairs(vector, other, near_index, far_index, contact_set)
    result = result + collect(terms, near_index, nodes)
    far_terms = partner(collect(terms, far_index, nodes).astype(jnp.bfloat16), "dom", 0).astype(
        jnp.float32
    )
    result = result - far_terms
    return result


def body(
    rhs,
    precond,
    diag_tiles,
    off_tiles,
    off_cols,
    link_tiles,
    contact_tiles,
    contact_owner,
    contact_anode,
    contact_bnode,
):
    groups = lax.axis_size("rep")
    tiles = contact_tiles.shape[0]
    slots = groups * CAP
    target = contact_owner[:, 0]
    choose = (target[:, None] == jnp.arange(groups, dtype=jnp.int32)[None, :]).astype(jnp.int32)
    rank = jnp.sum((jnp.cumsum(choose, axis=0) - choose) * choose, axis=1)
    slot_of = target * CAP + rank
    pick = (slot_of[None, :] == jnp.arange(slots, dtype=jnp.int32)[:, None]).astype(jnp.bfloat16)
    send_set = jnp.einsum(
        "sc,cij->sij", pick, contact_tiles, preferred_element_type=jnp.float32
    ).astype(jnp.bfloat16)
    labels = jnp.stack([contact_anode, contact_bnode], axis=1)
    wide = jnp.concatenate([labels // 256, labels % 256], axis=1).astype(jnp.bfloat16)
    send_labels = jnp.einsum("sc,cl->sl", pick, wide, preferred_element_type=jnp.float32)
    extra = jnp.zeros((slots, 16, B), jnp.float32).at[:, 0, :4].set(send_labels)
    payload = jnp.concatenate([send_set, extra.astype(jnp.bfloat16)], axis=1)
    got = lax.all_to_all(
        payload.reshape(groups, CAP, B + 16, B), "rep", split_axis=0, concat_axis=0, tiled=True
    ).reshape(slots, B + 16, B)
    contact_set = got[:, :B]
    got_labels = got[:, B, :4].astype(jnp.int32)
    got_labels = got_labels[:, :2] * 256 + got_labels[:, 2:]
    near_index = got_labels[:, 0]
    far_index = got_labels[:, 1]
    link_tile = link_tiles[0]
    scale = precond[:, None, :]
    solution = jnp.zeros_like(rhs)
    residual = rhs
    preconditioned = scale * residual
    direction = preconditioned
    res_dot = jnp.sum(residual * preconditioned, axis=(0, 2))
    for step in range(ITERS):
        image = apply_operator(
            direction,
            diag_tiles,
            off_tiles,
            off_cols,
            link_tile,
            contact_set,
            near_index,
            far_index,
        )
        curve = jnp.sum(direction * image, axis=(0, 2))
        if step == 0:
            both = total(jnp.stack([res_dot, curve]))
            res_dot, curve = both[0], both[1]
        else:
            curve = total(curve)
        alpha = res_dot / curve
        solution = solution + alpha[None, :, None] * direction
        residual = residual - alpha[None, :, None] * image
        preconditioned = scale * residual
        next_dot = total(jnp.sum(residual * preconditioned, axis=(0, 2)))
        direction = preconditioned + (next_dot / res_dot)[None, :, None] * direction
        res_dot = next_dot
    return (solution, residual)


def solution(mesh):
    in_specs = (
        P(("dom", "rep"), None, None),
        P(("dom", "rep"), None),
        P(("dom", "rep"), None, None),
        P(("dom", "rep"), None, None, None),
        P(("dom", "rep"), None),
        P(("dom", "rep"), None, None),
        P(("dom", "rep"), None, None),
        P(("dom", "rep"), None),
        P(("dom", "rep")),
        P(("dom", "rep")),
    )
    out_specs = (P(("dom", "rep"), None, None), P(("dom", "rep"), None, None))
    return jax.shard_map(body, mesh=mesh, in_specs=in_specs, out_specs=out_specs, check_vma=False)
```

```python
import jax
import jax.numpy as jnp
from jax import lax
from jax.sharding import PartitionSpec as P

B = 128
ITERS = 4
CAP = 8


def from_behind(value, axis, steps):
    count = lax.axis_size(axis)
    pairs = [(source, (source + steps) % count) for source in range(count)]
    return lax.ppermute(value, axis, pairs)


def partner(value, axis, distance):
    return lax.ppermute(value, axis, [(i, i ^ 1 << distance) for i in range(lax.axis_size(axis))])


def total(value):
    count = lax.axis_size("dom") * lax.axis_size("rep")
    spread = jnp.broadcast_to(value[None], (count,) + value.shape)
    gathered = lax.all_to_all(spread, ("dom", "rep"), 0, 0, tiled=True)
    return jnp.sum(gathered, axis=0)


def local_stiffness(rounded, diag_tiles, off_tiles, off_cols):
    nodes = rounded.shape[0]
    result = jnp.einsum("nrk,nkj->nrj", rounded, diag_tiles, preferred_element_type=jnp.float32)
    picked = rounded[off_cols]
    result = result + jnp.einsum(
        "nmrk,nmkj->nrj", picked, off_tiles, preferred_element_type=jnp.float32
    )
    mirror = jnp.einsum("nrk,nmjk->nmrj", rounded, off_tiles, preferred_element_type=jnp.float32)
    flat_cols = off_cols.reshape(-1)
    onehot = (flat_cols[:, None] == jnp.arange(nodes, dtype=jnp.int32)[None, :]).astype(jnp.float32)
    mirror = mirror.reshape(flat_cols.shape[0], rounded.shape[1], rounded.shape[2])
    return result + jnp.einsum("pn,prj->nrj", onehot, mirror, precision=lax.Precision.HIGHEST)


def contact_pairs(vector, other, near_index, far_index, contact_set):
    difference = (vector[near_index] - other[far_index]).astype(jnp.bfloat16)
    multiplier = jnp.einsum(
        "srk,skj->srj", difference, contact_set, preferred_element_type=jnp.float32
    ).astype(jnp.bfloat16)
    return jnp.einsum("srj,skj->srk", multiplier, contact_set, preferred_element_type=jnp.float32)


def collect(values, index, nodes):
    onehot = (index[:, None] == jnp.arange(nodes, dtype=jnp.int32)[None, :]).astype(jnp.float32)
    return jnp.einsum("sn,srk->nrk", onehot, values, precision=lax.Precision.HIGHEST)


def apply_operator(
    vector, diag_tiles, off_tiles, off_cols, link_tile, contact_set, near_index, far_index
):
    nodes = vector.shape[0]
    rounded = vector.astype(jnp.bfloat16)
    result = local_stiffness(rounded, diag_tiles, off_tiles, off_cols)
    before = from_behind(rounded[nodes - 1], "rep", 1)
    first_add = jnp.dot(before, link_tile, preferred_element_type=jnp.float32)
    back_term = lax.dot_general(
        rounded[0], link_tile, (((1,), (1,)), ((), ())), preferred_element_type=jnp.float32
    )
    after = from_behind(back_term, "rep", -1)
    result = result.at[0].add(first_add)
    result = result.at[nodes - 1].add(after)
    other = partner(vector.astype(jnp.bfloat16), "dom", 0).astype(vector.dtype)
    terms = contact_pairs(vector, other, near_index, far_index, contact_set)
    result = result + collect(terms, near_index, nodes)
    far_terms = partner(collect(terms, far_index, nodes).astype(jnp.bfloat16), "dom", 0).astype(
        jnp.float32
    )
    result = result - far_terms
    return result


def body(
    rhs,
    precond,
    diag_tiles,
    off_tiles,
    off_cols,
    link_tiles,
    contact_tiles,
    contact_owner,
    contact_anode,
    contact_bnode,
):
    groups = lax.axis_size("rep")
    target = contact_owner[:, 0]
    choose = (target[:, None] == jnp.arange(groups, dtype=jnp.int32)[None, :]).astype(jnp.int32)
    rank = jnp.sum((jnp.cumsum(choose, axis=0) - choose) * choose, axis=1)
    send_set = jnp.zeros((groups, CAP, B, B), jnp.bfloat16).at[target, rank].set(contact_tiles)
    labels = jnp.stack([contact_anode, contact_bnode], axis=1)
    send_labels = jnp.zeros((groups, CAP, 2), jnp.int32).at[target, rank].set(labels)
    got_set, got_labels = (
        lax.all_to_all(send_set, "rep", split_axis=0, concat_axis=0, tiled=True),
        lax.all_to_all(send_labels, "rep", split_axis=0, concat_axis=0, tiled=True),
    )
    slots = groups * CAP
    contact_set = got_set.reshape(slots, B, B)
    got_labels = got_labels.reshape(slots, 2)
    near_index = got_labels[:, 0]
    far_index = got_labels[:, 1]
    link_tile = link_tiles[0]
    scale = precond[:, None, :]
    solution = jnp.zeros_like(rhs)
    residual = rhs
    preconditioned = scale * residual
    direction = preconditioned
    res_dot = jnp.sum(residual * preconditioned, axis=(0, 2))
    for step in range(ITERS):
        image = apply_operator(
            direction,
            diag_tiles,
            off_tiles,
            off_cols,
            link_tile,
            contact_set,
            near_index,
            far_index,
        )
        curve = jnp.sum(direction * image, axis=(0, 2))
        if step == 0:
            both = total(jnp.stack([res_dot, curve]))
            res_dot, curve = both[0], both[1]
        else:
            curve = total(curve)
        alpha = res_dot / curve
        solution = solution + alpha[None, :, None] * direction
        residual = residual - alpha[None, :, None] * image
        preconditioned = scale * residual
        next_dot = total(jnp.sum(residual * preconditioned, axis=(0, 2)))
        direction = preconditioned + (next_dot / res_dot)[None, :, None] * direction
        res_dot = next_dot
    return (solution, residual)


def solution(mesh):
    in_specs = (
        P(("dom", "rep"), None, None),
        P(("dom", "rep"), None),
        P(("dom", "rep"), None, None),
        P(("dom", "rep"), None, None, None),
        P(("dom", "rep"), None),
        P(("dom", "rep"), None, None),
        P(("dom", "rep"), None, None),
        P(("dom", "rep"), None),
        P(("dom", "rep")),
        P(("dom", "rep")),
    )
    out_specs = (P(("dom", "rep"), None, None), P(("dom", "rep"), None, None))
    return jax.shard_map(body, mesh=mesh, in_specs=in_specs, out_specs=out_specs, check_vma=False)
```

```python
import jax
import jax.numpy as jnp
from jax import lax
from jax.sharding import PartitionSpec as P

B = 128
ITERS = 4
CAP = 8


def from_behind(value, axis, steps):
    count = lax.axis_size(axis)
    pairs = [(source, (source + steps) % count) for source in range(count)]
    return lax.ppermute(value, axis, pairs)


def partner(value, axis, distance):
    return lax.ppermute(value, axis, [(i, i ^ 1 << distance) for i in range(lax.axis_size(axis))])


def total(value):
    count = lax.axis_size("dom") * lax.axis_size("rep")
    spread = jnp.broadcast_to(value[None], (count,) + value.shape)
    gathered = lax.all_to_all(spread, ("dom", "rep"), 0, 0, tiled=True)
    return jnp.sum(gathered, axis=0)


def local_stiffness(rounded, diag_tiles, off_tiles, off_cols):
    nodes = rounded.shape[0]
    result = jnp.einsum("nrk,nkj->nrj", rounded, diag_tiles, preferred_element_type=jnp.float32)
    picked = rounded[off_cols]
    result = result + jnp.einsum(
        "nmrk,nmkj->nrj", picked, off_tiles, preferred_element_type=jnp.float32
    )
    mirror = jnp.einsum("nrk,nmjk->nmrj", rounded, off_tiles, preferred_element_type=jnp.float32)
    flat_cols = off_cols.reshape(-1)
    onehot = (flat_cols[:, None] == jnp.arange(nodes, dtype=jnp.int32)[None, :]).astype(jnp.float32)
    mirror = mirror.reshape(flat_cols.shape[0], rounded.shape[1], rounded.shape[2])
    return result + jnp.einsum("pn,prj->nrj", onehot, mirror, precision=lax.Precision.HIGHEST)


def contact_pairs(vector, other, near_index, far_index, contact_set):
    difference = (vector[near_index] - other[far_index]).astype(jnp.bfloat16)
    multiplier = jnp.einsum(
        "srk,skj->srj", difference, contact_set, preferred_element_type=jnp.float32
    ).astype(jnp.bfloat16)
    return jnp.einsum("srj,skj->srk", multiplier, contact_set, preferred_element_type=jnp.float32)


def collect(values, index, nodes):
    onehot = (index[:, None] == jnp.arange(nodes, dtype=jnp.int32)[None, :]).astype(jnp.float32)
    return jnp.einsum("sn,srk->nrk", onehot, values, precision=lax.Precision.HIGHEST)


def apply_operator(
    vector, diag_tiles, off_tiles, off_cols, link_tile, contact_set, near_index, far_index
):
    nodes = vector.shape[0]
    rounded = vector.astype(jnp.bfloat16)
    result = local_stiffness(rounded, diag_tiles, off_tiles, off_cols)
    before = from_behind(rounded[nodes - 1], "rep", 1)
    first_add = jnp.dot(before, link_tile, preferred_element_type=jnp.float32)
    back_term = lax.dot_general(
        rounded[0], link_tile, (((1,), (1,)), ((), ())), preferred_element_type=jnp.float32
    )
    after = from_behind(back_term, "rep", -1)
    result = result.at[0].add(first_add)
    result = result.at[nodes - 1].add(after)
    other = partner(vector.astype(jnp.bfloat16), "dom", 0).astype(vector.dtype)
    terms = contact_pairs(vector, other, near_index, far_index, contact_set)
    result = result + collect(terms, near_index, nodes)
    far_terms = partner(collect(terms, far_index, nodes).astype(jnp.bfloat16), "dom", 0).astype(
        jnp.float32
    )
    result = result - far_terms
    return result


def body(
    rhs,
    precond,
    diag_tiles,
    off_tiles,
    off_cols,
    link_tiles,
    contact_tiles,
    contact_owner,
    contact_anode,
    contact_bnode,
):
    groups = lax.axis_size("rep")
    target = contact_owner[:, 0]
    choose = (target[:, None] == jnp.arange(groups, dtype=jnp.int32)[None, :]).astype(jnp.int32)
    rank = jnp.sum((jnp.cumsum(choose, axis=0) - choose) * choose, axis=1)
    send_set = jnp.zeros((groups, CAP, B, B), jnp.bfloat16).at[target, rank].set(contact_tiles)
    labels = jnp.stack([contact_anode, contact_bnode], axis=1)
    send_labels = jnp.zeros((groups, CAP, 2), jnp.int32).at[target, rank].set(labels)
    got_set, got_labels = (
        lax.all_to_all(send_set, "rep", split_axis=0, concat_axis=0, tiled=True),
        lax.all_to_all(send_labels, "rep", split_axis=0, concat_axis=0, tiled=True),
    )
    slots = groups * CAP
    contact_set = got_set.reshape(slots, B, B)
    got_labels = got_labels.reshape(slots, 2)
    near_index = got_labels[:, 0]
    far_index = got_labels[:, 1]
    link_tile = link_tiles[0]
    scale = precond[:, None, :]
    solution = jnp.zeros_like(rhs)
    residual = rhs
    preconditioned = scale * residual
    direction = preconditioned
    for step in range(ITERS):
        image = apply_operator(
            direction,
            diag_tiles,
            off_tiles,
            off_cols,
            link_tile,
            contact_set,
            near_index,
            far_index,
        )
        parts = [
            jnp.sum(direction * image, axis=(0, 2)),
            jnp.sum(residual * preconditioned, axis=(0, 2)),
        ]
        if step < ITERS - 1:
            parts.append(jnp.sum(preconditioned * image, axis=(0, 2)))
            parts.append(jnp.sum(image * (scale * image), axis=(0, 2)))
        sums = total(jnp.stack(parts))
        curve, res_dot = sums[0], sums[1]
        alpha = res_dot / curve
        solution = solution + alpha[None, :, None] * direction
        residual = residual - alpha[None, :, None] * image
        if step < ITERS - 1:
            preconditioned = scale * residual
            next_dot = res_dot - 2.0 * alpha * sums[2] + alpha * alpha * sums[3]
            direction = preconditioned + (next_dot / res_dot)[None, :, None] * direction
    return (solution, residual)


def solution(mesh):
    in_specs = (
        P(("dom", "rep"), None, None),
        P(("dom", "rep"), None),
        P(("dom", "rep"), None, None),
        P(("dom", "rep"), None, None, None),
        P(("dom", "rep"), None),
        P(("dom", "rep"), None, None),
        P(("dom", "rep"), None, None),
        P(("dom", "rep"), None),
        P(("dom", "rep")),
        P(("dom", "rep")),
    )
    out_specs = (P(("dom", "rep"), None, None), P(("dom", "rep"), None, None))
    return jax.shard_map(body, mesh=mesh, in_specs=in_specs, out_specs=out_specs, check_vma=False)
```

```python
import jax
import jax.numpy as jnp
from jax import lax
from jax.sharding import PartitionSpec as P

B = 128
ITERS = 4
CAP = 8


def from_behind(value, axis, steps):
    count = lax.axis_size(axis)
    pairs = [(source, (source + steps) % count) for source in range(count)]
    return lax.ppermute(value, axis, pairs)


def partner(value, axis, distance):
    return lax.ppermute(value, axis, [(i, i ^ 1 << distance) for i in range(lax.axis_size(axis))])


def total(value):
    count = lax.axis_size("dom") * lax.axis_size("rep")
    spread = jnp.broadcast_to(value[None], (count,) + value.shape)
    gathered = lax.all_to_all(spread, ("dom", "rep"), 0, 0, tiled=True)
    return jnp.sum(gathered, axis=0)


def local_stiffness(rounded, diag_tiles, off_tiles, off_cols):
    nodes = rounded.shape[0]
    result = jnp.einsum("nrk,nkj->nrj", rounded, diag_tiles, preferred_element_type=jnp.float32)
    picked = rounded[off_cols]
    result = result + jnp.einsum(
        "nmrk,nmkj->nrj", picked, off_tiles, preferred_element_type=jnp.float32
    )
    mirror = jnp.einsum("nrk,nmjk->nmrj", rounded, off_tiles, preferred_element_type=jnp.float32)
    flat_cols = off_cols.reshape(-1)
    onehot = (flat_cols[:, None] == jnp.arange(nodes, dtype=jnp.int32)[None, :]).astype(jnp.float32)
    mirror = mirror.reshape(flat_cols.shape[0], rounded.shape[1], rounded.shape[2])
    return result + jnp.einsum("pn,prj->nrj", onehot, mirror, precision=lax.Precision.HIGHEST)


def contact_pairs(vector, other, near_index, far_index, contact_set):
    difference = (vector[near_index] - other[far_index]).astype(jnp.bfloat16)
    multiplier = jnp.einsum(
        "srk,skj->srj", difference, contact_set, preferred_element_type=jnp.float32
    ).astype(jnp.bfloat16)
    return jnp.einsum("srj,skj->srk", multiplier, contact_set, preferred_element_type=jnp.float32)


def collect(values, index, nodes):
    onehot = (index[:, None] == jnp.arange(nodes, dtype=jnp.int32)[None, :]).astype(jnp.float32)
    return jnp.einsum("sn,srk->nrk", onehot, values, precision=lax.Precision.HIGHEST)


def apply_operator(
    vector, diag_tiles, off_tiles, off_cols, link_tile, contact_set, near_index, far_index
):
    nodes = vector.shape[0]
    rounded = vector.astype(jnp.bfloat16)
    result = local_stiffness(rounded, diag_tiles, off_tiles, off_cols)
    before = from_behind(rounded[nodes - 1], "rep", 1)
    first_add = jnp.dot(before, link_tile, preferred_element_type=jnp.float32)
    back_term = lax.dot_general(
        rounded[0], link_tile, (((1,), (1,)), ((), ())), preferred_element_type=jnp.float32
    )
    after = from_behind(back_term, "rep", -1)
    result = result.at[0].add(first_add)
    result = result.at[nodes - 1].add(after)
    other = partner(vector.astype(jnp.bfloat16), "dom", 0).astype(vector.dtype)
    terms = contact_pairs(vector, other, near_index, far_index, contact_set)
    result = result + collect(terms, near_index, nodes)
    far_terms = partner(collect(terms, far_index, nodes).astype(jnp.bfloat16), "dom", 0).astype(
        jnp.float32
    )
    result = result - far_terms
    return result


def body(
    rhs,
    precond,
    diag_tiles,
    off_tiles,
    off_cols,
    link_tiles,
    contact_tiles,
    contact_owner,
    contact_anode,
    contact_bnode,
):
    groups = lax.axis_size("rep")
    target = contact_owner[:, 0]
    choose = (target[:, None] == jnp.arange(groups, dtype=jnp.int32)[None, :]).astype(jnp.int32)
    rank = jnp.sum((jnp.cumsum(choose, axis=0) - choose) * choose, axis=1)
    slot_of = target * CAP + rank
    pick = slot_of[None, :] == jnp.arange(groups * CAP, dtype=jnp.int32)[:, None]
    send_set = jnp.einsum(
        "sc,cij->sij", pick.astype(jnp.bfloat16), contact_tiles, preferred_element_type=jnp.float32
    ).astype(jnp.bfloat16).reshape(groups, CAP, B, B)
    labels = jnp.stack([contact_anode, contact_bnode], axis=1)
    send_labels = jnp.sum(
        jnp.where(pick[:, :, None], labels[None, :, :], 0), axis=1
    ).reshape(groups, CAP, 2)
    got_set, got_labels = (
        lax.all_to_all(send_set, "rep", split_axis=0, concat_axis=0, tiled=True),
        lax.all_to_all(send_labels, "rep", split_axis=0, concat_axis=0, tiled=True),
    )
    slots = groups * CAP
    contact_set = got_set.reshape(slots, B, B)
    got_labels = got_labels.reshape(slots, 2)
    near_index = got_labels[:, 0]
    far_index = got_labels[:, 1]
    link_tile = link_tiles[0]
    scale = precond[:, None, :]
    solution = jnp.zeros_like(rhs)
    residual = rhs
    preconditioned = scale * residual
    direction = preconditioned
    for step in range(ITERS):
        image = apply_operator(
            direction,
            diag_tiles,
            off_tiles,
            off_cols,
            link_tile,
            contact_set,
            near_index,
            far_index,
        )
        parts = [
            jnp.sum(direction * image, axis=(0, 2)),
            jnp.sum(residual * preconditioned, axis=(0, 2)),
        ]
        if step < ITERS - 1:
            parts.append(jnp.sum(preconditioned * image, axis=(0, 2)))
            parts.append(jnp.sum(image * (scale * image), axis=(0, 2)))
        sums = total(jnp.stack(parts))
        curve, res_dot = sums[0], sums[1]
        alpha = res_dot / curve
        solution = solution + alpha[None, :, None] * direction
        residual = residual - alpha[None, :, None] * image
        if step < ITERS - 1:
            preconditioned = scale * residual
            next_dot = res_dot - 2.0 * alpha * sums[2] + alpha * alpha * sums[3]
            direction = preconditioned + (next_dot / res_dot)[None, :, None] * direction
    return (solution, residual)


def solution(mesh):
    in_specs = (
        P(("dom", "rep"), None, None),
        P(("dom", "rep"), None),
        P(("dom", "rep"), None, None),
        P(("dom", "rep"), None, None, None),
        P(("dom", "rep"), None),
        P(("dom", "rep"), None, None),
        P(("dom", "rep"), None, None),
        P(("dom", "rep"), None),
        P(("dom", "rep")),
        P(("dom", "rep")),
    )
    out_specs = (P(("dom", "rep"), None, None), P(("dom", "rep"), None, None))
    return jax.shard_map(body, mesh=mesh, in_specs=in_specs, out_specs=out_specs, check_vma=False)
```

```python
import jax
import jax.numpy as jnp
from jax import lax
from jax.sharding import PartitionSpec as P

B = 128
ITERS = 4
CAP = 8


def from_behind(value, axis, steps):
    count = lax.axis_size(axis)
    pairs = [(source, (source + steps) % count) for source in range(count)]
    return lax.ppermute(value, axis, pairs)


def partner(value, axis, distance):
    return lax.ppermute(value, axis, [(i, i ^ 1 << distance) for i in range(lax.axis_size(axis))])


def total(value):
    count = lax.axis_size("dom") * lax.axis_size("rep")
    spread = jnp.broadcast_to(value[None], (count,) + value.shape)
    gathered = lax.all_to_all(spread, ("dom", "rep"), 0, 0, tiled=True)
    return jnp.sum(gathered, axis=0)


def local_stiffness(rounded, diag_tiles, off_tiles, off_cols):
    nodes = rounded.shape[0]
    result = jnp.einsum("nrk,nkj->nrj", rounded, diag_tiles, preferred_element_type=jnp.float32)
    picked = rounded[off_cols]
    result = result + jnp.einsum(
        "nmrk,nmkj->nrj", picked, off_tiles, preferred_element_type=jnp.float32
    )
    mirror = jnp.einsum("nrk,nmjk->nmrj", rounded, off_tiles, preferred_element_type=jnp.float32)
    flat_cols = off_cols.reshape(-1)
    onehot = (flat_cols[:, None] == jnp.arange(nodes, dtype=jnp.int32)[None, :]).astype(jnp.float32)
    mirror = mirror.reshape(flat_cols.shape[0], rounded.shape[1], rounded.shape[2])
    return result + jnp.einsum("pn,prj->nrj", onehot, mirror, precision=lax.Precision.HIGHEST)


def contact_pairs(vector, other, near_index, far_index, contact_set):
    difference = (vector[near_index] - other[far_index]).astype(jnp.bfloat16)
    multiplier = jnp.einsum(
        "srk,skj->srj", difference, contact_set, preferred_element_type=jnp.float32
    ).astype(jnp.bfloat16)
    return jnp.einsum("srj,skj->srk", multiplier, contact_set, preferred_element_type=jnp.float32)


def collect(values, index, nodes):
    onehot = (index[:, None] == jnp.arange(nodes, dtype=jnp.int32)[None, :]).astype(jnp.float32)
    return jnp.einsum("sn,srk->nrk", onehot, values, precision=lax.Precision.HIGHEST)


def apply_operator(
    vector, diag_tiles, off_tiles, off_cols, link_tile, contact_set, near_index, far_index
):
    nodes = vector.shape[0]
    rounded = vector.astype(jnp.bfloat16)
    result = local_stiffness(rounded, diag_tiles, off_tiles, off_cols)
    before = from_behind(rounded[nodes - 1], "rep", 1)
    first_add = jnp.dot(before, link_tile, preferred_element_type=jnp.float32)
    back_term = lax.dot_general(
        rounded[0], link_tile, (((1,), (1,)), ((), ())), preferred_element_type=jnp.float32
    )
    after = from_behind(back_term, "rep", -1)
    result = result.at[0].add(first_add)
    result = result.at[nodes - 1].add(after)
    other = partner(vector.astype(jnp.bfloat16), "dom", 0).astype(vector.dtype)
    terms = contact_pairs(vector, other, near_index, far_index, contact_set)
    result = result + collect(terms, near_index, nodes)
    far_terms = partner(collect(terms, far_index, nodes).astype(jnp.bfloat16), "dom", 0).astype(
        jnp.float32
    )
    result = result - far_terms
    return result


def body(
    rhs,
    precond,
    diag_tiles,
    off_tiles,
    off_cols,
    link_tiles,
    contact_tiles,
    contact_owner,
    contact_anode,
    contact_bnode,
):
    groups = lax.axis_size("rep")
    target = contact_owner[:, 0]
    choose = (target[:, None] == jnp.arange(groups, dtype=jnp.int32)[None, :]).astype(jnp.int32)
    rank = jnp.sum((jnp.cumsum(choose, axis=0) - choose) * choose, axis=1)
    slot_of = target * CAP + rank
    pick = slot_of[None, :] == jnp.arange(groups * CAP, dtype=jnp.int32)[:, None]
    send_set = jnp.einsum(
        "sc,cij->sij", pick.astype(jnp.bfloat16), contact_tiles, preferred_element_type=jnp.float32
    ).astype(jnp.bfloat16).reshape(groups, CAP, B, B)
    labels = jnp.stack([contact_anode, contact_bnode], axis=1)
    send_labels = jnp.sum(
        jnp.where(pick[:, :, None], labels[None, :, :], 0), axis=1
    ).reshape(groups, CAP, 2)
    lane = lax.axis_index("rep")
    got_set = [jnp.take(send_set, lane, axis=0)]
    got_labels = [jnp.take(send_labels, lane, axis=0)]
    for shift in range(1, groups):
        ahead = (lane + shift) % groups
        got_set.append(from_behind(jnp.take(send_set, ahead, axis=0), "rep", shift))
        got_labels.append(from_behind(jnp.take(send_labels, ahead, axis=0), "rep", shift))
    got_set = jnp.stack(got_set)
    got_labels = jnp.stack(got_labels)
    slots = groups * CAP
    contact_set = got_set.reshape(slots, B, B)
    got_labels = got_labels.reshape(slots, 2)
    near_index = got_labels[:, 0]
    far_index = got_labels[:, 1]
    link_tile = link_tiles[0]
    scale = precond[:, None, :]
    solution = jnp.zeros_like(rhs)
    residual = rhs
    preconditioned = scale * residual
    direction = preconditioned
    for step in range(ITERS):
        image = apply_operator(
            direction,
            diag_tiles,
            off_tiles,
            off_cols,
            link_tile,
            contact_set,
            near_index,
            far_index,
        )
        parts = [
            jnp.sum(direction * image, axis=(0, 2)),
            jnp.sum(residual * preconditioned, axis=(0, 2)),
        ]
        if step < ITERS - 1:
            parts.append(jnp.sum(preconditioned * image, axis=(0, 2)))
            parts.append(jnp.sum(image * (scale * image), axis=(0, 2)))
        sums = total(jnp.stack(parts))
        curve, res_dot = sums[0], sums[1]
        alpha = res_dot / curve
        solution = solution + alpha[None, :, None] * direction
        residual = residual - alpha[None, :, None] * image
        if step < ITERS - 1:
            preconditioned = scale * residual
            next_dot = res_dot - 2.0 * alpha * sums[2] + alpha * alpha * sums[3]
            direction = preconditioned + (next_dot / res_dot)[None, :, None] * direction
    return (solution, residual)


def solution(mesh):
    in_specs = (
        P(("dom", "rep"), None, None),
        P(("dom", "rep"), None),
        P(("dom", "rep"), None, None),
        P(("dom", "rep"), None, None, None),
        P(("dom", "rep"), None),
        P(("dom", "rep"), None, None),
        P(("dom", "rep"), None, None),
        P(("dom", "rep"), None),
        P(("dom", "rep")),
        P(("dom", "rep")),
    )
    out_specs = (P(("dom", "rep"), None, None), P(("dom", "rep"), None, None))
    return jax.shard_map(body, mesh=mesh, in_specs=in_specs, out_specs=out_specs, check_vma=False)
```

```python
import jax
import jax.numpy as jnp
from jax import lax
from jax.sharding import PartitionSpec as P

B = 128
ITERS = 4
CAP = 8


def from_behind(value, axis, steps):
    count = lax.axis_size(axis)
    pairs = [(source, (source + steps) % count) for source in range(count)]
    return lax.ppermute(value, axis, pairs)


def partner(value, axis, distance):
    return lax.ppermute(value, axis, [(i, i ^ 1 << distance) for i in range(lax.axis_size(axis))])


def total(value):
    count = lax.axis_size("dom") * lax.axis_size("rep")
    spread = jnp.broadcast_to(value[None], (count,) + value.shape)
    gathered = lax.all_to_all(spread, ("dom", "rep"), 0, 0, tiled=True)
    return jnp.sum(gathered, axis=0)


def local_stiffness(rounded, diag_tiles, off_tiles, off_cols):
    nodes = rounded.shape[0]
    result = jnp.einsum("nrk,nkj->nrj", rounded, diag_tiles, preferred_element_type=jnp.float32)
    picked = rounded[off_cols]
    result = result + jnp.einsum(
        "nmrk,nmkj->nrj", picked, off_tiles, preferred_element_type=jnp.float32
    )
    mirror = jnp.einsum("nrk,nmjk->nmrj", rounded, off_tiles, preferred_element_type=jnp.float32)
    flat_cols = off_cols.reshape(-1)
    onehot = (flat_cols[:, None] == jnp.arange(nodes, dtype=jnp.int32)[None, :]).astype(jnp.float32)
    mirror = mirror.reshape(flat_cols.shape[0], rounded.shape[1], rounded.shape[2])
    return result + jnp.einsum("pn,prj->nrj", onehot, mirror, precision=lax.Precision.HIGHEST)


def apply_operator(
    vector, diag_tiles, off_tiles, off_cols, link_tile, contact_set, near_index, far_index, signs
):
    nodes = vector.shape[0]
    rounded = vector.astype(jnp.bfloat16)
    result = local_stiffness(rounded, diag_tiles, off_tiles, off_cols)
    before = from_behind(rounded[nodes - 1], "rep", 1)
    first_add = jnp.dot(before, link_tile, preferred_element_type=jnp.float32)
    back_term = lax.dot_general(
        rounded[0], link_tile, (((1,), (1,)), ((), ())), preferred_element_type=jnp.float32
    )
    after = from_behind(back_term, "rep", -1)
    result = result.at[0].add(first_add)
    result = result.at[nodes - 1].add(after)
    other = partner(vector, "dom", 0)
    field = jnp.concatenate([vector, other], axis=0)
    difference = (field[near_index] - field[far_index]).astype(jnp.bfloat16)
    multiplier = jnp.einsum(
        "srk,skj->srj", difference, contact_set, preferred_element_type=jnp.float32
    ).astype(jnp.bfloat16)
    terms = jnp.einsum("srj,skj->srk", multiplier, contact_set, preferred_element_type=jnp.float32)
    return result + jnp.einsum("sn,srk->nrk", signs, terms, precision=lax.Precision.HIGHEST)
    return result


def body(
    rhs,
    precond,
    diag_tiles,
    off_tiles,
    off_cols,
    link_tiles,
    contact_tiles,
    contact_owner,
    contact_anode,
    contact_bnode,
):
    groups = lax.axis_size("rep")
    target = contact_owner[:, 0]
    choose = (target[:, None] == jnp.arange(groups, dtype=jnp.int32)[None, :]).astype(jnp.int32)
    rank = jnp.sum((jnp.cumsum(choose, axis=0) - choose) * choose, axis=1)
    slot_of = target * CAP + rank
    pick = slot_of[None, :] == jnp.arange(groups * CAP, dtype=jnp.int32)[:, None]
    send_set = jnp.einsum(
        "sc,cij->sij", pick.astype(jnp.bfloat16), contact_tiles, preferred_element_type=jnp.float32
    ).astype(jnp.bfloat16).reshape(groups, CAP, B, B)
    labels = jnp.stack([contact_anode, contact_bnode], axis=1)
    send_labels = jnp.sum(
        jnp.where(pick[:, :, None], labels[None, :, :], 0), axis=1
    ).reshape(groups, CAP, 2)
    lane = lax.axis_index("rep")
    got_set = [jnp.take(send_set, lane, axis=0)]
    got_labels = [jnp.take(send_labels, lane, axis=0)]
    for shift in range(1, groups):
        ahead = (lane + shift) % groups
        got_set.append(from_behind(jnp.take(send_set, ahead, axis=0), "rep", shift))
        got_labels.append(from_behind(jnp.take(send_labels, ahead, axis=0), "rep", shift))
    rows = lax.axis_size("dom")
    for shift in range(groups):
        ahead = (lane + shift) % groups
        pairs = [
            (d * groups + q, (d ^ 1) * groups + (q + shift) % groups)
            for d in range(rows)
            for q in range(groups)
        ]
        got_set.append(lax.ppermute(jnp.take(send_set, ahead, axis=0), ("dom", "rep"), pairs))
        got_labels.append(lax.ppermute(jnp.take(send_labels, ahead, axis=0), ("dom", "rep"), pairs))
    got_set = jnp.stack(got_set)
    got_labels = jnp.stack(got_labels)
    slots = 2 * groups * CAP
    nodes = rhs.shape[0]
    contact_set = got_set.reshape(slots, B, B)
    got_labels = got_labels.reshape(2, groups * CAP, 2)
    near_index = jnp.concatenate([got_labels[0, :, 0], nodes + got_labels[1, :, 0]])
    far_index = jnp.concatenate([nodes + got_labels[0, :, 1], got_labels[1, :, 1]])
    own = jnp.arange(slots) < groups * CAP
    local = jnp.where(own, near_index, far_index)
    signs = jnp.where(own, 1.0, -1.0)[:, None] * (
        local[:, None] == jnp.arange(nodes, dtype=jnp.int32)[None, :]
    ).astype(jnp.float32)
    link_tile = link_tiles[0]
    scale = precond[:, None, :]
    solution = jnp.zeros_like(rhs)
    residual = rhs
    preconditioned = scale * residual
    direction = preconditioned
    for step in range(ITERS):
        image = apply_operator(
            direction,
            diag_tiles,
            off_tiles,
            off_cols,
            link_tile,
            contact_set,
            near_index,
            far_index,
            signs,
        )
        parts = [
            jnp.sum(direction * image, axis=(0, 2)),
            jnp.sum(residual * preconditioned, axis=(0, 2)),
        ]
        if step < ITERS - 1:
            parts.append(jnp.sum(preconditioned * image, axis=(0, 2)))
            parts.append(jnp.sum(image * (scale * image), axis=(0, 2)))
        sums = total(jnp.stack(parts))
        curve, res_dot = sums[0], sums[1]
        alpha = res_dot / curve
        solution = solution + alpha[None, :, None] * direction
        residual = residual - alpha[None, :, None] * image
        if step < ITERS - 1:
            preconditioned = scale * residual
            next_dot = res_dot - 2.0 * alpha * sums[2] + alpha * alpha * sums[3]
            direction = preconditioned + (next_dot / res_dot)[None, :, None] * direction
    return (solution, residual)


def solution(mesh):
    in_specs = (
        P(("dom", "rep"), None, None),
        P(("dom", "rep"), None),
        P(("dom", "rep"), None, None),
        P(("dom", "rep"), None, None, None),
        P(("dom", "rep"), None),
        P(("dom", "rep"), None, None),
        P(("dom", "rep"), None, None),
        P(("dom", "rep"), None),
        P(("dom", "rep")),
        P(("dom", "rep")),
    )
    out_specs = (P(("dom", "rep"), None, None), P(("dom", "rep"), None, None))
    return jax.shard_map(body, mesh=mesh, in_specs=in_specs, out_specs=out_specs, check_vma=False)
```

```python
import jax
import jax.numpy as jnp
from jax import lax
from jax.sharding import PartitionSpec as P

B = 128
ITERS = 4
CAP = 8


def from_behind(value, axis, steps):
    count = lax.axis_size(axis)
    pairs = [(source, (source + steps) % count) for source in range(count)]
    return lax.ppermute(value, axis, pairs)


def partner(value, axis, distance):
    return lax.ppermute(value, axis, [(i, i ^ 1 << distance) for i in range(lax.axis_size(axis))])


def total(value):
    count = lax.axis_size("dom") * lax.axis_size("rep")
    spread = jnp.broadcast_to(value[None], (count,) + value.shape)
    gathered = lax.all_to_all(spread, ("dom", "rep"), 0, 0, tiled=True)
    return jnp.sum(gathered, axis=0)


def local_stiffness(rounded, diag_tiles, off_tiles, cols_onehot, mirror_onehot):
    result = jnp.einsum("nrk,nkj->nrj", rounded, diag_tiles, preferred_element_type=jnp.float32)
    picked = jnp.einsum(
        "pn,nrk->prk", cols_onehot, rounded, preferred_element_type=jnp.float32
    ).astype(jnp.bfloat16)
    picked = picked.reshape(off_tiles.shape[0], off_tiles.shape[1], rounded.shape[1], rounded.shape[2])
    result = result + jnp.einsum(
        "nmrk,nmkj->nrj", picked, off_tiles, preferred_element_type=jnp.float32
    )
    mirror = jnp.einsum("nrk,nmjk->nmrj", rounded, off_tiles, preferred_element_type=jnp.float32)
    mirror = mirror.reshape(-1, rounded.shape[1], rounded.shape[2])
    return result + jnp.einsum("pn,prj->nrj", mirror_onehot, mirror, precision=lax.Precision.HIGHEST)


def apply_operator(vector, diag_tiles, off_tiles, link_tile, contact_set, tables):
    cols_onehot, mirror_onehot, near_onehot, far_onehot, near_collect, far_collect = tables
    nodes = vector.shape[0]
    rounded = vector.astype(jnp.bfloat16)
    before = from_behind(rounded[nodes - 1], "rep", 1)
    back_term = lax.dot_general(
        rounded[0], link_tile, (((1,), (1,)), ((), ())), preferred_element_type=jnp.float32
    )
    after = from_behind(back_term, "rep", -1)
    other = partner(rounded, "dom", 0).astype(vector.dtype)
    near = jnp.einsum("sn,nrk->srk", near_onehot, vector, precision=lax.Precision.HIGHEST)
    far = jnp.einsum("sn,nrk->srk", far_onehot, other, precision=lax.Precision.HIGHEST)
    difference = (near - far).astype(jnp.bfloat16)
    multiplier = jnp.einsum(
        "srk,skj->srj", difference, contact_set, preferred_element_type=jnp.float32
    ).astype(jnp.bfloat16)
    terms = jnp.einsum("srj,skj->srk", multiplier, contact_set, preferred_element_type=jnp.float32)
    far_sum = jnp.einsum("sn,srk->nrk", far_collect, terms, precision=lax.Precision.HIGHEST)
    far_sum, rounded = lax.optimization_barrier((far_sum.astype(jnp.bfloat16), rounded))
    far_terms = partner(far_sum, "dom", 0).astype(jnp.float32)
    result = local_stiffness(rounded, diag_tiles, off_tiles, cols_onehot, mirror_onehot)
    first_add = jnp.dot(before, link_tile, preferred_element_type=jnp.float32)
    result = result.at[0].add(first_add)
    result = result.at[nodes - 1].add(after)
    result = result + jnp.einsum("sn,srk->nrk", near_collect, terms, precision=lax.Precision.HIGHEST)
    return result - far_terms


def body(
    rhs,
    precond,
    diag_tiles,
    off_tiles,
    off_cols,
    link_tiles,
    contact_tiles,
    contact_owner,
    contact_anode,
    contact_bnode,
):
    groups = lax.axis_size("rep")
    target = contact_owner[:, 0]
    choose = (target[:, None] == jnp.arange(groups, dtype=jnp.int32)[None, :]).astype(jnp.int32)
    rank = jnp.sum((jnp.cumsum(choose, axis=0) - choose) * choose, axis=1)
    slot_of = target * CAP + rank
    pick = slot_of[None, :] == jnp.arange(groups * CAP, dtype=jnp.int32)[:, None]
    send_set = jnp.einsum(
        "sc,cij->sij", pick.astype(jnp.bfloat16), contact_tiles, preferred_element_type=jnp.float32
    ).astype(jnp.bfloat16).reshape(groups, CAP, B, B)
    labels = jnp.stack([contact_anode, contact_bnode], axis=1)
    send_labels = jnp.sum(
        jnp.where(pick[:, :, None], labels[None, :, :], 0), axis=1
    ).reshape(groups, CAP, 2)
    lane = lax.axis_index("rep")
    got_set = [jnp.take(send_set, lane, axis=0)]
    got_labels = [jnp.take(send_labels, lane, axis=0)]
    for shift in range(1, groups):
        ahead = (lane + shift) % groups
        got_set.append(from_behind(jnp.take(send_set, ahead, axis=0), "rep", shift))
        got_labels.append(from_behind(jnp.take(send_labels, ahead, axis=0), "rep", shift))
    got_set = jnp.stack(got_set)
    got_labels = jnp.stack(got_labels)
    slots = groups * CAP
    contact_set = got_set.reshape(slots, B, B)
    got_labels = got_labels.reshape(slots, 2)
    near_index = got_labels[:, 0]
    far_index = got_labels[:, 1]
    nodes = rhs.shape[0]
    blocks = jnp.arange(nodes, dtype=jnp.int32)[None, :]
    near_collect = (near_index[:, None] == blocks).astype(jnp.float32)
    far_collect = (far_index[:, None] == blocks).astype(jnp.float32)
    mirror_onehot = (off_cols.reshape(-1)[:, None] == blocks).astype(jnp.float32)
    tables = (
        mirror_onehot.astype(jnp.bfloat16),
        mirror_onehot,
        near_collect,
        far_collect,
        near_collect,
        far_collect,
    )
    link_tile = link_tiles[0]
    scale = precond[:, None, :]
    solution = jnp.zeros_like(rhs)
    residual = rhs
    preconditioned = scale * residual
    direction = preconditioned
    for step in range(ITERS):
        image = apply_operator(direction, diag_tiles, off_tiles, link_tile, contact_set, tables)
        parts = [
            jnp.sum(direction * image, axis=(0, 2)),
            jnp.sum(residual * preconditioned, axis=(0, 2)),
        ]
        if step < ITERS - 1:
            parts.append(jnp.sum(preconditioned * image, axis=(0, 2)))
            parts.append(jnp.sum(image * (scale * image), axis=(0, 2)))
        sums = total(jnp.stack(parts))
        curve, res_dot = sums[0], sums[1]
        alpha = res_dot / curve
        solution = solution + alpha[None, :, None] * direction
        residual = residual - alpha[None, :, None] * image
        if step < ITERS - 1:
            preconditioned = scale * residual
            next_dot = res_dot - 2.0 * alpha * sums[2] + alpha * alpha * sums[3]
            direction = preconditioned + (next_dot / res_dot)[None, :, None] * direction
    return (solution, residual)


def solution(mesh):
    in_specs = (
        P(("dom", "rep"), None, None),
        P(("dom", "rep"), None),
        P(("dom", "rep"), None, None),
        P(("dom", "rep"), None, None, None),
        P(("dom", "rep"), None),
        P(("dom", "rep"), None, None),
        P(("dom", "rep"), None, None),
        P(("dom", "rep"), None),
        P(("dom", "rep")),
        P(("dom", "rep")),
    )
    out_specs = (P(("dom", "rep"), None, None), P(("dom", "rep"), None, None))
    return jax.shard_map(body, mesh=mesh, in_specs=in_specs, out_specs=out_specs, check_vma=False)
```

```python
import jax
import jax.numpy as jnp
from jax import lax
from jax.sharding import PartitionSpec as P

B = 128
ITERS = 4
CAP = 8


def from_behind(value, axis, steps):
    count = lax.axis_size(axis)
    pairs = [(source, (source + steps) % count) for source in range(count)]
    return lax.ppermute(value, axis, pairs)


def partner(value, axis, distance):
    return lax.ppermute(value, axis, [(i, i ^ 1 << distance) for i in range(lax.axis_size(axis))])


def total(value):
    count = lax.axis_size("dom") * lax.axis_size("rep")
    spread = jnp.broadcast_to(value[None], (count,) + value.shape)
    gathered = lax.all_to_all(spread, ("dom", "rep"), 0, 0, tiled=True)
    return jnp.sum(gathered, axis=0)


def local_stiffness(rounded, diag_tiles, off_tiles, cols_onehot, mirror_onehot):
    result = jnp.einsum("nrk,nkj->nrj", rounded, diag_tiles, preferred_element_type=jnp.float32)
    picked = jnp.einsum(
        "pn,nrk->prk", cols_onehot, rounded, preferred_element_type=jnp.float32
    ).astype(jnp.bfloat16)
    picked = picked.reshape(off_tiles.shape[0], off_tiles.shape[1], rounded.shape[1], rounded.shape[2])
    result = result + jnp.einsum(
        "nmrk,nmkj->nrj", picked, off_tiles, preferred_element_type=jnp.float32
    )
    mirror = jnp.einsum("nrk,nmjk->nmrj", rounded, off_tiles, preferred_element_type=jnp.float32)
    mirror = mirror.reshape(-1, rounded.shape[1], rounded.shape[2])
    return result + jnp.einsum("pn,prj->nrj", mirror_onehot, mirror, precision=lax.Precision.HIGHEST)


def apply_operator(vector, diag_tiles, off_tiles, link_tile, contact_set, tables):
    cols_onehot, mirror_onehot, near_onehot, far_onehot, near_collect, far_collect = tables
    nodes = vector.shape[0]
    rounded = vector.astype(jnp.bfloat16)
    before = from_behind(rounded[nodes - 1], "rep", 1)
    back_term = lax.dot_general(
        rounded[0], link_tile, (((1,), (1,)), ((), ())), preferred_element_type=jnp.float32
    )
    after = from_behind(back_term, "rep", -1)
    other = partner(rounded, "dom", 0).astype(vector.dtype)
    near = jnp.einsum("sn,nrk->srk", near_onehot, vector, precision=lax.Precision.HIGHEST)
    far = jnp.einsum("sn,nrk->srk", far_onehot, other, precision=lax.Precision.HIGHEST)
    difference = (near - far).astype(jnp.bfloat16)
    multiplier = jnp.einsum(
        "srk,skj->srj", difference, contact_set, preferred_element_type=jnp.float32
    ).astype(jnp.bfloat16)
    terms = jnp.einsum("srj,skj->srk", multiplier, contact_set, preferred_element_type=jnp.float32)
    far_sum = jnp.einsum("sn,srk->nrk", far_collect, terms, precision=lax.Precision.HIGHEST)
    far_sum, rounded = lax.optimization_barrier((far_sum.astype(jnp.bfloat16), rounded))
    far_terms = partner(far_sum, "dom", 0).astype(jnp.float32)
    result = local_stiffness(rounded, diag_tiles, off_tiles, cols_onehot, mirror_onehot)
    first_add = jnp.dot(before, link_tile, preferred_element_type=jnp.float32)
    ends = jnp.concatenate(
        [first_add[None], jnp.zeros((nodes - 2,) + first_add.shape, jnp.float32), after[None]]
    )
    result = result + ends
    result = result + jnp.einsum("sn,srk->nrk", near_collect, terms, precision=lax.Precision.HIGHEST)
    return result - far_terms


def body(
    rhs,
    precond,
    diag_tiles,
    off_tiles,
    off_cols,
    link_tiles,
    contact_tiles,
    contact_owner,
    contact_anode,
    contact_bnode,
):
    groups = lax.axis_size("rep")
    target = contact_owner[:, 0]
    choose = (target[:, None] == jnp.arange(groups, dtype=jnp.int32)[None, :]).astype(jnp.int32)
    rank = jnp.sum((jnp.cumsum(choose, axis=0) - choose) * choose, axis=1)
    slot_of = target * CAP + rank
    pick = slot_of[None, :] == jnp.arange(groups * CAP, dtype=jnp.int32)[:, None]
    send_set = jnp.einsum(
        "sc,cij->sij", pick.astype(jnp.bfloat16), contact_tiles, preferred_element_type=jnp.float32
    ).astype(jnp.bfloat16).reshape(groups, CAP, B, B)
    labels = jnp.stack([contact_anode, contact_bnode], axis=1)
    send_labels = jnp.sum(
        jnp.where(pick[:, :, None], labels[None, :, :], 0), axis=1
    ).reshape(groups, CAP, 2)
    lane = lax.axis_index("rep")
    got_set = [jnp.take(send_set, lane, axis=0)]
    got_labels = [jnp.take(send_labels, lane, axis=0)]
    for shift in range(1, groups):
        ahead = (lane + shift) % groups
        got_set.append(from_behind(jnp.take(send_set, ahead, axis=0), "rep", shift))
        got_labels.append(from_behind(jnp.take(send_labels, ahead, axis=0), "rep", shift))
    got_set = jnp.stack(got_set)
    got_labels = jnp.stack(got_labels)
    slots = groups * CAP
    contact_set = got_set.reshape(slots, B, B)
    got_labels = got_labels.reshape(slots, 2)
    near_index = got_labels[:, 0]
    far_index = got_labels[:, 1]
    nodes = rhs.shape[0]
    blocks = jnp.arange(nodes, dtype=jnp.int32)[None, :]
    near_collect = (near_index[:, None] == blocks).astype(jnp.float32)
    far_collect = (far_index[:, None] == blocks).astype(jnp.float32)
    mirror_onehot = (off_cols.reshape(-1)[:, None] == blocks).astype(jnp.float32)
    tables = (
        mirror_onehot.astype(jnp.bfloat16),
        mirror_onehot,
        near_collect,
        far_collect,
        near_collect,
        far_collect,
    )
    link_tile = link_tiles[0]
    scale = precond[:, None, :]
    solution = jnp.zeros_like(rhs)
    residual = rhs
    preconditioned = scale * residual
    direction = preconditioned
    for step in range(ITERS):
        image = apply_operator(direction, diag_tiles, off_tiles, link_tile, contact_set, tables)
        parts = [
            jnp.sum(direction * image, axis=(0, 2)),
            jnp.sum(residual * preconditioned, axis=(0, 2)),
        ]
        if step < ITERS - 1:
            parts.append(jnp.sum(preconditioned * image, axis=(0, 2)))
            parts.append(jnp.sum(image * (scale * image), axis=(0, 2)))
        sums = total(jnp.stack(parts))
        curve, res_dot = sums[0], sums[1]
        alpha = res_dot / curve
        solution = solution + alpha[None, :, None] * direction
        residual = residual - alpha[None, :, None] * image
        if step < ITERS - 1:
            preconditioned = scale * residual
            next_dot = res_dot - 2.0 * alpha * sums[2] + alpha * alpha * sums[3]
            direction = preconditioned + (next_dot / res_dot)[None, :, None] * direction
    return (solution, residual)


def solution(mesh):
    in_specs = (
        P(("dom", "rep"), None, None),
        P(("dom", "rep"), None),
        P(("dom", "rep"), None, None),
        P(("dom", "rep"), None, None, None),
        P(("dom", "rep"), None),
        P(("dom", "rep"), None, None),
        P(("dom", "rep"), None, None),
        P(("dom", "rep"), None),
        P(("dom", "rep")),
        P(("dom", "rep")),
    )
    out_specs = (P(("dom", "rep"), None, None), P(("dom", "rep"), None, None))
    return jax.shard_map(body, mesh=mesh, in_specs=in_specs, out_specs=out_specs, check_vma=False)
```

```python
import jax
import jax.numpy as jnp
from jax import lax
from jax.sharding import PartitionSpec as P

B = 128
ITERS = 4
CAP = 8


def from_behind(value, axis, steps):
    count = lax.axis_size(axis)
    pairs = [(source, (source + steps) % count) for source in range(count)]
    return lax.ppermute(value, axis, pairs)


def partner(value, axis, distance):
    return lax.ppermute(value, axis, [(i, i ^ 1 << distance) for i in range(lax.axis_size(axis))])


def total(value):
    count = lax.axis_size("dom") * lax.axis_size("rep")
    spread = jnp.broadcast_to(value[None], (count,) + value.shape)
    gathered = lax.all_to_all(spread, ("dom", "rep"), 0, 0, tiled=True)
    return jnp.sum(gathered, axis=0)


def local_stiffness(rounded, diag_tiles, off_tiles, cols_onehot, mirror_onehot):
    result = jnp.einsum("nrk,nkj->nrj", rounded, diag_tiles, preferred_element_type=jnp.float32)
    picked = jnp.einsum(
        "pn,nrk->prk", cols_onehot, rounded, preferred_element_type=jnp.float32
    ).astype(jnp.bfloat16)
    picked = picked.reshape(off_tiles.shape[0], off_tiles.shape[1], rounded.shape[1], rounded.shape[2])
    result = result + jnp.einsum(
        "nmrk,nmkj->nrj", picked, off_tiles, preferred_element_type=jnp.float32
    )
    mirror = jnp.einsum("nrk,nmjk->nmrj", rounded, off_tiles, preferred_element_type=jnp.float32)
    mirror = mirror.reshape(-1, rounded.shape[1], rounded.shape[2])
    return result + jnp.einsum("pn,prj->nrj", mirror_onehot, mirror, precision=lax.Precision.HIGHEST)


def apply_operator(vector, diag_tiles, off_tiles, link_tile, contact_set, flipped_set, tables):
    cols_onehot, mirror_onehot, near_onehot, far_onehot, near_collect, far_collect = tables
    nodes = vector.shape[0]
    rounded = vector.astype(jnp.bfloat16)
    before = from_behind(rounded[nodes - 1], "rep", 1)
    back_term = lax.dot_general(
        rounded[0], link_tile, (((1,), (1,)), ((), ())), preferred_element_type=jnp.float32
    )
    after = from_behind(back_term, "rep", -1)
    other = partner(rounded, "dom", 0).astype(vector.dtype)
    near = jnp.einsum("sn,nrk->srk", near_onehot, vector, precision=lax.Precision.HIGHEST)
    far = jnp.einsum("sn,nrk->srk", far_onehot, other, precision=lax.Precision.HIGHEST)
    difference = (near - far).astype(jnp.bfloat16)
    multiplier = jnp.einsum(
        "srk,skj->srj", difference, contact_set, preferred_element_type=jnp.float32
    ).astype(jnp.bfloat16)
    terms = jnp.einsum("srj,sjk->srk", multiplier, flipped_set, preferred_element_type=jnp.float32)
    far_sum = jnp.einsum("sn,srk->nrk", far_collect, terms, precision=lax.Precision.HIGHEST)
    far_sum, rounded = lax.optimization_barrier((far_sum.astype(jnp.bfloat16), rounded))
    far_terms = partner(far_sum, "dom", 0).astype(jnp.float32)
    result = local_stiffness(rounded, diag_tiles, off_tiles, cols_onehot, mirror_onehot)
    first_add = jnp.dot(before, link_tile, preferred_element_type=jnp.float32)
    ends = jnp.concatenate(
        [first_add[None], jnp.zeros((nodes - 2,) + first_add.shape, jnp.float32), after[None]]
    )
    result = result + ends
    result = result + jnp.einsum("sn,srk->nrk", near_collect, terms, precision=lax.Precision.HIGHEST)
    return result - far_terms


def body(
    rhs,
    precond,
    diag_tiles,
    off_tiles,
    off_cols,
    link_tiles,
    contact_tiles,
    contact_owner,
    contact_anode,
    contact_bnode,
):
    groups = lax.axis_size("rep")
    target = contact_owner[:, 0]
    choose = (target[:, None] == jnp.arange(groups, dtype=jnp.int32)[None, :]).astype(jnp.int32)
    rank = jnp.sum((jnp.cumsum(choose, axis=0) - choose) * choose, axis=1)
    slot_of = target * CAP + rank
    pick = slot_of[None, :] == jnp.arange(groups * CAP, dtype=jnp.int32)[:, None]
    send_set = jnp.einsum(
        "sc,cij->sij", pick.astype(jnp.bfloat16), contact_tiles, preferred_element_type=jnp.float32
    ).astype(jnp.bfloat16).reshape(groups, CAP, B, B)
    labels = jnp.stack([contact_anode, contact_bnode], axis=1)
    send_labels = jnp.sum(
        jnp.where(pick[:, :, None], labels[None, :, :], 0), axis=1
    ).reshape(groups, CAP, 2)
    lane = lax.axis_index("rep")
    got_set = [jnp.take(send_set, lane, axis=0)]
    got_labels = [jnp.take(send_labels, lane, axis=0)]
    for shift in range(1, groups):
        ahead = (lane + shift) % groups
        got_set.append(from_behind(jnp.take(send_set, ahead, axis=0), "rep", shift))
        got_labels.append(from_behind(jnp.take(send_labels, ahead, axis=0), "rep", shift))
    got_set = jnp.stack(got_set)
    got_labels = jnp.stack(got_labels)
    slots = groups * CAP
    contact_set = got_set.reshape(slots, B, B)
    got_labels = got_labels.reshape(slots, 2)
    near_index = got_labels[:, 0]
    far_index = got_labels[:, 1]
    nodes = rhs.shape[0]
    blocks = jnp.arange(nodes, dtype=jnp.int32)[None, :]
    near_collect = (near_index[:, None] == blocks).astype(jnp.float32)
    far_collect = (far_index[:, None] == blocks).astype(jnp.float32)
    mirror_onehot = (off_cols.reshape(-1)[:, None] == blocks).astype(jnp.float32)
    tables = (
        mirror_onehot.astype(jnp.bfloat16),
        mirror_onehot,
        near_collect,
        far_collect,
        near_collect,
        far_collect,
    )
    link_tile = link_tiles[0]
    flipped_set = jnp.swapaxes(contact_set, 1, 2)
    scale = precond[:, None, :]
    solution = jnp.zeros_like(rhs)
    residual = rhs
    preconditioned = scale * residual
    direction = preconditioned
    for step in range(ITERS):
        image = apply_operator(
            direction, diag_tiles, off_tiles, link_tile, contact_set, flipped_set, tables
        )
        parts = [
            jnp.sum(direction * image, axis=(0, 2)),
            jnp.sum(residual * preconditioned, axis=(0, 2)),
        ]
        if step < ITERS - 1:
            parts.append(jnp.sum(preconditioned * image, axis=(0, 2)))
            parts.append(jnp.sum(image * (scale * image), axis=(0, 2)))
        sums = total(jnp.stack(parts))
        curve, res_dot = sums[0], sums[1]
        alpha = res_dot / curve
        solution = solution + alpha[None, :, None] * direction
        residual = residual - alpha[None, :, None] * image
        if step < ITERS - 1:
            preconditioned = scale * residual
            next_dot = res_dot - 2.0 * alpha * sums[2] + alpha * alpha * sums[3]
            direction = preconditioned + (next_dot / res_dot)[None, :, None] * direction
    return (solution, residual)


def solution(mesh):
    in_specs = (
        P(("dom", "rep"), None, None),
        P(("dom", "rep"), None),
        P(("dom", "rep"), None, None),
        P(("dom", "rep"), None, None, None),
        P(("dom", "rep"), None),
        P(("dom", "rep"), None, None),
        P(("dom", "rep"), None, None),
        P(("dom", "rep"), None),
        P(("dom", "rep")),
        P(("dom", "rep")),
    )
    out_specs = (P(("dom", "rep"), None, None), P(("dom", "rep"), None, None))
    return jax.shard_map(body, mesh=mesh, in_specs=in_specs, out_specs=out_specs, check_vma=False)
```

```python
import jax
import jax.numpy as jnp
from jax import lax
from jax.sharding import PartitionSpec as P

B = 128
ITERS = 4
CAP = 8


def from_behind(value, axis, steps):
    count = lax.axis_size(axis)
    pairs = [(source, (source + steps) % count) for source in range(count)]
    return lax.ppermute(value, axis, pairs)


def partner(value, axis, distance):
    return lax.ppermute(value, axis, [(i, i ^ 1 << distance) for i in range(lax.axis_size(axis))])


def total(value):
    count = lax.axis_size("dom") * lax.axis_size("rep")
    spread = jnp.broadcast_to(value[None], (count,) + value.shape)
    gathered = lax.all_to_all(spread, ("dom", "rep"), 0, 0, tiled=True)
    return jnp.sum(gathered, axis=0)


def local_stiffness(rounded, diag_tiles, off_tiles, cols_onehot, mirror_onehot):
    result = jnp.einsum("nrk,nkj->nrj", rounded, diag_tiles, preferred_element_type=jnp.float32)
    picked = jnp.einsum(
        "pn,nrk->prk", cols_onehot, rounded, preferred_element_type=jnp.float32
    ).astype(jnp.bfloat16)
    picked = picked.reshape(off_tiles.shape[0], off_tiles.shape[1], rounded.shape[1], rounded.shape[2])
    result = result + jnp.einsum(
        "nmrk,nmkj->nrj", picked, off_tiles, preferred_element_type=jnp.float32
    )
    mirror = jnp.einsum("nrk,nmjk->nmrj", rounded, off_tiles, preferred_element_type=jnp.float32)
    mirror = mirror.reshape(-1, rounded.shape[1], rounded.shape[2])
    return result + jnp.einsum("pn,prj->nrj", mirror_onehot, mirror, precision=lax.Precision.HIGHEST)


def apply_operator(vector, diag_tiles, off_tiles, link_tile, contact_set, tables):
    cols_onehot, mirror_onehot, near_onehot, far_onehot, near_collect, far_collect = tables
    nodes = vector.shape[0]
    rounded = vector.astype(jnp.bfloat16)
    before = from_behind(rounded[nodes - 1], "rep", 1)
    back_term = lax.dot_general(
        rounded[0], link_tile, (((1,), (1,)), ((), ())), preferred_element_type=jnp.float32
    )
    after = from_behind(back_term, "rep", -1)
    other = partner(rounded, "dom", 0).astype(vector.dtype)
    near = jnp.einsum("sn,nrk->srk", near_onehot, vector, precision=lax.Precision.HIGHEST)
    far = jnp.einsum("sn,nrk->srk", far_onehot, other, precision=lax.Precision.HIGHEST)
    difference = (near - far).astype(jnp.bfloat16)
    multiplier = jnp.einsum(
        "srk,skj->srj", difference, contact_set, preferred_element_type=jnp.float32
    ).astype(jnp.bfloat16)
    terms = jnp.einsum("srj,skj->srk", multiplier, contact_set, preferred_element_type=jnp.float32)
    far_sum = jnp.einsum("sn,srk->nrk", far_collect, terms, precision=lax.Precision.HIGHEST)
    far_sum, rounded, terms = lax.optimization_barrier(
        (far_sum.astype(jnp.bfloat16), rounded, terms)
    )
    far_terms = partner(far_sum, "dom", 0).astype(jnp.float32)
    result = local_stiffness(rounded, diag_tiles, off_tiles, cols_onehot, mirror_onehot)
    first_add = jnp.dot(before, link_tile, preferred_element_type=jnp.float32)
    ends = jnp.concatenate(
        [first_add[None], jnp.zeros((nodes - 2,) + first_add.shape, jnp.float32), after[None]]
    )
    result = result + ends
    result = result + jnp.einsum("sn,srk->nrk", near_collect, terms, precision=lax.Precision.HIGHEST)
    return result - far_terms


def body(
    rhs,
    precond,
    diag_tiles,
    off_tiles,
    off_cols,
    link_tiles,
    contact_tiles,
    contact_owner,
    contact_anode,
    contact_bnode,
):
    groups = lax.axis_size("rep")
    target = contact_owner[:, 0]
    choose = (target[:, None] == jnp.arange(groups, dtype=jnp.int32)[None, :]).astype(jnp.int32)
    rank = jnp.sum((jnp.cumsum(choose, axis=0) - choose) * choose, axis=1)
    slot_of = target * CAP + rank
    pick = slot_of[None, :] == jnp.arange(groups * CAP, dtype=jnp.int32)[:, None]
    send_set = jnp.einsum(
        "sc,cij->sij", pick.astype(jnp.bfloat16), contact_tiles, preferred_element_type=jnp.float32
    ).astype(jnp.bfloat16).reshape(groups, CAP, B, B)
    labels = jnp.stack([contact_anode, contact_bnode], axis=1)
    send_labels = jnp.sum(
        jnp.where(pick[:, :, None], labels[None, :, :], 0), axis=1
    ).reshape(groups, CAP, 2)
    lane = lax.axis_index("rep")
    got_set = [jnp.take(send_set, lane, axis=0)]
    got_labels = [jnp.take(send_labels, lane, axis=0)]
    for shift in range(1, groups):
        ahead = (lane + shift) % groups
        got_set.append(from_behind(jnp.take(send_set, ahead, axis=0), "rep", shift))
        got_labels.append(from_behind(jnp.take(send_labels, ahead, axis=0), "rep", shift))
    got_set = jnp.stack(got_set)
    got_labels = jnp.stack(got_labels)
    slots = groups * CAP
    contact_set = got_set.reshape(slots, B, B)
    got_labels = got_labels.reshape(slots, 2)
    near_index = got_labels[:, 0]
    far_index = got_labels[:, 1]
    nodes = rhs.shape[0]
    blocks = jnp.arange(nodes, dtype=jnp.int32)[None, :]
    near_collect = (near_index[:, None] == blocks).astype(jnp.float32)
    far_collect = (far_index[:, None] == blocks).astype(jnp.float32)
    mirror_onehot = (off_cols.reshape(-1)[:, None] == blocks).astype(jnp.float32)
    tables = (
        mirror_onehot.astype(jnp.bfloat16),
        mirror_onehot,
        near_collect,
        far_collect,
        near_collect,
        far_collect,
    )
    link_tile = link_tiles[0]
    scale = precond[:, None, :]
    solution = jnp.zeros_like(rhs)
    residual = rhs
    preconditioned = scale * residual
    direction = preconditioned
    for step in range(ITERS):
        image = apply_operator(direction, diag_tiles, off_tiles, link_tile, contact_set, tables)
        parts = [
            jnp.sum(direction * image, axis=(0, 2)),
            jnp.sum(residual * preconditioned, axis=(0, 2)),
        ]
        if step < ITERS - 1:
            parts.append(jnp.sum(preconditioned * image, axis=(0, 2)))
            parts.append(jnp.sum(image * (scale * image), axis=(0, 2)))
        sums = total(jnp.stack(parts))
        curve, res_dot = sums[0], sums[1]
        alpha = res_dot / curve
        solution = solution + alpha[None, :, None] * direction
        residual = residual - alpha[None, :, None] * image
        if step < ITERS - 1:
            preconditioned = scale * residual
            next_dot = res_dot - 2.0 * alpha * sums[2] + alpha * alpha * sums[3]
            direction = preconditioned + (next_dot / res_dot)[None, :, None] * direction
    return (solution, residual)


def solution(mesh):
    in_specs = (
        P(("dom", "rep"), None, None),
        P(("dom", "rep"), None),
        P(("dom", "rep"), None, None),
        P(("dom", "rep"), None, None, None),
        P(("dom", "rep"), None),
        P(("dom", "rep"), None, None),
        P(("dom", "rep"), None, None),
        P(("dom", "rep"), None),
        P(("dom", "rep")),
        P(("dom", "rep")),
    )
    out_specs = (P(("dom", "rep"), None, None), P(("dom", "rep"), None, None))
    return jax.shard_map(body, mesh=mesh, in_specs=in_specs, out_specs=out_specs, check_vma=False)
```

```python
import jax
import jax.numpy as jnp
from jax import lax
from jax.sharding import PartitionSpec as P

B = 128
ITERS = 4
CAP = 8


def from_behind(value, axis, steps):
    count = lax.axis_size(axis)
    pairs = [(source, (source + steps) % count) for source in range(count)]
    return lax.ppermute(value, axis, pairs)


def partner(value, axis, distance):
    return lax.ppermute(value, axis, [(i, i ^ 1 << distance) for i in range(lax.axis_size(axis))])


def total(value):
    count = lax.axis_size("dom") * lax.axis_size("rep")
    spread = jnp.broadcast_to(value[None], (count,) + value.shape)
    gathered = lax.all_to_all(spread, ("dom", "rep"), 0, 0, tiled=True)
    return jnp.sum(gathered, axis=0)


def local_stiffness(rounded, diag_tiles, off_tiles, cols_onehot, mirror_onehot):
    result = jnp.einsum("nrk,nkj->nrj", rounded, diag_tiles, preferred_element_type=jnp.float32)
    picked = jnp.einsum(
        "pn,nrk->prk", cols_onehot, rounded, preferred_element_type=jnp.float32
    ).astype(jnp.bfloat16)
    picked = picked.reshape(off_tiles.shape[0], off_tiles.shape[1], rounded.shape[1], rounded.shape[2])
    result = result + jnp.einsum(
        "nmrk,nmkj->nrj", picked, off_tiles, preferred_element_type=jnp.float32
    )
    mirror = jnp.einsum("nrk,nmjk->nmrj", rounded, off_tiles, preferred_element_type=jnp.float32)
    mirror = mirror.reshape(-1, rounded.shape[1], rounded.shape[2])
    return result + jnp.einsum("pn,prj->nrj", mirror_onehot, mirror, precision=lax.Precision.HIGHEST)


def apply_operator(vector, diag_tiles, off_tiles, link_tile, contact_set, tables):
    cols_onehot, mirror_onehot, near_onehot, far_onehot, near_collect, far_collect = tables
    nodes = vector.shape[0]
    rounded = vector.astype(jnp.bfloat16)
    before = from_behind(rounded[nodes - 1], "rep", 1)
    other = partner(rounded, "dom", 0).astype(vector.dtype)
    near = jnp.einsum("sn,nrk->srk", near_onehot, vector, precision=lax.Precision.HIGHEST)
    far = jnp.einsum("sn,nrk->srk", far_onehot, other, precision=lax.Precision.HIGHEST)
    difference = (near - far).astype(jnp.bfloat16)
    multiplier = jnp.einsum(
        "srk,skj->srj", difference, contact_set, preferred_element_type=jnp.float32
    ).astype(jnp.bfloat16)
    terms = jnp.einsum("srj,skj->srk", multiplier, contact_set, preferred_element_type=jnp.float32)
    far_sum = jnp.einsum("sn,srk->nrk", far_collect, terms, precision=lax.Precision.HIGHEST)
    far_sum, rounded, terms = lax.optimization_barrier(
        (far_sum.astype(jnp.bfloat16), rounded, terms)
    )
    far_terms = partner(far_sum, "dom", 0).astype(jnp.float32)
    back_term = lax.dot_general(
        rounded[0], link_tile, (((1,), (1,)), ((), ())), preferred_element_type=jnp.float32
    )
    after = from_behind(back_term, "rep", -1)
    result = local_stiffness(rounded, diag_tiles, off_tiles, cols_onehot, mirror_onehot)
    first_add = jnp.dot(before, link_tile, preferred_element_type=jnp.float32)
    ends = jnp.concatenate(
        [first_add[None], jnp.zeros((nodes - 2,) + first_add.shape, jnp.float32), after[None]]
    )
    result = result + ends
    result = result + jnp.einsum("sn,srk->nrk", near_collect, terms, precision=lax.Precision.HIGHEST)
    return result - far_terms


def body(
    rhs,
    precond,
    diag_tiles,
    off_tiles,
    off_cols,
    link_tiles,
    contact_tiles,
    contact_owner,
    contact_anode,
    contact_bnode,
):
    groups = lax.axis_size("rep")
    target = contact_owner[:, 0]
    choose = (target[:, None] == jnp.arange(groups, dtype=jnp.int32)[None, :]).astype(jnp.int32)
    rank = jnp.sum((jnp.cumsum(choose, axis=0) - choose) * choose, axis=1)
    slot_of = target * CAP + rank
    pick = slot_of[None, :] == jnp.arange(groups * CAP, dtype=jnp.int32)[:, None]
    send_set = jnp.einsum(
        "sc,cij->sij", pick.astype(jnp.bfloat16), contact_tiles, preferred_element_type=jnp.float32
    ).astype(jnp.bfloat16).reshape(groups, CAP, B, B)
    labels = jnp.stack([contact_anode, contact_bnode], axis=1)
    send_labels = jnp.sum(
        jnp.where(pick[:, :, None], labels[None, :, :], 0), axis=1
    ).reshape(groups, CAP, 2)
    lane = lax.axis_index("rep")
    got_set = [jnp.take(send_set, lane, axis=0)]
    got_labels = [jnp.take(send_labels, lane, axis=0)]
    for shift in range(1, groups):
        ahead = (lane + shift) % groups
        got_set.append(from_behind(jnp.take(send_set, ahead, axis=0), "rep", shift))
        got_labels.append(from_behind(jnp.take(send_labels, ahead, axis=0), "rep", shift))
    got_set = jnp.stack(got_set)
    got_labels = jnp.stack(got_labels)
    slots = groups * CAP
    contact_set = got_set.reshape(slots, B, B)
    got_labels = got_labels.reshape(slots, 2)
    near_index = got_labels[:, 0]
    far_index = got_labels[:, 1]
    nodes = rhs.shape[0]
    blocks = jnp.arange(nodes, dtype=jnp.int32)[None, :]
    near_collect = (near_index[:, None] == blocks).astype(jnp.float32)
    far_collect = (far_index[:, None] == blocks).astype(jnp.float32)
    mirror_onehot = (off_cols.reshape(-1)[:, None] == blocks).astype(jnp.float32)
    tables = (
        mirror_onehot.astype(jnp.bfloat16),
        mirror_onehot,
        near_collect,
        far_collect,
        near_collect,
        far_collect,
    )
    link_tile = link_tiles[0]
    scale = precond[:, None, :]
    solution = jnp.zeros_like(rhs)
    residual = rhs
    preconditioned = scale * residual
    direction = preconditioned
    for step in range(ITERS):
        image = apply_operator(direction, diag_tiles, off_tiles, link_tile, contact_set, tables)
        parts = [
            jnp.sum(direction * image, axis=(0, 2)),
            jnp.sum(residual * preconditioned, axis=(0, 2)),
        ]
        if step < ITERS - 1:
            parts.append(jnp.sum(preconditioned * image, axis=(0, 2)))
            parts.append(jnp.sum(image * (scale * image), axis=(0, 2)))
        sums = total(jnp.stack(parts))
        curve, res_dot = sums[0], sums[1]
        alpha = res_dot / curve
        solution = solution + alpha[None, :, None] * direction
        residual = residual - alpha[None, :, None] * image
        if step < ITERS - 1:
            preconditioned = scale * residual
            next_dot = res_dot - 2.0 * alpha * sums[2] + alpha * alpha * sums[3]
            direction = preconditioned + (next_dot / res_dot)[None, :, None] * direction
    return (solution, residual)


def solution(mesh):
    in_specs = (
        P(("dom", "rep"), None, None),
        P(("dom", "rep"), None),
        P(("dom", "rep"), None, None),
        P(("dom", "rep"), None, None, None),
        P(("dom", "rep"), None),
        P(("dom", "rep"), None, None),
        P(("dom", "rep"), None, None),
        P(("dom", "rep"), None),
        P(("dom", "rep")),
        P(("dom", "rep")),
    )
    out_specs = (P(("dom", "rep"), None, None), P(("dom", "rep"), None, None))
    return jax.shard_map(body, mesh=mesh, in_specs=in_specs, out_specs=out_specs, check_vma=False)
```

```python
import jax
import jax.numpy as jnp
from jax import lax
from jax.sharding import PartitionSpec as P

B = 128
ITERS = 4
CAP = 8


def from_behind(value, axis, steps):
    count = lax.axis_size(axis)
    pairs = [(source, (source + steps) % count) for source in range(count)]
    return lax.ppermute(value, axis, pairs)


def partner(value, axis, distance):
    return lax.ppermute(value, axis, [(i, i ^ 1 << distance) for i in range(lax.axis_size(axis))])


def total(value):
    count = lax.axis_size("dom") * lax.axis_size("rep")
    spread = jnp.broadcast_to(value[None], (count,) + value.shape)
    gathered = lax.all_to_all(spread, ("dom", "rep"), 0, 0, tiled=True)
    return jnp.sum(gathered, axis=0)


def local_stiffness(rounded, diag_tiles, off_tiles, cols_onehot, mirror_onehot):
    result = jnp.einsum("nrk,nkj->nrj", rounded, diag_tiles, preferred_element_type=jnp.float32)
    picked = jnp.einsum(
        "pn,nrk->prk", cols_onehot, rounded, preferred_element_type=jnp.float32
    ).astype(jnp.bfloat16)
    picked = picked.reshape(off_tiles.shape[0], off_tiles.shape[1], rounded.shape[1], rounded.shape[2])
    result = result + jnp.einsum(
        "nmrk,nmkj->nrj", picked, off_tiles, preferred_element_type=jnp.float32
    )
    mirror = jnp.einsum("nrk,nmjk->nmrj", rounded, off_tiles, preferred_element_type=jnp.float32)
    mirror = mirror.reshape(-1, rounded.shape[1], rounded.shape[2])
    return result + jnp.einsum("pn,prj->nrj", mirror_onehot, mirror, precision=lax.Precision.HIGHEST)


def apply_operator(vector, diag_tiles, off_tiles, link_tile, contact_set, tables):
    cols_onehot, mirror_onehot, near_onehot, far_onehot, near_collect, far_collect = tables
    nodes = vector.shape[0]
    rounded = vector.astype(jnp.bfloat16)
    before = from_behind(rounded[nodes - 1], "rep", 1)
    other = partner(rounded, "dom", 0).astype(vector.dtype)
    near = jnp.einsum("sn,nrk->srk", near_onehot, vector, precision=lax.Precision.HIGHEST)
    far = jnp.einsum("sn,nrk->srk", far_onehot, other, precision=lax.Precision.HIGHEST)
    difference = (near - far).astype(jnp.bfloat16)
    multiplier = jnp.einsum(
        "srk,skj->srj", difference, contact_set, preferred_element_type=jnp.float32
    ).astype(jnp.bfloat16)
    terms = jnp.einsum("srj,skj->srk", multiplier, contact_set, preferred_element_type=jnp.float32)
    far_sum = jnp.einsum("sn,srk->nrk", far_collect, terms, precision=lax.Precision.HIGHEST)
    far_sum, rounded, terms = lax.optimization_barrier(
        (far_sum.astype(jnp.bfloat16), rounded, terms)
    )
    far_terms = partner(far_sum, "dom", 0).astype(jnp.float32)
    back_term = lax.dot_general(
        rounded[0], link_tile, (((1,), (1,)), ((), ())), preferred_element_type=jnp.float32
    )
    after = from_behind(back_term, "rep", -1)
    result = local_stiffness(rounded, diag_tiles, off_tiles, cols_onehot, mirror_onehot)
    first_add = jnp.dot(before, link_tile, preferred_element_type=jnp.float32)
    ends = jnp.concatenate(
        [first_add[None], jnp.zeros((nodes - 2,) + first_add.shape, jnp.float32), after[None]]
    )
    result = result + ends
    result = result + jnp.einsum("sn,srk->nrk", near_collect, terms, precision=lax.Precision.HIGHEST)
    return result - far_terms


def body(
    rhs,
    precond,
    diag_tiles,
    off_tiles,
    off_cols,
    link_tiles,
    contact_tiles,
    contact_owner,
    contact_anode,
    contact_bnode,
):
    groups = lax.axis_size("rep")
    target = contact_owner[:, 0]
    choose = (target[:, None] == jnp.arange(groups, dtype=jnp.int32)[None, :]).astype(jnp.int32)
    rank = jnp.sum((jnp.cumsum(choose, axis=0) - choose) * choose, axis=1)
    slot_of = target * CAP + rank
    pick = slot_of[None, :] == jnp.arange(groups * CAP, dtype=jnp.int32)[:, None]
    send_set = jnp.einsum(
        "sc,cij->sij", pick.astype(jnp.bfloat16), contact_tiles, preferred_element_type=jnp.float32
    ).astype(jnp.bfloat16)
    labels = jnp.stack([contact_anode, contact_bnode], axis=1)
    digits = jnp.concatenate([labels // 256, labels % 256], axis=1).astype(jnp.float32)
    send_labels = jnp.einsum(
        "sc,cl->sl", pick.astype(jnp.float32), digits, precision=lax.Precision.HIGHEST
    )
    extra = jnp.pad(send_labels[:, None, :], ((0, 0), (0, 15), (0, B - 4))).astype(jnp.bfloat16)
    payload = jnp.concatenate([send_set, extra], axis=1).reshape(groups, CAP, B + 16, B)
    lane = lax.axis_index("rep")
    got = [jnp.take(payload, lane, axis=0)]
    for shift in range(1, groups):
        ahead = (lane + shift) % groups
        got.append(from_behind(jnp.take(payload, ahead, axis=0), "rep", shift))
    slots = groups * CAP
    got = jnp.stack(got).reshape(slots, B + 16, B)
    contact_set = lax.optimization_barrier(got[:, :B, :])
    digits = got[:, B, :4].astype(jnp.int32)
    got_labels = digits[:, :2] * 256 + digits[:, 2:]
    near_index = got_labels[:, 0]
    far_index = got_labels[:, 1]
    nodes = rhs.shape[0]
    blocks = jnp.arange(nodes, dtype=jnp.int32)[None, :]
    near_collect = (near_index[:, None] == blocks).astype(jnp.float32)
    far_collect = (far_index[:, None] == blocks).astype(jnp.float32)
    mirror_onehot = (off_cols.reshape(-1)[:, None] == blocks).astype(jnp.float32)
    tables = (
        mirror_onehot.astype(jnp.bfloat16),
        mirror_onehot,
        near_collect,
        far_collect,
        near_collect,
        far_collect,
    )
    link_tile = link_tiles[0]
    scale = precond[:, None, :]
    solution = jnp.zeros_like(rhs)
    residual = rhs
    preconditioned = scale * residual
    direction = preconditioned
    for step in range(ITERS):
        image = apply_operator(direction, diag_tiles, off_tiles, link_tile, contact_set, tables)
        parts = [
            jnp.sum(direction * image, axis=(0, 2)),
            jnp.sum(residual * preconditioned, axis=(0, 2)),
        ]
        if step < ITERS - 1:
            parts.append(jnp.sum(preconditioned * image, axis=(0, 2)))
            parts.append(jnp.sum(image * (scale * image), axis=(0, 2)))
        sums = total(jnp.stack(parts))
        curve, res_dot = sums[0], sums[1]
        alpha = res_dot / curve
        solution = solution + alpha[None, :, None] * direction
        residual = residual - alpha[None, :, None] * image
        if step < ITERS - 1:
            preconditioned = scale * residual
            next_dot = res_dot - 2.0 * alpha * sums[2] + alpha * alpha * sums[3]
            direction = preconditioned + (next_dot / res_dot)[None, :, None] * direction
    return (solution, residual)


def solution(mesh):
    in_specs = (
        P(("dom", "rep"), None, None),
        P(("dom", "rep"), None),
        P(("dom", "rep"), None, None),
        P(("dom", "rep"), None, None, None),
        P(("dom", "rep"), None),
        P(("dom", "rep"), None, None),
        P(("dom", "rep"), None, None),
        P(("dom", "rep"), None),
        P(("dom", "rep")),
        P(("dom", "rep")),
    )
    out_specs = (P(("dom", "rep"), None, None), P(("dom", "rep"), None, None))
    return jax.shard_map(body, mesh=mesh, in_specs=in_specs, out_specs=out_specs, check_vma=False)
```

```python
import jax
import jax.numpy as jnp
from jax import lax
from jax.sharding import PartitionSpec as P

B = 128
ITERS = 4
CAP = 8


def from_behind(value, axis, steps):
    count = lax.axis_size(axis)
    pairs = [(source, (source + steps) % count) for source in range(count)]
    return lax.ppermute(value, axis, pairs)


def partner(value, axis, distance):
    return lax.ppermute(value, axis, [(i, i ^ 1 << distance) for i in range(lax.axis_size(axis))])


def total(value):
    count = lax.axis_size("dom") * lax.axis_size("rep")
    spread = jnp.broadcast_to(value[None], (count,) + value.shape)
    gathered = lax.all_to_all(spread, ("dom", "rep"), 0, 0, tiled=True)
    return jnp.sum(gathered, axis=0)


def local_stiffness(rounded, diag_tiles, off_tiles, cols_onehot, mirror_onehot):
    result = jnp.einsum("nrk,nkj->nrj", rounded, diag_tiles, preferred_element_type=jnp.float32)
    picked = jnp.einsum(
        "pn,nrk->prk", cols_onehot, rounded, preferred_element_type=jnp.float32
    ).astype(jnp.bfloat16)
    picked = picked.reshape(off_tiles.shape[0], off_tiles.shape[1], rounded.shape[1], rounded.shape[2])
    result = result + jnp.einsum(
        "nmrk,nmkj->nrj", picked, off_tiles, preferred_element_type=jnp.float32
    )
    mirror = jnp.einsum("nrk,nmjk->nmrj", rounded, off_tiles, preferred_element_type=jnp.float32)
    mirror = mirror.reshape(-1, rounded.shape[1], rounded.shape[2])
    return result + jnp.einsum("pn,prj->nrj", mirror_onehot, mirror, precision=lax.Precision.HIGHEST)


def apply_operator(vector, other, diag_tiles, off_tiles, link_tile, contact_set, tables):
    cols_onehot, mirror_onehot, near_onehot, far_onehot, near_collect, far_collect = tables
    nodes = vector.shape[0]
    rounded = vector.astype(jnp.bfloat16)
    before = from_behind(rounded[nodes - 1], "rep", 1)
    near = jnp.einsum("sn,nrk->srk", near_onehot, vector, precision=lax.Precision.HIGHEST)
    far = jnp.einsum("sn,nrk->srk", far_onehot, other, precision=lax.Precision.HIGHEST)
    difference = (near - far).astype(jnp.bfloat16)
    multiplier = jnp.einsum(
        "srk,skj->srj", difference, contact_set, preferred_element_type=jnp.float32
    ).astype(jnp.bfloat16)
    terms = jnp.einsum("srj,skj->srk", multiplier, contact_set, preferred_element_type=jnp.float32)
    far_sum = jnp.einsum("sn,srk->nrk", far_collect, terms, precision=lax.Precision.HIGHEST)
    far_sum, rounded, terms = lax.optimization_barrier(
        (far_sum.astype(jnp.bfloat16), rounded, terms)
    )
    far_terms = partner(far_sum, "dom", 0).astype(jnp.float32)
    back_term = lax.dot_general(
        rounded[0], link_tile, (((1,), (1,)), ((), ())), preferred_element_type=jnp.float32
    )
    after = from_behind(back_term, "rep", -1)
    result = local_stiffness(rounded, diag_tiles, off_tiles, cols_onehot, mirror_onehot)
    first_add = jnp.dot(before, link_tile, preferred_element_type=jnp.float32)
    ends = jnp.concatenate(
        [first_add[None], jnp.zeros((nodes - 2,) + first_add.shape, jnp.float32), after[None]]
    )
    result = result + ends
    result = result + jnp.einsum("sn,srk->nrk", near_collect, terms, precision=lax.Precision.HIGHEST)
    return result - far_terms


def body(
    rhs,
    precond,
    diag_tiles,
    off_tiles,
    off_cols,
    link_tiles,
    contact_tiles,
    contact_owner,
    contact_anode,
    contact_bnode,
):
    groups = lax.axis_size("rep")
    target = contact_owner[:, 0]
    choose = (target[:, None] == jnp.arange(groups, dtype=jnp.int32)[None, :]).astype(jnp.int32)
    rank = jnp.sum((jnp.cumsum(choose, axis=0) - choose) * choose, axis=1)
    slot_of = target * CAP + rank
    pick = slot_of[None, :] == jnp.arange(groups * CAP, dtype=jnp.int32)[:, None]
    send_set = jnp.einsum(
        "sc,cij->sij", pick.astype(jnp.bfloat16), contact_tiles, preferred_element_type=jnp.float32
    ).astype(jnp.bfloat16).reshape(groups, CAP, B, B)
    labels = jnp.stack([contact_anode, contact_bnode], axis=1)
    send_labels = jnp.sum(
        jnp.where(pick[:, :, None], labels[None, :, :], 0), axis=1
    ).reshape(groups, CAP, 2)
    lane = lax.axis_index("rep")
    got_set = [jnp.take(send_set, lane, axis=0)]
    got_labels = [jnp.take(send_labels, lane, axis=0)]
    for shift in range(1, groups):
        ahead = (lane + shift) % groups
        got_set.append(from_behind(jnp.take(send_set, ahead, axis=0), "rep", shift))
        got_labels.append(from_behind(jnp.take(send_labels, ahead, axis=0), "rep", shift))
    got_set = jnp.stack(got_set)
    got_labels = jnp.stack(got_labels)
    slots = groups * CAP
    contact_set = got_set.reshape(slots, B, B)
    got_labels = got_labels.reshape(slots, 2)
    near_index = got_labels[:, 0]
    far_index = got_labels[:, 1]
    nodes = rhs.shape[0]
    blocks = jnp.arange(nodes, dtype=jnp.int32)[None, :]
    near_collect = (near_index[:, None] == blocks).astype(jnp.float32)
    far_collect = (far_index[:, None] == blocks).astype(jnp.float32)
    mirror_onehot = (off_cols.reshape(-1)[:, None] == blocks).astype(jnp.float32)
    tables = (
        mirror_onehot.astype(jnp.bfloat16),
        mirror_onehot,
        near_collect,
        far_collect,
        near_collect,
        far_collect,
    )
    link_tile = link_tiles[0]
    scale = precond[:, None, :]
    solution = jnp.zeros_like(rhs)
    residual = rhs
    preconditioned = scale * residual
    direction = preconditioned
    mate_scale = partner(precond, "dom", 0)[:, None, :]
    mate_residual = partner(rhs, "dom", 0)
    mate_direction = mate_scale * mate_residual
    for step in range(ITERS):
        image = apply_operator(
            direction, mate_direction, diag_tiles, off_tiles, link_tile, contact_set, tables
        )
        parts = [
            jnp.sum(direction * image, axis=(0, 2)),
            jnp.sum(residual * preconditioned, axis=(0, 2)),
        ]
        if step < ITERS - 1:
            mate_image = partner(image, "dom", 0)
            parts.append(jnp.sum(preconditioned * image, axis=(0, 2)))
            parts.append(jnp.sum(image * (scale * image), axis=(0, 2)))
        sums = total(jnp.stack(parts))
        curve, res_dot = sums[0], sums[1]
        alpha = res_dot / curve
        solution = solution + alpha[None, :, None] * direction
        residual = residual - alpha[None, :, None] * image
        if step < ITERS - 1:
            next_dot = res_dot - 2.0 * alpha * sums[2] + alpha * alpha * sums[3]
            beta = (next_dot / res_dot)[None, :, None]
            preconditioned = scale * residual
            direction = preconditioned + beta * direction
            mate_residual = mate_residual - alpha[None, :, None] * mate_image
            mate_direction = mate_scale * mate_residual + beta * mate_direction
    return (solution, residual)


def solution(mesh):
    in_specs = (
        P(("dom", "rep"), None, None),
        P(("dom", "rep"), None),
        P(("dom", "rep"), None, None),
        P(("dom", "rep"), None, None, None),
        P(("dom", "rep"), None),
        P(("dom", "rep"), None, None),
        P(("dom", "rep"), None, None),
        P(("dom", "rep"), None),
        P(("dom", "rep")),
        P(("dom", "rep")),
    )
    out_specs = (P(("dom", "rep"), None, None), P(("dom", "rep"), None, None))
    return jax.shard_map(body, mesh=mesh, in_specs=in_specs, out_specs=out_specs, check_vma=False)
```

```python
import jax
import jax.numpy as jnp
from jax import lax
from jax.sharding import PartitionSpec as P

B = 128
ITERS = 4
CAP = 8


def from_behind(value, axis, steps):
    count = lax.axis_size(axis)
    pairs = [(source, (source + steps) % count) for source in range(count)]
    return lax.ppermute(value, axis, pairs)


def partner(value, axis, distance):
    return lax.ppermute(value, axis, [(i, i ^ 1 << distance) for i in range(lax.axis_size(axis))])


def total(value):
    count = lax.axis_size("dom") * lax.axis_size("rep")
    spread = jnp.broadcast_to(value[None], (count,) + value.shape)
    gathered = lax.all_to_all(spread, ("dom", "rep"), 0, 0, tiled=True)
    return jnp.sum(gathered, axis=0)


def local_stiffness(rounded, diag_tiles, off_tiles, cols_onehot, mirror_onehot):
    result = jnp.einsum("nrk,nkj->nrj", rounded, diag_tiles, preferred_element_type=jnp.float32)
    picked = jnp.einsum(
        "pn,nrk->prk", cols_onehot, rounded, preferred_element_type=jnp.float32
    ).astype(jnp.bfloat16)
    picked = picked.reshape(off_tiles.shape[0], off_tiles.shape[1], rounded.shape[1], rounded.shape[2])
    result = result + jnp.einsum(
        "nmrk,nmkj->nrj", picked, off_tiles, preferred_element_type=jnp.float32
    )
    mirror = jnp.einsum("nrk,nmjk->nmrj", rounded, off_tiles, preferred_element_type=jnp.float32)
    mirror = mirror.reshape(-1, rounded.shape[1], rounded.shape[2])
    return result + jnp.einsum("pn,prj->nrj", mirror_onehot, mirror, precision=lax.Precision.HIGHEST)


def apply_operator(vector, diag_tiles, off_tiles, link_tile, contact_set, tables):
    cols_onehot, mirror_onehot, near_onehot, far_onehot, near_collect, far_collect = tables
    nodes = vector.shape[0]
    rounded = vector.astype(jnp.bfloat16)
    before = from_behind(rounded[nodes - 1], "rep", 1)
    other = partner(rounded, "dom", 0).astype(vector.dtype)
    result = local_stiffness(rounded, diag_tiles, off_tiles, cols_onehot, mirror_onehot)
    near = jnp.einsum("sn,nrk->srk", near_onehot, vector, precision=lax.Precision.HIGHEST)
    far = jnp.einsum("sn,nrk->srk", far_onehot, other, precision=lax.Precision.HIGHEST)
    difference = (near - far).astype(jnp.bfloat16)
    multiplier = jnp.einsum(
        "srk,skj->srj", difference, contact_set, preferred_element_type=jnp.float32
    ).astype(jnp.bfloat16)
    terms = jnp.einsum("srj,skj->srk", multiplier, contact_set, preferred_element_type=jnp.float32)
    far_sum = jnp.einsum("sn,srk->nrk", far_collect, terms, precision=lax.Precision.HIGHEST)
    far_sum, rounded, terms = lax.optimization_barrier(
        (far_sum.astype(jnp.bfloat16), rounded, terms)
    )
    far_terms = partner(far_sum, "dom", 0).astype(jnp.float32)
    back_term = lax.dot_general(
        rounded[0], link_tile, (((1,), (1,)), ((), ())), preferred_element_type=jnp.float32
    )
    after = from_behind(back_term, "rep", -1)
    first_add = jnp.dot(before, link_tile, preferred_element_type=jnp.float32)
    ends = jnp.concatenate(
        [first_add[None], jnp.zeros((nodes - 2,) + first_add.shape, jnp.float32), after[None]]
    )
    result = result + ends
    result = result + jnp.einsum("sn,srk->nrk", near_collect, terms, precision=lax.Precision.HIGHEST)
    return result - far_terms


def body(
    rhs,
    precond,
    diag_tiles,
    off_tiles,
    off_cols,
    link_tiles,
    contact_tiles,
    contact_owner,
    contact_anode,
    contact_bnode,
):
    groups = lax.axis_size("rep")
    target = contact_owner[:, 0]
    choose = (target[:, None] == jnp.arange(groups, dtype=jnp.int32)[None, :]).astype(jnp.int32)
    rank = jnp.sum((jnp.cumsum(choose, axis=0) - choose) * choose, axis=1)
    slot_of = target * CAP + rank
    pick = slot_of[None, :] == jnp.arange(groups * CAP, dtype=jnp.int32)[:, None]
    send_set = jnp.einsum(
        "sc,cij->sij", pick.astype(jnp.bfloat16), contact_tiles, preferred_element_type=jnp.float32
    ).astype(jnp.bfloat16).reshape(groups, CAP, B, B)
    labels = jnp.stack([contact_anode, contact_bnode], axis=1)
    send_labels = jnp.sum(
        jnp.where(pick[:, :, None], labels[None, :, :], 0), axis=1
    ).reshape(groups, CAP, 2)
    lane = lax.axis_index("rep")
    got_set = [jnp.take(send_set, lane, axis=0)]
    got_labels = [jnp.take(send_labels, lane, axis=0)]
    for shift in range(1, groups):
        ahead = (lane + shift) % groups
        got_set.append(from_behind(jnp.take(send_set, ahead, axis=0), "rep", shift))
        got_labels.append(from_behind(jnp.take(send_labels, ahead, axis=0), "rep", shift))
    got_set = jnp.stack(got_set)
    got_labels = jnp.stack(got_labels)
    slots = groups * CAP
    contact_set = got_set.reshape(slots, B, B)
    got_labels = got_labels.reshape(slots, 2)
    near_index = got_labels[:, 0]
    far_index = got_labels[:, 1]
    nodes = rhs.shape[0]
    blocks = jnp.arange(nodes, dtype=jnp.int32)[None, :]
    near_collect = (near_index[:, None] == blocks).astype(jnp.float32)
    far_collect = (far_index[:, None] == blocks).astype(jnp.float32)
    mirror_onehot = (off_cols.reshape(-1)[:, None] == blocks).astype(jnp.float32)
    tables = (
        mirror_onehot.astype(jnp.bfloat16),
        mirror_onehot,
        near_collect,
        far_collect,
        near_collect,
        far_collect,
    )
    link_tile = link_tiles[0]
    scale = precond[:, None, :]
    solution = jnp.zeros_like(rhs)
    residual = rhs
    preconditioned = scale * residual
    direction = preconditioned
    for step in range(ITERS):
        image = apply_operator(direction, diag_tiles, off_tiles, link_tile, contact_set, tables)
        parts = [
            jnp.sum(direction * image, axis=(0, 2)),
            jnp.sum(residual * preconditioned, axis=(0, 2)),
        ]
        if step < ITERS - 1:
            parts.append(jnp.sum(preconditioned * image, axis=(0, 2)))
            parts.append(jnp.sum(image * (scale * image), axis=(0, 2)))
        sums = total(jnp.stack(parts))
        curve, res_dot = sums[0], sums[1]
        alpha = res_dot / curve
        solution = solution + alpha[None, :, None] * direction
        residual = residual - alpha[None, :, None] * image
        if step < ITERS - 1:
            preconditioned = scale * residual
            next_dot = res_dot - 2.0 * alpha * sums[2] + alpha * alpha * sums[3]
            direction = preconditioned + (next_dot / res_dot)[None, :, None] * direction
    return (solution, residual)


def solution(mesh):
    in_specs = (
        P(("dom", "rep"), None, None),
        P(("dom", "rep"), None),
        P(("dom", "rep"), None, None),
        P(("dom", "rep"), None, None, None),
        P(("dom", "rep"), None),
        P(("dom", "rep"), None, None),
        P(("dom", "rep"), None, None),
        P(("dom", "rep"), None),
        P(("dom", "rep")),
        P(("dom", "rep")),
    )
    out_specs = (P(("dom", "rep"), None, None), P(("dom", "rep"), None, None))
    return jax.shard_map(body, mesh=mesh, in_specs=in_specs, out_specs=out_specs, check_vma=False)
```

```python
import jax
import jax.numpy as jnp
from jax import lax
from jax.sharding import PartitionSpec as P

B = 128
ITERS = 4
CAP = 8


def from_behind(value, axis, steps):
    count = lax.axis_size(axis)
    pairs = [(source, (source + steps) % count) for source in range(count)]
    return lax.ppermute(value, axis, pairs)


def partner(value, axis, distance):
    return lax.ppermute(value, axis, [(i, i ^ 1 << distance) for i in range(lax.axis_size(axis))])


def total(value):
    count = lax.axis_size("dom") * lax.axis_size("rep")
    flat = value.reshape(-1)
    spread = jnp.broadcast_to(flat[None, None], (count, 8, flat.shape[0]))
    gathered = lax.all_to_all(spread, ("dom", "rep"), 0, 0, tiled=True)
    return jnp.sum(gathered[:, 0], axis=0).reshape(value.shape)


def local_stiffness(rounded, diag_tiles, off_tiles, cols_onehot, mirror_onehot):
    result = jnp.einsum("nrk,nkj->nrj", rounded, diag_tiles, preferred_element_type=jnp.float32)
    picked = jnp.einsum(
        "pn,nrk->prk", cols_onehot, rounded, preferred_element_type=jnp.float32
    ).astype(jnp.bfloat16)
    picked = picked.reshape(off_tiles.shape[0], off_tiles.shape[1], rounded.shape[1], rounded.shape[2])
    result = result + jnp.einsum(
        "nmrk,nmkj->nrj", picked, off_tiles, preferred_element_type=jnp.float32
    )
    mirror = jnp.einsum("nrk,nmjk->nmrj", rounded, off_tiles, preferred_element_type=jnp.float32)
    mirror = mirror.reshape(-1, rounded.shape[1], rounded.shape[2])
    return result + jnp.einsum("pn,prj->nrj", mirror_onehot, mirror, precision=lax.Precision.HIGHEST)


def apply_operator(vector, diag_tiles, off_tiles, link_tile, contact_set, tables):
    cols_onehot, mirror_onehot, near_onehot, far_onehot, near_collect, far_collect = tables
    nodes = vector.shape[0]
    rounded = vector.astype(jnp.bfloat16)
    before = from_behind(rounded[nodes - 1], "rep", 1)
    other = partner(rounded, "dom", 0).astype(vector.dtype)
    near = jnp.einsum("sn,nrk->srk", near_onehot, vector, precision=lax.Precision.HIGHEST)
    far = jnp.einsum("sn,nrk->srk", far_onehot, other, precision=lax.Precision.HIGHEST)
    difference = (near - far).astype(jnp.bfloat16)
    multiplier = jnp.einsum(
        "srk,skj->srj", difference, contact_set, preferred_element_type=jnp.float32
    ).astype(jnp.bfloat16)
    terms = jnp.einsum("srj,skj->srk", multiplier, contact_set, preferred_element_type=jnp.float32)
    far_sum = jnp.einsum("sn,srk->nrk", far_collect, terms, precision=lax.Precision.HIGHEST)
    far_sum, rounded, terms = lax.optimization_barrier(
        (far_sum.astype(jnp.bfloat16), rounded, terms)
    )
    far_terms = partner(far_sum, "dom", 0).astype(jnp.float32)
    back_term = lax.dot_general(
        rounded[0], link_tile, (((1,), (1,)), ((), ())), preferred_element_type=jnp.float32
    )
    after = from_behind(back_term, "rep", -1)
    result = local_stiffness(rounded, diag_tiles, off_tiles, cols_onehot, mirror_onehot)
    first_add = jnp.dot(before, link_tile, preferred_element_type=jnp.float32)
    ends = jnp.concatenate(
        [first_add[None], jnp.zeros((nodes - 2,) + first_add.shape, jnp.float32), after[None]]
    )
    result = result + ends
    result = result + jnp.einsum("sn,srk->nrk", near_collect, terms, precision=lax.Precision.HIGHEST)
    return result - far_terms


def body(
    rhs,
    precond,
    diag_tiles,
    off_tiles,
    off_cols,
    link_tiles,
    contact_tiles,
    contact_owner,
    contact_anode,
    contact_bnode,
):
    groups = lax.axis_size("rep")
    target = contact_owner[:, 0]
    choose = (target[:, None] == jnp.arange(groups, dtype=jnp.int32)[None, :]).astype(jnp.int32)
    rank = jnp.sum((jnp.cumsum(choose, axis=0) - choose) * choose, axis=1)
    slot_of = target * CAP + rank
    pick = slot_of[None, :] == jnp.arange(groups * CAP, dtype=jnp.int32)[:, None]
    send_set = jnp.einsum(
        "sc,cij->sij", pick.astype(jnp.bfloat16), contact_tiles, preferred_element_type=jnp.float32
    ).astype(jnp.bfloat16).reshape(groups, CAP, B, B)
    labels = jnp.stack([contact_anode, contact_bnode], axis=1)
    send_labels = jnp.sum(
        jnp.where(pick[:, :, None], labels[None, :, :], 0), axis=1
    ).reshape(groups, CAP, 2)
    lane = lax.axis_index("rep")
    got_set = [jnp.take(send_set, lane, axis=0)]
    got_labels = [jnp.take(send_labels, lane, axis=0)]
    for shift in range(1, groups):
        ahead = (lane + shift) % groups
        got_set.append(from_behind(jnp.take(send_set, ahead, axis=0), "rep", shift))
        got_labels.append(from_behind(jnp.take(send_labels, ahead, axis=0), "rep", shift))
    got_set = jnp.stack(got_set)
    got_labels = jnp.stack(got_labels)
    slots = groups * CAP
    contact_set = got_set.reshape(slots, B, B)
    got_labels = got_labels.reshape(slots, 2)
    near_index = got_labels[:, 0]
    far_index = got_labels[:, 1]
    nodes = rhs.shape[0]
    blocks = jnp.arange(nodes, dtype=jnp.int32)[None, :]
    near_collect = (near_index[:, None] == blocks).astype(jnp.float32)
    far_collect = (far_index[:, None] == blocks).astype(jnp.float32)
    mirror_onehot = (off_cols.reshape(-1)[:, None] == blocks).astype(jnp.float32)
    tables = (
        mirror_onehot.astype(jnp.bfloat16),
        mirror_onehot,
        near_collect,
        far_collect,
        near_collect,
        far_collect,
    )
    link_tile = link_tiles[0]
    scale = precond[:, None, :]
    solution = jnp.zeros_like(rhs)
    residual = rhs
    preconditioned = scale * residual
    direction = preconditioned
    for step in range(ITERS):
        image = apply_operator(direction, diag_tiles, off_tiles, link_tile, contact_set, tables)
        parts = [
            jnp.sum(direction * image, axis=(0, 2)),
            jnp.sum(residual * preconditioned, axis=(0, 2)),
        ]
        if step < ITERS - 1:
            parts.append(jnp.sum(preconditioned * image, axis=(0, 2)))
            parts.append(jnp.sum(image * (scale * image), axis=(0, 2)))
        sums = total(jnp.stack(parts))
        curve, res_dot = sums[0], sums[1]
        alpha = res_dot / curve
        solution = solution + alpha[None, :, None] * direction
        residual = residual - alpha[None, :, None] * image
        if step < ITERS - 1:
            preconditioned = scale * residual
            next_dot = res_dot - 2.0 * alpha * sums[2] + alpha * alpha * sums[3]
            direction = preconditioned + (next_dot / res_dot)[None, :, None] * direction
    return (solution, residual)


def solution(mesh):
    in_specs = (
        P(("dom", "rep"), None, None),
        P(("dom", "rep"), None),
        P(("dom", "rep"), None, None),
        P(("dom", "rep"), None, None, None),
        P(("dom", "rep"), None),
        P(("dom", "rep"), None, None),
        P(("dom", "rep"), None, None),
        P(("dom", "rep"), None),
        P(("dom", "rep")),
        P(("dom", "rep")),
    )
    out_specs = (P(("dom", "rep"), None, None), P(("dom", "rep"), None, None))
    return jax.shard_map(body, mesh=mesh, in_specs=in_specs, out_specs=out_specs, check_vma=False)
```

```python
import jax
import jax.numpy as jnp
from jax import lax
from jax.sharding import PartitionSpec as P

B = 128
ITERS = 4
CAP = 8


def from_behind(value, axis, steps):
    count = lax.axis_size(axis)
    pairs = [(source, (source + steps) % count) for source in range(count)]
    return lax.ppermute(value, axis, pairs)


def partner(value, axis, distance):
    return lax.ppermute(value, axis, [(i, i ^ 1 << distance) for i in range(lax.axis_size(axis))])


def total(value):
    count = lax.axis_size("dom") * lax.axis_size("rep")
    spread = jnp.broadcast_to(value[None], (count,) + value.shape)
    gathered = lax.all_to_all(spread, ("rep", "dom"), 0, 0, tiled=True)
    return jnp.sum(gathered, axis=0)


def local_stiffness(rounded, diag_tiles, off_tiles, cols_onehot, mirror_onehot):
    result = jnp.einsum("nrk,nkj->nrj", rounded, diag_tiles, preferred_element_type=jnp.float32)
    picked = jnp.einsum(
        "pn,nrk->prk", cols_onehot, rounded, preferred_element_type=jnp.float32
    ).astype(jnp.bfloat16)
    picked = picked.reshape(off_tiles.shape[0], off_tiles.shape[1], rounded.shape[1], rounded.shape[2])
    result = result + jnp.einsum(
        "nmrk,nmkj->nrj", picked, off_tiles, preferred_element_type=jnp.float32
    )
    mirror = jnp.einsum("nrk,nmjk->nmrj", rounded, off_tiles, preferred_element_type=jnp.float32)
    mirror = mirror.reshape(-1, rounded.shape[1], rounded.shape[2])
    return result + jnp.einsum("pn,prj->nrj", mirror_onehot, mirror, precision=lax.Precision.HIGHEST)


def apply_operator(vector, diag_tiles, off_tiles, link_tile, contact_set, tables):
    cols_onehot, mirror_onehot, near_onehot, far_onehot, near_collect, far_collect = tables
    nodes = vector.shape[0]
    rounded = vector.astype(jnp.bfloat16)
    before = from_behind(rounded[nodes - 1], "rep", 1)
    other = partner(rounded, "dom", 0).astype(vector.dtype)
    near = jnp.einsum("sn,nrk->srk", near_onehot, vector, precision=lax.Precision.HIGHEST)
    far = jnp.einsum("sn,nrk->srk", far_onehot, other, precision=lax.Precision.HIGHEST)
    difference = (near - far).astype(jnp.bfloat16)
    multiplier = jnp.einsum(
        "srk,skj->srj", difference, contact_set, preferred_element_type=jnp.float32
    ).astype(jnp.bfloat16)
    terms = jnp.einsum("srj,skj->srk", multiplier, contact_set, preferred_element_type=jnp.float32)
    far_sum = jnp.einsum("sn,srk->nrk", far_collect, terms, precision=lax.Precision.HIGHEST)
    far_sum, rounded, terms = lax.optimization_barrier(
        (far_sum.astype(jnp.bfloat16), rounded, terms)
    )
    far_terms = partner(far_sum, "dom", 0).astype(jnp.float32)
    back_term = lax.dot_general(
        rounded[0], link_tile, (((1,), (1,)), ((), ())), preferred_element_type=jnp.float32
    )
    after = from_behind(back_term, "rep", -1)
    result = local_stiffness(rounded, diag_tiles, off_tiles, cols_onehot, mirror_onehot)
    first_add = jnp.dot(before, link_tile, preferred_element_type=jnp.float32)
    ends = jnp.concatenate(
        [first_add[None], jnp.zeros((nodes - 2,) + first_add.shape, jnp.float32), after[None]]
    )
    result = result + ends
    result = result + jnp.einsum("sn,srk->nrk", near_collect, terms, precision=lax.Precision.HIGHEST)
    return result - far_terms


def body(
    rhs,
    precond,
    diag_tiles,
    off_tiles,
    off_cols,
    link_tiles,
    contact_tiles,
    contact_owner,
    contact_anode,
    contact_bnode,
):
    groups = lax.axis_size("rep")
    target = contact_owner[:, 0]
    choose = (target[:, None] == jnp.arange(groups, dtype=jnp.int32)[None, :]).astype(jnp.int32)
    rank = jnp.sum((jnp.cumsum(choose, axis=0) - choose) * choose, axis=1)
    slot_of = target * CAP + rank
    pick = slot_of[None, :] == jnp.arange(groups * CAP, dtype=jnp.int32)[:, None]
    send_set = jnp.einsum(
        "sc,cij->sij", pick.astype(jnp.bfloat16), contact_tiles, preferred_element_type=jnp.float32
    ).astype(jnp.bfloat16).reshape(groups, CAP, B, B)
    labels = jnp.stack([contact_anode, contact_bnode], axis=1)
    send_labels = jnp.sum(
        jnp.where(pick[:, :, None], labels[None, :, :], 0), axis=1
    ).reshape(groups, CAP, 2)
    lane = lax.axis_index("rep")
    got_set = [jnp.take(send_set, lane, axis=0)]
    got_labels = [jnp.take(send_labels, lane, axis=0)]
    for shift in range(1, groups):
        ahead = (lane + shift) % groups
        got_set.append(from_behind(jnp.take(send_set, ahead, axis=0), "rep", shift))
        got_labels.append(from_behind(jnp.take(send_labels, ahead, axis=0), "rep", shift))
    got_set = jnp.stack(got_set)
    got_labels = jnp.stack(got_labels)
    slots = groups * CAP
    contact_set = got_set.reshape(slots, B, B)
    got_labels = got_labels.reshape(slots, 2)
    near_index = got_labels[:, 0]
    far_index = got_labels[:, 1]
    nodes = rhs.shape[0]
    blocks = jnp.arange(nodes, dtype=jnp.int32)[None, :]
    near_collect = (near_index[:, None] == blocks).astype(jnp.float32)
    far_collect = (far_index[:, None] == blocks).astype(jnp.float32)
    mirror_onehot = (off_cols.reshape(-1)[:, None] == blocks).astype(jnp.float32)
    tables = (
        mirror_onehot.astype(jnp.bfloat16),
        mirror_onehot,
        near_collect,
        far_collect,
        near_collect,
        far_collect,
    )
    link_tile = link_tiles[0]
    scale = precond[:, None, :]
    solution = jnp.zeros_like(rhs)
    residual = rhs
    preconditioned = scale * residual
    direction = preconditioned
    for step in range(ITERS):
        image = apply_operator(direction, diag_tiles, off_tiles, link_tile, contact_set, tables)
        parts = [
            jnp.sum(direction * image, axis=(0, 2)),
            jnp.sum(residual * preconditioned, axis=(0, 2)),
        ]
        if step < ITERS - 1:
            parts.append(jnp.sum(preconditioned * image, axis=(0, 2)))
            parts.append(jnp.sum(image * (scale * image), axis=(0, 2)))
        sums = total(jnp.stack(parts))
        curve, res_dot = sums[0], sums[1]
        alpha = res_dot / curve
        solution = solution + alpha[None, :, None] * direction
        residual = residual - alpha[None, :, None] * image
        if step < ITERS - 1:
            preconditioned = scale * residual
            next_dot = res_dot - 2.0 * alpha * sums[2] + alpha * alpha * sums[3]
            direction = preconditioned + (next_dot / res_dot)[None, :, None] * direction
    return (solution, residual)


def solution(mesh):
    in_specs = (
        P(("dom", "rep"), None, None),
        P(("dom", "rep"), None),
        P(("dom", "rep"), None, None),
        P(("dom", "rep"), None, None, None),
        P(("dom", "rep"), None),
        P(("dom", "rep"), None, None),
        P(("dom", "rep"), None, None),
        P(("dom", "rep"), None),
        P(("dom", "rep")),
        P(("dom", "rep")),
    )
    out_specs = (P(("dom", "rep"), None, None), P(("dom", "rep"), None, None))
    return jax.shard_map(body, mesh=mesh, in_specs=in_specs, out_specs=out_specs, check_vma=False)
```

```python
import jax
import jax.numpy as jnp
from jax import lax
from jax.sharding import PartitionSpec as P

B = 128
ITERS = 4
CAP = 8


def from_behind(value, axis, steps):
    count = lax.axis_size(axis)
    pairs = [(source, (source + steps) % count) for source in range(count)]
    return lax.ppermute(value, axis, pairs)


def partner(value, axis, distance):
    return lax.ppermute(value, axis, [(i, i ^ 1 << distance) for i in range(lax.axis_size(axis))])


def total(value):
    count = lax.axis_size("dom") * lax.axis_size("rep")
    spread = jnp.broadcast_to(value[None], (count,) + value.shape)
    gathered = lax.all_to_all(spread, ("dom", "rep"), 0, 0, tiled=True)
    return jnp.sum(gathered, axis=0)


def local_stiffness(rounded, diag_tiles, off_tiles, cols_onehot, mirror_onehot):
    result = jnp.einsum("nrk,nkj->nrj", rounded, diag_tiles, preferred_element_type=jnp.float32)
    picked = jnp.einsum(
        "pn,nrk->prk", cols_onehot, rounded, preferred_element_type=jnp.float32
    ).astype(jnp.bfloat16)
    picked = picked.reshape(off_tiles.shape[0], off_tiles.shape[1], rounded.shape[1], rounded.shape[2])
    result = result + jnp.einsum(
        "nmrk,nmkj->nrj", picked, off_tiles, preferred_element_type=jnp.float32
    )
    mirror = jnp.einsum("nrk,nmjk->nmrj", rounded, off_tiles, preferred_element_type=jnp.float32)
    mirror = mirror.reshape(-1, rounded.shape[1], rounded.shape[2])
    return result + jnp.einsum("pn,prj->nrj", mirror_onehot, mirror, precision=lax.Precision.HIGHEST)


def apply_operator(vector, diag_tiles, off_tiles, link_tile, contact_set, tables):
    cols_onehot, mirror_onehot, near_onehot, far_onehot, near_collect, far_collect = tables
    nodes = vector.shape[0]
    rounded = vector.astype(jnp.bfloat16)
    other = partner(rounded, "dom", 0).astype(vector.dtype)
    near = jnp.einsum("sn,nrk->srk", near_onehot, vector, precision=lax.Precision.HIGHEST)
    far = jnp.einsum("sn,nrk->srk", far_onehot, other, precision=lax.Precision.HIGHEST)
    difference = (near - far).astype(jnp.bfloat16)
    multiplier = jnp.einsum(
        "srk,skj->srj", difference, contact_set, preferred_element_type=jnp.float32
    ).astype(jnp.bfloat16)
    terms = jnp.einsum("srj,skj->srk", multiplier, contact_set, preferred_element_type=jnp.float32)
    far_sum = jnp.einsum("sn,srk->nrk", far_collect, terms, precision=lax.Precision.HIGHEST)
    far_sum, rounded, terms = lax.optimization_barrier(
        (far_sum.astype(jnp.bfloat16), rounded, terms)
    )
    far_terms = partner(far_sum, "dom", 0).astype(jnp.float32)
    back_term = lax.dot_general(
        rounded[0], link_tile, (((1,), (1,)), ((), ())), preferred_element_type=jnp.float32
    )
    after = from_behind(back_term, "rep", -1)
    before = from_behind(rounded[nodes - 1], "rep", 1)
    result = local_stiffness(rounded, diag_tiles, off_tiles, cols_onehot, mirror_onehot)
    first_add = jnp.dot(before, link_tile, preferred_element_type=jnp.float32)
    ends = jnp.concatenate(
        [first_add[None], jnp.zeros((nodes - 2,) + first_add.shape, jnp.float32), after[None]]
    )
    result = result + ends
    result = result + jnp.einsum("sn,srk->nrk", near_collect, terms, precision=lax.Precision.HIGHEST)
    return result - far_terms


def body(
    rhs,
    precond,
    diag_tiles,
    off_tiles,
    off_cols,
    link_tiles,
    contact_tiles,
    contact_owner,
    contact_anode,
    contact_bnode,
):
    groups = lax.axis_size("rep")
    target = contact_owner[:, 0]
    choose = (target[:, None] == jnp.arange(groups, dtype=jnp.int32)[None, :]).astype(jnp.int32)
    rank = jnp.sum((jnp.cumsum(choose, axis=0) - choose) * choose, axis=1)
    slot_of = target * CAP + rank
    pick = slot_of[None, :] == jnp.arange(groups * CAP, dtype=jnp.int32)[:, None]
    send_set = jnp.einsum(
        "sc,cij->sij", pick.astype(jnp.bfloat16), contact_tiles, preferred_element_type=jnp.float32
    ).astype(jnp.bfloat16).reshape(groups, CAP, B, B)
    labels = jnp.stack([contact_anode, contact_bnode], axis=1)
    send_labels = jnp.sum(
        jnp.where(pick[:, :, None], labels[None, :, :], 0), axis=1
    ).reshape(groups, CAP, 2)
    lane = lax.axis_index("rep")
    got_set = [jnp.take(send_set, lane, axis=0)]
    got_labels = [jnp.take(send_labels, lane, axis=0)]
    for shift in range(1, groups):
        ahead = (lane + shift) % groups
        got_set.append(from_behind(jnp.take(send_set, ahead, axis=0), "rep", shift))
        got_labels.append(from_behind(jnp.take(send_labels, ahead, axis=0), "rep", shift))
    got_set = jnp.stack(got_set)
    got_labels = jnp.stack(got_labels)
    slots = groups * CAP
    contact_set = got_set.reshape(slots, B, B)
    got_labels = got_labels.reshape(slots, 2)
    near_index = got_labels[:, 0]
    far_index = got_labels[:, 1]
    nodes = rhs.shape[0]
    blocks = jnp.arange(nodes, dtype=jnp.int32)[None, :]
    near_collect = (near_index[:, None] == blocks).astype(jnp.float32)
    far_collect = (far_index[:, None] == blocks).astype(jnp.float32)
    mirror_onehot = (off_cols.reshape(-1)[:, None] == blocks).astype(jnp.float32)
    tables = (
        mirror_onehot.astype(jnp.bfloat16),
        mirror_onehot,
        near_collect,
        far_collect,
        near_collect,
        far_collect,
    )
    link_tile = link_tiles[0]
    scale = precond[:, None, :]
    solution = jnp.zeros_like(rhs)
    residual = rhs
    preconditioned = scale * residual
    direction = preconditioned
    for step in range(ITERS):
        image = apply_operator(direction, diag_tiles, off_tiles, link_tile, contact_set, tables)
        parts = [
            jnp.sum(direction * image, axis=(0, 2)),
            jnp.sum(residual * preconditioned, axis=(0, 2)),
        ]
        if step < ITERS - 1:
            parts.append(jnp.sum(preconditioned * image, axis=(0, 2)))
            parts.append(jnp.sum(image * (scale * image), axis=(0, 2)))
        sums = total(jnp.stack(parts))
        curve, res_dot = sums[0], sums[1]
        alpha = res_dot / curve
        solution = solution + alpha[None, :, None] * direction
        residual = residual - alpha[None, :, None] * image
        if step < ITERS - 1:
            preconditioned = scale * residual
            next_dot = res_dot - 2.0 * alpha * sums[2] + alpha * alpha * sums[3]
            direction = preconditioned + (next_dot / res_dot)[None, :, None] * direction
    return (solution, residual)


def solution(mesh):
    in_specs = (
        P(("dom", "rep"), None, None),
        P(("dom", "rep"), None),
        P(("dom", "rep"), None, None),
        P(("dom", "rep"), None, None, None),
        P(("dom", "rep"), None),
        P(("dom", "rep"), None, None),
        P(("dom", "rep"), None, None),
        P(("dom", "rep"), None),
        P(("dom", "rep")),
        P(("dom", "rep")),
    )
    out_specs = (P(("dom", "rep"), None, None), P(("dom", "rep"), None, None))
    return jax.shard_map(body, mesh=mesh, in_specs=in_specs, out_specs=out_specs, check_vma=False)
```

```python
import jax
import jax.numpy as jnp
from jax import lax
from jax.sharding import PartitionSpec as P

B = 128
ITERS = 4
CAP = 8


def from_behind(value, axis, steps):
    count = lax.axis_size(axis)
    pairs = [(source, (source + steps) % count) for source in range(count)]
    return lax.ppermute(value, axis, pairs)


def partner(value, axis, distance):
    return lax.ppermute(value, axis, [(i, i ^ 1 << distance) for i in range(lax.axis_size(axis))])


def total(value):
    count = lax.axis_size("dom") * lax.axis_size("rep")
    spread = jnp.broadcast_to(value[None], (count,) + value.shape)
    gathered = lax.all_to_all(spread, ("dom", "rep"), 0, 0, tiled=True)
    return jnp.sum(gathered, axis=0)


def local_stiffness(rounded, diag_tiles, off_tiles, cols_onehot, mirror_onehot):
    result = jnp.einsum("nrk,nkj->nrj", rounded, diag_tiles, preferred_element_type=jnp.float32)
    picked = jnp.einsum(
        "pn,nrk->prk", cols_onehot, rounded, preferred_element_type=jnp.float32
    ).astype(jnp.bfloat16)
    picked = picked.reshape(off_tiles.shape[0], off_tiles.shape[1], rounded.shape[1], rounded.shape[2])
    result = result + jnp.einsum(
        "nmrk,nmkj->nrj", picked, off_tiles, preferred_element_type=jnp.float32
    )
    mirror = jnp.einsum("nrk,nmjk->nmrj", rounded, off_tiles, preferred_element_type=jnp.float32)
    mirror = mirror.reshape(-1, rounded.shape[1], rounded.shape[2])
    return result + jnp.einsum("pn,prj->nrj", mirror_onehot, mirror, precision=lax.Precision.HIGHEST)


def apply_operator(vector, diag_tiles, off_tiles, link_tile, contact_set, tables):
    cols_onehot, mirror_onehot, near_onehot, far_onehot, near_collect, far_collect = tables
    nodes = vector.shape[0]
    rounded = vector.astype(jnp.bfloat16)
    before = from_behind(rounded[nodes - 1], "rep", 1)
    other = partner(rounded, "dom", 0).astype(vector.dtype)
    near = jnp.einsum("sn,nrk->srk", near_onehot, vector, precision=lax.Precision.HIGHEST)
    far = jnp.einsum("sn,nrk->srk", far_onehot, other, precision=lax.Precision.HIGHEST)
    difference = (near - far).astype(jnp.bfloat16)
    multiplier = jnp.einsum(
        "srk,skj->srj", difference, contact_set, preferred_element_type=jnp.float32
    ).astype(jnp.bfloat16)
    terms = jnp.einsum("srj,skj->srk", multiplier, contact_set, preferred_element_type=jnp.float32)
    far_sum = jnp.einsum("sn,srk->nrk", far_collect, terms, precision=lax.Precision.HIGHEST)
    far_sum, rounded, terms = lax.optimization_barrier(
        (far_sum.astype(jnp.bfloat16), rounded, terms)
    )
    far_terms = partner(far_sum, "dom", 0).astype(jnp.float32)
    back_term = lax.dot_general(
        rounded[0], link_tile, (((1,), (1,)), ((), ())), preferred_element_type=jnp.float32
    )
    after = from_behind(back_term, "rep", -1)
    result = local_stiffness(rounded, diag_tiles, off_tiles, cols_onehot, mirror_onehot)
    first_add = jnp.dot(before, link_tile, preferred_element_type=jnp.float32)
    ends = jnp.concatenate(
        [first_add[None], jnp.zeros((nodes - 2,) + first_add.shape, jnp.float32), after[None]]
    )
    result = result + ends
    result = result + jnp.einsum("sn,srk->nrk", near_collect, terms, precision=lax.Precision.HIGHEST)
    return result - far_terms


def body(
    rhs,
    precond,
    diag_tiles,
    off_tiles,
    off_cols,
    link_tiles,
    contact_tiles,
    contact_owner,
    contact_anode,
    contact_bnode,
):
    groups = lax.axis_size("rep")
    target = contact_owner[:, 0]
    order = jnp.arange(target.shape[0], dtype=jnp.int32)
    earlier = (target[None, :] == target[:, None]) & (order[None, :] < order[:, None])
    rank = jnp.sum(earlier.astype(jnp.int32), axis=1)
    slot_of = target * CAP + rank
    pick = slot_of[None, :] == jnp.arange(groups * CAP, dtype=jnp.int32)[:, None]
    send_set = jnp.einsum(
        "sc,cij->sij", pick.astype(jnp.bfloat16), contact_tiles, preferred_element_type=jnp.float32
    ).astype(jnp.bfloat16).reshape(groups, CAP, B, B)
    labels = jnp.stack([contact_anode, contact_bnode], axis=1)
    send_labels = jnp.sum(
        jnp.where(pick[:, :, None], labels[None, :, :], 0), axis=1
    ).reshape(groups, CAP, 2)
    lane = lax.axis_index("rep")
    got_set = [jnp.take(send_set, lane, axis=0)]
    got_labels = [jnp.take(send_labels, lane, axis=0)]
    for shift in range(1, groups):
        ahead = (lane + shift) % groups
        got_set.append(from_behind(jnp.take(send_set, ahead, axis=0), "rep", shift))
        got_labels.append(from_behind(jnp.take(send_labels, ahead, axis=0), "rep", shift))
    got_set = jnp.stack(got_set)
    got_labels = jnp.stack(got_labels)
    slots = groups * CAP
    contact_set = got_set.reshape(slots, B, B)
    got_labels = got_labels.reshape(slots, 2)
    near_index = got_labels[:, 0]
    far_index = got_labels[:, 1]
    nodes = rhs.shape[0]
    blocks = jnp.arange(nodes, dtype=jnp.int32)[None, :]
    near_collect = (near_index[:, None] == blocks).astype(jnp.float32)
    far_collect = (far_index[:, None] == blocks).astype(jnp.float32)
    mirror_onehot = (off_cols.reshape(-1)[:, None] == blocks).astype(jnp.float32)
    tables = (
        mirror_onehot.astype(jnp.bfloat16),
        mirror_onehot,
        near_collect,
        far_collect,
        near_collect,
        far_collect,
    )
    link_tile = link_tiles[0]
    scale = precond[:, None, :]
    solution = jnp.zeros_like(rhs)
    residual = rhs
    preconditioned = scale * residual
    direction = preconditioned
    for step in range(ITERS):
        image = apply_operator(direction, diag_tiles, off_tiles, link_tile, contact_set, tables)
        parts = [
            jnp.sum(direction * image, axis=(0, 2)),
            jnp.sum(residual * preconditioned, axis=(0, 2)),
        ]
        if step < ITERS - 1:
            parts.append(jnp.sum(preconditioned * image, axis=(0, 2)))
            parts.append(jnp.sum(image * (scale * image), axis=(0, 2)))
        sums = total(jnp.stack(parts))
        curve, res_dot = sums[0], sums[1]
        alpha = res_dot / curve
        solution = solution + alpha[None, :, None] * direction
        residual = residual - alpha[None, :, None] * image
        if step < ITERS - 1:
            preconditioned = scale * residual
            next_dot = res_dot - 2.0 * alpha * sums[2] + alpha * alpha * sums[3]
            direction = preconditioned + (next_dot / res_dot)[None, :, None] * direction
    return (solution, residual)


def solution(mesh):
    in_specs = (
        P(("dom", "rep"), None, None),
        P(("dom", "rep"), None),
        P(("dom", "rep"), None, None),
        P(("dom", "rep"), None, None, None),
        P(("dom", "rep"), None),
        P(("dom", "rep"), None, None),
        P(("dom", "rep"), None, None),
        P(("dom", "rep"), None),
        P(("dom", "rep")),
        P(("dom", "rep")),
    )
    out_specs = (P(("dom", "rep"), None, None), P(("dom", "rep"), None, None))
    return jax.shard_map(body, mesh=mesh, in_specs=in_specs, out_specs=out_specs, check_vma=False)
```

```python
import jax
import jax.numpy as jnp
from jax import lax
from jax.sharding import PartitionSpec as P

B = 128
ITERS = 4
CAP = 8


def from_behind(value, axis, steps):
    count = lax.axis_size(axis)
    pairs = [(source, (source + steps) % count) for source in range(count)]
    return lax.ppermute(value, axis, pairs)


def partner(value, axis, distance):
    return lax.ppermute(value, axis, [(i, i ^ 1 << distance) for i in range(lax.axis_size(axis))])


def total(value):
    count = lax.axis_size("dom") * lax.axis_size("rep")
    spread = jnp.broadcast_to(value[None], (count,) + value.shape)
    gathered = lax.all_to_all(spread, ("dom", "rep"), 0, 0, tiled=True)
    return jnp.sum(gathered, axis=0)


def local_stiffness(rounded, diag_tiles, off_tiles, cols_onehot, mirror_onehot):
    result = jnp.einsum("nrk,nkj->nrj", rounded, diag_tiles, preferred_element_type=jnp.float32)
    picked = jnp.einsum(
        "pn,nrk->prk", cols_onehot, rounded, preferred_element_type=jnp.float32
    ).astype(jnp.bfloat16)
    picked = picked.reshape(off_tiles.shape[0], off_tiles.shape[1], rounded.shape[1], rounded.shape[2])
    result = result + jnp.einsum(
        "nmrk,nmkj->nrj", picked, off_tiles, preferred_element_type=jnp.float32
    )
    mirror = jnp.einsum("nrk,nmjk->nmrj", rounded, off_tiles, preferred_element_type=jnp.float32)
    mirror = mirror.reshape(-1, rounded.shape[1], rounded.shape[2])
    return result + jnp.einsum("pn,prj->nrj", mirror_onehot, mirror, precision=lax.Precision.HIGHEST)


def apply_operator(vector, diag_tiles, off_tiles, link_tile, contact_set, tables):
    cols_onehot, mirror_onehot, near_onehot, far_onehot, near_collect, far_collect = tables
    nodes = vector.shape[0]
    rounded = vector.astype(jnp.bfloat16)
    before = from_behind(rounded[nodes - 1], "rep", 1)
    other = partner(rounded, "dom", 0).astype(vector.dtype)
    near = jnp.einsum("sn,nrk->srk", near_onehot, vector, precision=lax.Precision.HIGHEST)
    far = jnp.einsum("sn,nrk->srk", far_onehot, other, precision=lax.Precision.HIGHEST)
    difference = (near - far).astype(jnp.bfloat16)
    multiplier = jnp.einsum(
        "srk,skj->srj", difference, contact_set, preferred_element_type=jnp.float32
    ).astype(jnp.bfloat16)
    terms = jnp.einsum("srj,skj->srk", multiplier, contact_set, preferred_element_type=jnp.float32)
    far_sum = jnp.einsum("sn,srk->nrk", far_collect, terms, precision=lax.Precision.HIGHEST)
    far_sum, rounded, terms = lax.optimization_barrier(
        (far_sum.astype(jnp.bfloat16), rounded, terms)
    )
    far_terms = partner(far_sum, "dom", 0).astype(jnp.float32)
    back_term = lax.dot_general(
        rounded[0], link_tile, (((1,), (1,)), ((), ())), preferred_element_type=jnp.float32
    )
    after = from_behind(back_term, "rep", -1)
    result = local_stiffness(rounded, diag_tiles, off_tiles, cols_onehot, mirror_onehot)
    first_add = jnp.dot(before, link_tile, preferred_element_type=jnp.float32)
    ends = jnp.concatenate(
        [first_add[None], jnp.zeros((nodes - 2,) + first_add.shape, jnp.float32), after[None]]
    )
    result = result + ends
    result = result + jnp.einsum("sn,srk->nrk", near_collect, terms, precision=lax.Precision.HIGHEST)
    return result - far_terms


def body(
    rhs,
    precond,
    diag_tiles,
    off_tiles,
    off_cols,
    link_tiles,
    contact_tiles,
    contact_owner,
    contact_anode,
    contact_bnode,
):
    groups = lax.axis_size("rep")
    target = contact_owner[:, 0]
    order = jnp.arange(target.shape[0], dtype=jnp.int32)
    earlier = (target[None, :] == target[:, None]) & (order[None, :] < order[:, None])
    itself = jnp.where(order[None, :] == order[:, None], target[:, None] * CAP, 0)
    slot_of = jnp.sum(earlier.astype(jnp.int32) + itself, axis=1)
    pick = slot_of[None, :] == jnp.arange(groups * CAP, dtype=jnp.int32)[:, None]
    send_set = jnp.einsum(
        "sc,cij->sij", pick.astype(jnp.bfloat16), contact_tiles, preferred_element_type=jnp.float32
    ).astype(jnp.bfloat16).reshape(groups, CAP, B, B)
    labels = jnp.stack([contact_anode, contact_bnode], axis=1)
    send_labels = jnp.sum(
        jnp.where(pick[:, :, None], labels[None, :, :], 0), axis=1
    ).reshape(groups, CAP, 2)
    lane = lax.axis_index("rep")
    got_set = [jnp.take(send_set, lane, axis=0)]
    got_labels = [jnp.take(send_labels, lane, axis=0)]
    for shift in range(1, groups):
        ahead = (lane + shift) % groups
        got_set.append(from_behind(jnp.take(send_set, ahead, axis=0), "rep", shift))
        got_labels.append(from_behind(jnp.take(send_labels, ahead, axis=0), "rep", shift))
    got_set = jnp.stack(got_set)
    got_labels = jnp.stack(got_labels)
    slots = groups * CAP
    contact_set = got_set.reshape(slots, B, B)
    got_labels = got_labels.reshape(slots, 2)
    near_index = got_labels[:, 0]
    far_index = got_labels[:, 1]
    nodes = rhs.shape[0]
    blocks = jnp.arange(nodes, dtype=jnp.int32)[None, :]
    near_collect = (near_index[:, None] == blocks).astype(jnp.float32)
    far_collect = (far_index[:, None] == blocks).astype(jnp.float32)
    mirror_onehot = (off_cols.reshape(-1)[:, None] == blocks).astype(jnp.float32)
    tables = (
        mirror_onehot.astype(jnp.bfloat16),
        mirror_onehot,
        near_collect,
        far_collect,
        near_collect,
        far_collect,
    )
    link_tile = link_tiles[0]
    scale = precond[:, None, :]
    solution = jnp.zeros_like(rhs)
    residual = rhs
    preconditioned = scale * residual
    direction = preconditioned
    for step in range(ITERS):
        image = apply_operator(direction, diag_tiles, off_tiles, link_tile, contact_set, tables)
        parts = [
            jnp.sum(direction * image, axis=(0, 2)),
            jnp.sum(residual * preconditioned, axis=(0, 2)),
        ]
        if step < ITERS - 1:
            parts.append(jnp.sum(preconditioned * image, axis=(0, 2)))
            parts.append(jnp.sum(image * (scale * image), axis=(0, 2)))
        sums = total(jnp.stack(parts))
        curve, res_dot = sums[0], sums[1]
        alpha = res_dot / curve
        solution = solution + alpha[None, :, None] * direction
        residual = residual - alpha[None, :, None] * image
        if step < ITERS - 1:
            preconditioned = scale * residual
            next_dot = res_dot - 2.0 * alpha * sums[2] + alpha * alpha * sums[3]
            direction = preconditioned + (next_dot / res_dot)[None, :, None] * direction
    return (solution, residual)


def solution(mesh):
    in_specs = (
        P(("dom", "rep"), None, None),
        P(("dom", "rep"), None),
        P(("dom", "rep"), None, None),
        P(("dom", "rep"), None, None, None),
        P(("dom", "rep"), None),
        P(("dom", "rep"), None, None),
        P(("dom", "rep"), None, None),
        P(("dom", "rep"), None),
        P(("dom", "rep")),
        P(("dom", "rep")),
    )
    out_specs = (P(("dom", "rep"), None, None), P(("dom", "rep"), None, None))
    return jax.shard_map(body, mesh=mesh, in_specs=in_specs, out_specs=out_specs, check_vma=False)
```

```python
import jax
import jax.numpy as jnp
from jax import lax
from jax.sharding import PartitionSpec as P

B = 128
ITERS = 4
CAP = 8


def from_behind(value, axis, steps):
    count = lax.axis_size(axis)
    pairs = [(source, (source + steps) % count) for source in range(count)]
    return lax.ppermute(value, axis, pairs)


def partner(value, axis, distance):
    return lax.ppermute(value, axis, [(i, i ^ 1 << distance) for i in range(lax.axis_size(axis))])


def total(value):
    count = lax.axis_size("dom") * lax.axis_size("rep")
    spread = jnp.broadcast_to(value[None], (count,) + value.shape)
    gathered = lax.all_to_all(spread, ("dom", "rep"), 0, 0, tiled=True)
    return jnp.sum(gathered, axis=0)


def local_stiffness(rounded, diag_tiles, off_tiles, cols_onehot, mirror_onehot):
    result = jnp.einsum("nrk,nkj->nrj", rounded, diag_tiles, preferred_element_type=jnp.float32)
    picked = jnp.einsum(
        "pn,nrk->prk", cols_onehot, rounded, preferred_element_type=jnp.float32
    ).astype(jnp.bfloat16)
    picked = picked.reshape(off_tiles.shape[0], off_tiles.shape[1], rounded.shape[1], rounded.shape[2])
    result = result + jnp.einsum(
        "nmrk,nmkj->nrj", picked, off_tiles, preferred_element_type=jnp.float32
    )
    mirror = jnp.einsum("nrk,nmjk->nmrj", rounded, off_tiles, preferred_element_type=jnp.float32)
    mirror = mirror.reshape(-1, rounded.shape[1], rounded.shape[2])
    return result + jnp.einsum("pn,prj->nrj", mirror_onehot, mirror, precision=lax.Precision.HIGHEST)


def apply_operator(vector, diag_tiles, off_tiles, link_tile, contact_set, tables):
    cols_onehot, mirror_onehot, near_onehot, far_onehot, near_collect, far_collect = tables
    nodes = vector.shape[0]
    rounded = vector.astype(jnp.bfloat16)
    before = from_behind(rounded[nodes - 1], "rep", 1)
    other = partner(rounded, "dom", 0)
    near = jnp.einsum("sn,nrk->srk", near_onehot, vector, precision=lax.Precision.HIGHEST)
    far = jnp.einsum("sn,nrk->srk", far_onehot, other, preferred_element_type=jnp.float32)
    difference = (near - far).astype(jnp.bfloat16)
    multiplier = jnp.einsum(
        "srk,skj->srj", difference, contact_set, preferred_element_type=jnp.float32
    ).astype(jnp.bfloat16)
    terms = jnp.einsum("srj,skj->srk", multiplier, contact_set, preferred_element_type=jnp.float32)
    far_sum = jnp.einsum("sn,srk->nrk", far_collect, terms, precision=lax.Precision.HIGHEST)
    far_sum, rounded, terms = lax.optimization_barrier(
        (far_sum.astype(jnp.bfloat16), rounded, terms)
    )
    far_terms = partner(far_sum, "dom", 0).astype(jnp.float32)
    back_term = lax.dot_general(
        rounded[0], link_tile, (((1,), (1,)), ((), ())), preferred_element_type=jnp.float32
    )
    after = from_behind(back_term, "rep", -1)
    result = local_stiffness(rounded, diag_tiles, off_tiles, cols_onehot, mirror_onehot)
    first_add = jnp.dot(before, link_tile, preferred_element_type=jnp.float32)
    ends = jnp.concatenate(
        [first_add[None], jnp.zeros((nodes - 2,) + first_add.shape, jnp.float32), after[None]]
    )
    result = result + ends
    result = result + jnp.einsum("sn,srk->nrk", near_collect, terms, precision=lax.Precision.HIGHEST)
    return result - far_terms


def body(
    rhs,
    precond,
    diag_tiles,
    off_tiles,
    off_cols,
    link_tiles,
    contact_tiles,
    contact_owner,
    contact_anode,
    contact_bnode,
):
    groups = lax.axis_size("rep")
    target = contact_owner[:, 0]
    order = jnp.arange(target.shape[0], dtype=jnp.int32)
    earlier = (target[None, :] == target[:, None]) & (order[None, :] < order[:, None])
    itself = jnp.where(order[None, :] == order[:, None], target[:, None] * CAP, 0)
    slot_of = jnp.sum(earlier.astype(jnp.int32) + itself, axis=1)
    pick = slot_of[None, :] == jnp.arange(groups * CAP, dtype=jnp.int32)[:, None]
    send_set = jnp.einsum(
        "sc,cij->sij", pick.astype(jnp.bfloat16), contact_tiles, preferred_element_type=jnp.float32
    ).astype(jnp.bfloat16).reshape(groups, CAP, B, B)
    labels = jnp.stack([contact_anode, contact_bnode], axis=1)
    send_labels = jnp.sum(
        jnp.where(pick[:, :, None], labels[None, :, :], 0), axis=1
    ).reshape(groups, CAP, 2)
    lane = lax.axis_index("rep")
    got_set = [jnp.take(send_set, lane, axis=0)]
    got_labels = [jnp.take(send_labels, lane, axis=0)]
    for shift in range(1, groups):
        ahead = (lane + shift) % groups
        got_set.append(from_behind(jnp.take(send_set, ahead, axis=0), "rep", shift))
        got_labels.append(from_behind(jnp.take(send_labels, ahead, axis=0), "rep", shift))
    got_set = jnp.stack(got_set)
    got_labels = jnp.stack(got_labels)
    slots = groups * CAP
    contact_set = got_set.reshape(slots, B, B)
    got_labels = got_labels.reshape(slots, 2)
    near_index = got_labels[:, 0]
    far_index = got_labels[:, 1]
    nodes = rhs.shape[0]
    blocks = jnp.arange(nodes, dtype=jnp.int32)[None, :]
    near_collect = (near_index[:, None] == blocks).astype(jnp.float32)
    far_collect = (far_index[:, None] == blocks).astype(jnp.float32)
    mirror_onehot = (off_cols.reshape(-1)[:, None] == blocks).astype(jnp.float32)
    tables = (
        mirror_onehot.astype(jnp.bfloat16),
        mirror_onehot,
        near_collect,
        far_collect.astype(jnp.bfloat16),
        near_collect,
        far_collect,
    )
    link_tile = link_tiles[0]
    scale = precond[:, None, :]
    solution = jnp.zeros_like(rhs)
    residual = rhs
    preconditioned = scale * residual
    direction = preconditioned
    for step in range(ITERS):
        image = apply_operator(direction, diag_tiles, off_tiles, link_tile, contact_set, tables)
        parts = [
            jnp.sum(direction * image, axis=(0, 2)),
            jnp.sum(residual * preconditioned, axis=(0, 2)),
        ]
        if step < ITERS - 1:
            parts.append(jnp.sum(preconditioned * image, axis=(0, 2)))
            parts.append(jnp.sum(image * (scale * image), axis=(0, 2)))
        sums = total(jnp.stack(parts))
        curve, res_dot = sums[0], sums[1]
        alpha = res_dot / curve
        solution = solution + alpha[None, :, None] * direction
        residual = residual - alpha[None, :, None] * image
        if step < ITERS - 1:
            preconditioned = scale * residual
            next_dot = res_dot - 2.0 * alpha * sums[2] + alpha * alpha * sums[3]
            direction = preconditioned + (next_dot / res_dot)[None, :, None] * direction
    return (solution, residual)


def solution(mesh):
    in_specs = (
        P(("dom", "rep"), None, None),
        P(("dom", "rep"), None),
        P(("dom", "rep"), None, None),
        P(("dom", "rep"), None, None, None),
        P(("dom", "rep"), None),
        P(("dom", "rep"), None, None),
        P(("dom", "rep"), None, None),
        P(("dom", "rep"), None),
        P(("dom", "rep")),
        P(("dom", "rep")),
    )
    out_specs = (P(("dom", "rep"), None, None), P(("dom", "rep"), None, None))
    return jax.shard_map(body, mesh=mesh, in_specs=in_specs, out_specs=out_specs, check_vma=False)
```

```python
import jax
import jax.numpy as jnp
from jax import lax
from jax.sharding import PartitionSpec as P

B = 128
ITERS = 4
CAP = 8


def from_behind(value, axis, steps):
    count = lax.axis_size(axis)
    pairs = [(source, (source + steps) % count) for source in range(count)]
    return lax.ppermute(value, axis, pairs)


def partner(value, axis, distance):
    return lax.ppermute(value, axis, [(i, i ^ 1 << distance) for i in range(lax.axis_size(axis))])


def total(value):
    count = lax.axis_size("dom") * lax.axis_size("rep")
    spread = jnp.broadcast_to(value[None], (count,) + value.shape)
    gathered = lax.all_to_all(spread, ("dom", "rep"), 0, 0, tiled=True)
    return jnp.sum(gathered, axis=0)


def local_stiffness(rounded, diag_tiles, off_tiles, cols_onehot, mirror_onehot):
    result = jnp.einsum("nrk,nkj->nrj", rounded, diag_tiles, preferred_element_type=jnp.float32)
    picked = jnp.einsum(
        "pn,nrk->prk", cols_onehot, rounded, preferred_element_type=jnp.float32
    ).astype(jnp.bfloat16)
    picked = picked.reshape(off_tiles.shape[0], off_tiles.shape[1], rounded.shape[1], rounded.shape[2])
    result = result + jnp.einsum(
        "nmrk,nmkj->nrj", picked, off_tiles, preferred_element_type=jnp.float32
    )
    mirror = jnp.einsum("nrk,nmjk->nmrj", rounded, off_tiles, preferred_element_type=jnp.float32)
    mirror = mirror.reshape(-1, rounded.shape[1], rounded.shape[2])
    return result + jnp.einsum("pn,prj->nrj", mirror_onehot, mirror, precision=lax.Precision.HIGHEST)


def apply_operator(vector, diag_tiles, off_tiles, link_tile, contact_set, tables):
    cols_onehot, mirror_onehot, near_onehot, far_onehot, near_collect, far_pick = tables
    nodes = vector.shape[0]
    rounded = vector.astype(jnp.bfloat16)
    before = from_behind(rounded[nodes - 1], "rep", 1)
    other = partner(rounded, "dom", 0).astype(vector.dtype)
    near = jnp.einsum("sn,nrk->srk", near_onehot, vector, precision=lax.Precision.HIGHEST)
    far = jnp.einsum("sn,nrk->srk", far_onehot, other, precision=lax.Precision.HIGHEST)
    difference = (near - far).astype(jnp.bfloat16)
    multiplier = jnp.einsum(
        "srk,skj->srj", difference, contact_set, preferred_element_type=jnp.float32
    ).astype(jnp.bfloat16)
    spread = far_pick[:, :, None, None] * multiplier[:, None, :, :]
    far_sum = jnp.einsum("snrj,skj->nrk", spread, contact_set, preferred_element_type=jnp.float32)
    far_sum, rounded, multiplier = lax.optimization_barrier(
        (far_sum.astype(jnp.bfloat16), rounded, multiplier)
    )
    terms = jnp.einsum("srj,skj->srk", multiplier, contact_set, preferred_element_type=jnp.float32)
    far_terms = partner(far_sum, "dom", 0).astype(jnp.float32)
    back_term = lax.dot_general(
        rounded[0], link_tile, (((1,), (1,)), ((), ())), preferred_element_type=jnp.float32
    )
    after = from_behind(back_term, "rep", -1)
    result = local_stiffness(rounded, diag_tiles, off_tiles, cols_onehot, mirror_onehot)
    first_add = jnp.dot(before, link_tile, preferred_element_type=jnp.float32)
    ends = jnp.concatenate(
        [first_add[None], jnp.zeros((nodes - 2,) + first_add.shape, jnp.float32), after[None]]
    )
    result = result + ends
    result = result + jnp.einsum("sn,srk->nrk", near_collect, terms, precision=lax.Precision.HIGHEST)
    return result - far_terms


def body(
    rhs,
    precond,
    diag_tiles,
    off_tiles,
    off_cols,
    link_tiles,
    contact_tiles,
    contact_owner,
    contact_anode,
    contact_bnode,
):
    groups = lax.axis_size("rep")
    target = contact_owner[:, 0]
    order = jnp.arange(target.shape[0], dtype=jnp.int32)
    earlier = (target[None, :] == target[:, None]) & (order[None, :] < order[:, None])
    itself = jnp.where(order[None, :] == order[:, None], target[:, None] * CAP, 0)
    slot_of = jnp.sum(earlier.astype(jnp.int32) + itself, axis=1)
    pick = slot_of[None, :] == jnp.arange(groups * CAP, dtype=jnp.int32)[:, None]
    send_set = jnp.einsum(
        "sc,cij->sij", pick.astype(jnp.bfloat16), contact_tiles, preferred_element_type=jnp.float32
    ).astype(jnp.bfloat16).reshape(groups, CAP, B, B)
    labels = jnp.stack([contact_anode, contact_bnode], axis=1)
    send_labels = jnp.sum(
        jnp.where(pick[:, :, None], labels[None, :, :], 0), axis=1
    ).reshape(groups, CAP, 2)
    lane = lax.axis_index("rep")
    got_set = [jnp.take(send_set, lane, axis=0)]
    got_labels = [jnp.take(send_labels, lane, axis=0)]
    for shift in range(1, groups):
        ahead = (lane + shift) % groups
        got_set.append(from_behind(jnp.take(send_set, ahead, axis=0), "rep", shift))
        got_labels.append(from_behind(jnp.take(send_labels, ahead, axis=0), "rep", shift))
    got_set = jnp.stack(got_set)
    got_labels = jnp.stack(got_labels)
    slots = groups * CAP
    contact_set = got_set.reshape(slots, B, B)
    got_labels = got_labels.reshape(slots, 2)
    near_index = got_labels[:, 0]
    far_index = got_labels[:, 1]
    nodes = rhs.shape[0]
    blocks = jnp.arange(nodes, dtype=jnp.int32)[None, :]
    near_collect = (near_index[:, None] == blocks).astype(jnp.float32)
    far_collect = (far_index[:, None] == blocks).astype(jnp.float32)
    mirror_onehot = (off_cols.reshape(-1)[:, None] == blocks).astype(jnp.float32)
    tables = (
        mirror_onehot.astype(jnp.bfloat16),
        mirror_onehot,
        near_collect,
        far_collect,
        near_collect,
        far_collect.astype(jnp.bfloat16),
    )
    link_tile = link_tiles[0]
    scale = precond[:, None, :]
    solution = jnp.zeros_like(rhs)
    residual = rhs
    preconditioned = scale * residual
    direction = preconditioned
    for step in range(ITERS):
        image = apply_operator(direction, diag_tiles, off_tiles, link_tile, contact_set, tables)
        parts = [
            jnp.sum(direction * image, axis=(0, 2)),
            jnp.sum(residual * preconditioned, axis=(0, 2)),
        ]
        if step < ITERS - 1:
            parts.append(jnp.sum(preconditioned * image, axis=(0, 2)))
            parts.append(jnp.sum(image * (scale * image), axis=(0, 2)))
        sums = total(jnp.stack(parts))
        curve, res_dot = sums[0], sums[1]
        alpha = res_dot / curve
        solution = solution + alpha[None, :, None] * direction
        residual = residual - alpha[None, :, None] * image
        if step < ITERS - 1:
            preconditioned = scale * residual
            next_dot = res_dot - 2.0 * alpha * sums[2] + alpha * alpha * sums[3]
            direction = preconditioned + (next_dot / res_dot)[None, :, None] * direction
    return (solution, residual)


def solution(mesh):
    in_specs = (
        P(("dom", "rep"), None, None),
        P(("dom", "rep"), None),
        P(("dom", "rep"), None, None),
        P(("dom", "rep"), None, None, None),
        P(("dom", "rep"), None),
        P(("dom", "rep"), None, None),
        P(("dom", "rep"), None, None),
        P(("dom", "rep"), None),
        P(("dom", "rep")),
        P(("dom", "rep")),
    )
    out_specs = (P(("dom", "rep"), None, None), P(("dom", "rep"), None, None))
    return jax.shard_map(body, mesh=mesh, in_specs=in_specs, out_specs=out_specs, check_vma=False)
```

```python
import jax
import jax.numpy as jnp
from jax import lax
from jax.sharding import PartitionSpec as P

B = 128
ITERS = 4
CAP = 8


def from_behind(value, axis, steps):
    count = lax.axis_size(axis)
    pairs = [(source, (source + steps) % count) for source in range(count)]
    return lax.ppermute(value, axis, pairs)


def partner(value, axis, distance):
    return lax.ppermute(value, axis, [(i, i ^ 1 << distance) for i in range(lax.axis_size(axis))])


def total(value):
    count = lax.axis_size("dom") * lax.axis_size("rep")
    spread = jnp.broadcast_to(value[None], (count,) + value.shape)
    gathered = lax.all_to_all(spread, ("dom", "rep"), 0, 0, tiled=True)
    return jnp.sum(gathered, axis=0)


def local_stiffness(rounded, diag_tiles, off_tiles, cols_onehot, mirror_onehot):
    result = jnp.einsum("nrk,nkj->nrj", rounded, diag_tiles, preferred_element_type=jnp.float32)
    picked = jnp.einsum(
        "pn,nrk->prk", cols_onehot, rounded, preferred_element_type=jnp.float32
    ).astype(jnp.bfloat16)
    picked = picked.reshape(off_tiles.shape[0], off_tiles.shape[1], rounded.shape[1], rounded.shape[2])
    result = result + jnp.einsum(
        "nmrk,nmkj->nrj", picked, off_tiles, preferred_element_type=jnp.float32
    )
    mirror = jnp.einsum("nrk,nmjk->nmrj", rounded, off_tiles, preferred_element_type=jnp.float32)
    mirror = mirror.reshape(-1, rounded.shape[1], rounded.shape[2])
    return result + jnp.einsum("pn,prj->nrj", mirror_onehot, mirror, precision=lax.Precision.HIGHEST)


def apply_operator(vector, diag_tiles, off_tiles, link_tile, contact_set, tables):
    cols_onehot, mirror_onehot, near_onehot, far_onehot, near_pick, far_pick = tables
    nodes = vector.shape[0]
    rounded = vector.astype(jnp.bfloat16)
    before = from_behind(rounded[nodes - 1], "rep", 1)
    other = partner(rounded, "dom", 0).astype(vector.dtype)
    near = jnp.einsum("sn,nrk->srk", near_onehot, vector, precision=lax.Precision.HIGHEST)
    far = jnp.einsum("sn,nrk->srk", far_onehot, other, precision=lax.Precision.HIGHEST)
    difference = (near - far).astype(jnp.bfloat16)
    multiplier = jnp.einsum(
        "srk,skj->srj", difference, contact_set, preferred_element_type=jnp.float32
    ).astype(jnp.bfloat16)
    spread = far_pick[:, :, None, None] * multiplier[:, None, :, :]
    far_sum = jnp.einsum("snrj,skj->nrk", spread, contact_set, preferred_element_type=jnp.float32)
    far_sum, rounded, multiplier = lax.optimization_barrier(
        (far_sum.astype(jnp.bfloat16), rounded, multiplier)
    )
    far_terms = partner(far_sum, "dom", 0).astype(jnp.float32)
    back_term = lax.dot_general(
        rounded[0], link_tile, (((1,), (1,)), ((), ())), preferred_element_type=jnp.float32
    )
    after = from_behind(back_term, "rep", -1)
    result = local_stiffness(rounded, diag_tiles, off_tiles, cols_onehot, mirror_onehot)
    first_add = jnp.dot(before, link_tile, preferred_element_type=jnp.float32)
    ends = jnp.concatenate(
        [first_add[None], jnp.zeros((nodes - 2,) + first_add.shape, jnp.float32), after[None]]
    )
    result = result + ends
    near_spread = near_pick[:, :, None, None] * multiplier[:, None, :, :]
    result = result + jnp.einsum(
        "snrj,skj->nrk", near_spread, contact_set, preferred_element_type=jnp.float32
    )
    return result - far_terms


def body(
    rhs,
    precond,
    diag_tiles,
    off_tiles,
    off_cols,
    link_tiles,
    contact_tiles,
    contact_owner,
    contact_anode,
    contact_bnode,
):
    groups = lax.axis_size("rep")
    target = contact_owner[:, 0]
    order = jnp.arange(target.shape[0], dtype=jnp.int32)
    earlier = (target[None, :] == target[:, None]) & (order[None, :] < order[:, None])
    itself = jnp.where(order[None, :] == order[:, None], target[:, None] * CAP, 0)
    slot_of = jnp.sum(earlier.astype(jnp.int32) + itself, axis=1)
    pick = slot_of[None, :] == jnp.arange(groups * CAP, dtype=jnp.int32)[:, None]
    send_set = jnp.einsum(
        "sc,cij->sij", pick.astype(jnp.bfloat16), contact_tiles, preferred_element_type=jnp.float32
    ).astype(jnp.bfloat16).reshape(groups, CAP, B, B)
    labels = jnp.stack([contact_anode, contact_bnode], axis=1)
    send_labels = jnp.sum(
        jnp.where(pick[:, :, None], labels[None, :, :], 0), axis=1
    ).reshape(groups, CAP, 2)
    lane = lax.axis_index("rep")
    got_set = [jnp.take(send_set, lane, axis=0)]
    got_labels = [jnp.take(send_labels, lane, axis=0)]
    for shift in range(1, groups):
        ahead = (lane + shift) % groups
        got_set.append(from_behind(jnp.take(send_set, ahead, axis=0), "rep", shift))
        got_labels.append(from_behind(jnp.take(send_labels, ahead, axis=0), "rep", shift))
    got_set = jnp.stack(got_set)
    got_labels = jnp.stack(got_labels)
    slots = groups * CAP
    contact_set = got_set.reshape(slots, B, B)
    got_labels = got_labels.reshape(slots, 2)
    near_index = got_labels[:, 0]
    far_index = got_labels[:, 1]
    nodes = rhs.shape[0]
    blocks = jnp.arange(nodes, dtype=jnp.int32)[None, :]
    near_collect = (near_index[:, None] == blocks).astype(jnp.float32)
    far_collect = (far_index[:, None] == blocks).astype(jnp.float32)
    mirror_onehot = (off_cols.reshape(-1)[:, None] == blocks).astype(jnp.float32)
    tables = (
        mirror_onehot.astype(jnp.bfloat16),
        mirror_onehot,
        near_collect,
        far_collect,
        near_collect.astype(jnp.bfloat16),
        far_collect.astype(jnp.bfloat16),
    )
    link_tile = link_tiles[0]
    scale = precond[:, None, :]
    solution = jnp.zeros_like(rhs)
    residual = rhs
    preconditioned = scale * residual
    direction = preconditioned
    for step in range(ITERS):
        image = apply_operator(direction, diag_tiles, off_tiles, link_tile, contact_set, tables)
        parts = [
            jnp.sum(direction * image, axis=(0, 2)),
            jnp.sum(residual * preconditioned, axis=(0, 2)),
        ]
        if step < ITERS - 1:
            parts.append(jnp.sum(preconditioned * image, axis=(0, 2)))
            parts.append(jnp.sum(image * (scale * image), axis=(0, 2)))
        sums = total(jnp.stack(parts))
        curve, res_dot = sums[0], sums[1]
        alpha = res_dot / curve
        solution = solution + alpha[None, :, None] * direction
        residual = residual - alpha[None, :, None] * image
        if step < ITERS - 1:
            preconditioned = scale * residual
            next_dot = res_dot - 2.0 * alpha * sums[2] + alpha * alpha * sums[3]
            direction = preconditioned + (next_dot / res_dot)[None, :, None] * direction
    return (solution, residual)


def solution(mesh):
    in_specs = (
        P(("dom", "rep"), None, None),
        P(("dom", "rep"), None),
        P(("dom", "rep"), None, None),
        P(("dom", "rep"), None, None, None),
        P(("dom", "rep"), None),
        P(("dom", "rep"), None, None),
        P(("dom", "rep"), None, None),
        P(("dom", "rep"), None),
        P(("dom", "rep")),
        P(("dom", "rep")),
    )
    out_specs = (P(("dom", "rep"), None, None), P(("dom", "rep"), None, None))
    return jax.shard_map(body, mesh=mesh, in_specs=in_specs, out_specs=out_specs, check_vma=False)
```

```python
import jax
import jax.numpy as jnp
from jax import lax
from jax.sharding import PartitionSpec as P

B = 128
ITERS = 4
CAP = 8


def from_behind(value, axis, steps):
    count = lax.axis_size(axis)
    pairs = [(source, (source + steps) % count) for source in range(count)]
    return lax.ppermute(value, axis, pairs)


def partner(value, axis, distance):
    return lax.ppermute(value, axis, [(i, i ^ 1 << distance) for i in range(lax.axis_size(axis))])


def total(value):
    count = lax.axis_size("dom") * lax.axis_size("rep")
    spread = jnp.broadcast_to(value[None], (count,) + value.shape)
    gathered = lax.all_to_all(spread, ("dom", "rep"), 0, 0, tiled=True)
    return jnp.sum(gathered, axis=0)


def local_stiffness(rounded, diag_tiles, off_tiles, cols_onehot, mirror_onehot):
    result = jnp.einsum("nrk,nkj->nrj", rounded, diag_tiles, preferred_element_type=jnp.float32)
    picked = jnp.einsum(
        "pn,nrk->prk", cols_onehot, rounded, preferred_element_type=jnp.float32
    ).astype(jnp.bfloat16)
    picked = picked.reshape(off_tiles.shape[0], off_tiles.shape[1], rounded.shape[1], rounded.shape[2])
    result = result + jnp.einsum(
        "nmrk,nmkj->nrj", picked, off_tiles, preferred_element_type=jnp.float32
    )
    nodes = rounded.shape[0]
    chosen = mirror_onehot.reshape(nodes, off_tiles.shape[1], nodes)
    spread = chosen[:, :, :, None, None] * rounded[:, None, None, :, :]
    return result + jnp.einsum(
        "nmirk,nmjk->irj", spread, off_tiles, preferred_element_type=jnp.float32
    )


def apply_operator(vector, diag_tiles, off_tiles, link_tile, contact_set, tables):
    cols_onehot, mirror_onehot, near_onehot, far_onehot, near_pick, far_pick = tables
    nodes = vector.shape[0]
    rounded = vector.astype(jnp.bfloat16)
    before = from_behind(rounded[nodes - 1], "rep", 1)
    other = partner(rounded, "dom", 0).astype(vector.dtype)
    near = jnp.einsum("sn,nrk->srk", near_onehot, vector, precision=lax.Precision.HIGHEST)
    far = jnp.einsum("sn,nrk->srk", far_onehot, other, precision=lax.Precision.HIGHEST)
    difference = (near - far).astype(jnp.bfloat16)
    multiplier = jnp.einsum(
        "srk,skj->srj", difference, contact_set, preferred_element_type=jnp.float32
    ).astype(jnp.bfloat16)
    spread = far_pick[:, :, None, None] * multiplier[:, None, :, :]
    far_sum = jnp.einsum("snrj,skj->nrk", spread, contact_set, preferred_element_type=jnp.float32)
    far_sum, rounded, multiplier = lax.optimization_barrier(
        (far_sum.astype(jnp.bfloat16), rounded, multiplier)
    )
    far_terms = partner(far_sum, "dom", 0).astype(jnp.float32)
    back_term = lax.dot_general(
        rounded[0], link_tile, (((1,), (1,)), ((), ())), preferred_element_type=jnp.float32
    )
    after = from_behind(back_term, "rep", -1)
    result = local_stiffness(rounded, diag_tiles, off_tiles, cols_onehot, mirror_onehot)
    first_add = jnp.dot(before, link_tile, preferred_element_type=jnp.float32)
    ends = jnp.concatenate(
        [first_add[None], jnp.zeros((nodes - 2,) + first_add.shape, jnp.float32), after[None]]
    )
    result = result + ends
    near_spread = near_pick[:, :, None, None] * multiplier[:, None, :, :]
    result = result + jnp.einsum(
        "snrj,skj->nrk", near_spread, contact_set, preferred_element_type=jnp.float32
    )
    return result - far_terms


def body(
    rhs,
    precond,
    diag_tiles,
    off_tiles,
    off_cols,
    link_tiles,
    contact_tiles,
    contact_owner,
    contact_anode,
    contact_bnode,
):
    groups = lax.axis_size("rep")
    target = contact_owner[:, 0]
    order = jnp.arange(target.shape[0], dtype=jnp.int32)
    earlier = (target[None, :] == target[:, None]) & (order[None, :] < order[:, None])
    itself = jnp.where(order[None, :] == order[:, None], target[:, None] * CAP, 0)
    slot_of = jnp.sum(earlier.astype(jnp.int32) + itself, axis=1)
    pick = slot_of[None, :] == jnp.arange(groups * CAP, dtype=jnp.int32)[:, None]
    send_set = jnp.einsum(
        "sc,cij->sij", pick.astype(jnp.bfloat16), contact_tiles, preferred_element_type=jnp.float32
    ).astype(jnp.bfloat16).reshape(groups, CAP, B, B)
    labels = jnp.stack([contact_anode, contact_bnode], axis=1)
    send_labels = jnp.sum(
        jnp.where(pick[:, :, None], labels[None, :, :], 0), axis=1
    ).reshape(groups, CAP, 2)
    lane = lax.axis_index("rep")
    got_set = [jnp.take(send_set, lane, axis=0)]
    got_labels = [jnp.take(send_labels, lane, axis=0)]
    for shift in range(1, groups):
        ahead = (lane + shift) % groups
        got_set.append(from_behind(jnp.take(send_set, ahead, axis=0), "rep", shift))
        got_labels.append(from_behind(jnp.take(send_labels, ahead, axis=0), "rep", shift))
    got_set = jnp.stack(got_set)
    got_labels = jnp.stack(got_labels)
    slots = groups * CAP
    contact_set = got_set.reshape(slots, B, B)
    got_labels = got_labels.reshape(slots, 2)
    near_index = got_labels[:, 0]
    far_index = got_labels[:, 1]
    nodes = rhs.shape[0]
    blocks = jnp.arange(nodes, dtype=jnp.int32)[None, :]
    near_collect = (near_index[:, None] == blocks).astype(jnp.float32)
    far_collect = (far_index[:, None] == blocks).astype(jnp.float32)
    mirror_onehot = (off_cols.reshape(-1)[:, None] == blocks).astype(jnp.float32)
    tables = (
        mirror_onehot.astype(jnp.bfloat16),
        mirror_onehot.astype(jnp.bfloat16),
        near_collect,
        far_collect,
        near_collect.astype(jnp.bfloat16),
        far_collect.astype(jnp.bfloat16),
    )
    link_tile = link_tiles[0]
    scale = precond[:, None, :]
    solution = jnp.zeros_like(rhs)
    residual = rhs
    preconditioned = scale * residual
    direction = preconditioned
    for step in range(ITERS):
        image = apply_operator(direction, diag_tiles, off_tiles, link_tile, contact_set, tables)
        parts = [
            jnp.sum(direction * image, axis=(0, 2)),
            jnp.sum(residual * preconditioned, axis=(0, 2)),
        ]
        if step < ITERS - 1:
            parts.append(jnp.sum(preconditioned * image, axis=(0, 2)))
            parts.append(jnp.sum(image * (scale * image), axis=(0, 2)))
        sums = total(jnp.stack(parts))
        curve, res_dot = sums[0], sums[1]
        alpha = res_dot / curve
        solution = solution + alpha[None, :, None] * direction
        residual = residual - alpha[None, :, None] * image
        if step < ITERS - 1:
            preconditioned = scale * residual
            next_dot = res_dot - 2.0 * alpha * sums[2] + alpha * alpha * sums[3]
            direction = preconditioned + (next_dot / res_dot)[None, :, None] * direction
    return (solution, residual)


def solution(mesh):
    in_specs = (
        P(("dom", "rep"), None, None),
        P(("dom", "rep"), None),
        P(("dom", "rep"), None, None),
        P(("dom", "rep"), None, None, None),
        P(("dom", "rep"), None),
        P(("dom", "rep"), None, None),
        P(("dom", "rep"), None, None),
        P(("dom", "rep"), None),
        P(("dom", "rep")),
        P(("dom", "rep")),
    )
    out_specs = (P(("dom", "rep"), None, None), P(("dom", "rep"), None, None))
    return jax.shard_map(body, mesh=mesh, in_specs=in_specs, out_specs=out_specs, check_vma=False)
```

```python
import jax
import jax.numpy as jnp
from jax import lax
from jax.sharding import PartitionSpec as P

B = 128
ITERS = 4
CAP = 8


def from_behind(value, axis, steps):
    count = lax.axis_size(axis)
    pairs = [(source, (source + steps) % count) for source in range(count)]
    return lax.ppermute(value, axis, pairs)


def partner(value, axis, distance):
    return lax.ppermute(value, axis, [(i, i ^ 1 << distance) for i in range(lax.axis_size(axis))])


def total(value):
    count = lax.axis_size("dom") * lax.axis_size("rep")
    spread = jnp.broadcast_to(value[None], (count,) + value.shape)
    gathered = lax.all_to_all(spread, ("dom", "rep"), 0, 0, tiled=True)
    return jnp.sum(gathered, axis=0)


def local_stiffness(rounded, diag_tiles, off_tiles, cols_onehot, mirror_onehot):
    result = jnp.einsum("nrk,nkj->nrj", rounded, diag_tiles, preferred_element_type=jnp.float32)
    picked = jnp.einsum(
        "pn,nrk->prk", cols_onehot, rounded, preferred_element_type=jnp.float32
    ).astype(jnp.bfloat16)
    picked = picked.reshape(off_tiles.shape[0], off_tiles.shape[1], rounded.shape[1], rounded.shape[2])
    result = result + jnp.einsum(
        "nmrk,nmkj->nrj", picked, off_tiles, preferred_element_type=jnp.float32
    )
    nodes = rounded.shape[0]
    chosen = mirror_onehot.reshape(nodes, off_tiles.shape[1], nodes)
    spread = chosen[:, :, :, None, None] * rounded[:, None, None, :, :]
    return result + jnp.einsum(
        "nmirk,nmjk->irj", spread, off_tiles, preferred_element_type=jnp.float32
    )


def apply_operator(vector, diag_tiles, off_tiles, link_tile, contact_set, tables):
    cols_onehot, mirror_onehot, near_onehot, far_onehot, near_pick, far_pick = tables
    nodes = vector.shape[0]
    rounded = vector.astype(jnp.bfloat16)
    before = from_behind(rounded[nodes - 1], "rep", 1)
    other = partner(rounded, "dom", 0).astype(vector.dtype)
    near = jnp.einsum("sn,nrk->srk", near_onehot, vector, precision=lax.Precision.HIGHEST)
    far = jnp.einsum("sn,nrk->srk", far_onehot, other, precision=lax.Precision.HIGHEST)
    difference = (near - far).astype(jnp.bfloat16)
    multiplier = jnp.einsum(
        "srk,skj->srj", difference, contact_set, preferred_element_type=jnp.float32
    ).astype(jnp.bfloat16)
    spread = far_pick[:, :, None, None] * multiplier[:, None, :, :]
    far_sum = jnp.einsum("snrj,skj->nrk", spread, contact_set, preferred_element_type=jnp.float32)
    far_sum, rounded, multiplier = lax.optimization_barrier(
        (far_sum.astype(jnp.bfloat16), rounded, multiplier)
    )
    far_terms = partner(far_sum, "dom", 0).astype(jnp.float32)
    back_term = lax.dot_general(
        rounded[0], link_tile, (((1,), (1,)), ((), ())), preferred_element_type=jnp.float32
    )
    after = from_behind(back_term, "rep", -1)
    result = local_stiffness(rounded, diag_tiles, off_tiles, cols_onehot, mirror_onehot)
    first_add = jnp.dot(before, link_tile, preferred_element_type=jnp.float32)
    ends = jnp.concatenate(
        [first_add[None], jnp.zeros((nodes - 2,) + first_add.shape, jnp.float32), after[None]]
    )
    result = result + ends
    near_spread = near_pick[:, :, None, None] * multiplier[:, None, :, :]
    result = result + jnp.einsum(
        "snrj,skj->nrk", near_spread, contact_set, preferred_element_type=jnp.float32
    )
    result = lax.optimization_barrier(result)
    return result - far_terms


def body(
    rhs,
    precond,
    diag_tiles,
    off_tiles,
    off_cols,
    link_tiles,
    contact_tiles,
    contact_owner,
    contact_anode,
    contact_bnode,
):
    groups = lax.axis_size("rep")
    target = contact_owner[:, 0]
    order = jnp.arange(target.shape[0], dtype=jnp.int32)
    earlier = (target[None, :] == target[:, None]) & (order[None, :] < order[:, None])
    itself = jnp.where(order[None, :] == order[:, None], target[:, None] * CAP, 0)
    slot_of = jnp.sum(earlier.astype(jnp.int32) + itself, axis=1)
    pick = slot_of[None, :] == jnp.arange(groups * CAP, dtype=jnp.int32)[:, None]
    send_set = jnp.einsum(
        "sc,cij->sij", pick.astype(jnp.bfloat16), contact_tiles, preferred_element_type=jnp.float32
    ).astype(jnp.bfloat16).reshape(groups, CAP, B, B)
    labels = jnp.stack([contact_anode, contact_bnode], axis=1)
    send_labels = jnp.sum(
        jnp.where(pick[:, :, None], labels[None, :, :], 0), axis=1
    ).reshape(groups, CAP, 2)
    lane = lax.axis_index("rep")
    got_set = [jnp.take(send_set, lane, axis=0)]
    got_labels = [jnp.take(send_labels, lane, axis=0)]
    for shift in range(1, groups):
        ahead = (lane + shift) % groups
        got_set.append(from_behind(jnp.take(send_set, ahead, axis=0), "rep", shift))
        got_labels.append(from_behind(jnp.take(send_labels, ahead, axis=0), "rep", shift))
    got_set = jnp.stack(got_set)
    got_labels = jnp.stack(got_labels)
    slots = groups * CAP
    contact_set = got_set.reshape(slots, B, B)
    got_labels = got_labels.reshape(slots, 2)
    near_index = got_labels[:, 0]
    far_index = got_labels[:, 1]
    nodes = rhs.shape[0]
    blocks = jnp.arange(nodes, dtype=jnp.int32)[None, :]
    near_collect = (near_index[:, None] == blocks).astype(jnp.float32)
    far_collect = (far_index[:, None] == blocks).astype(jnp.float32)
    mirror_onehot = (off_cols.reshape(-1)[:, None] == blocks).astype(jnp.float32)
    tables = (
        mirror_onehot.astype(jnp.bfloat16),
        mirror_onehot.astype(jnp.bfloat16),
        near_collect,
        far_collect,
        near_collect.astype(jnp.bfloat16),
        far_collect.astype(jnp.bfloat16),
    )
    link_tile = link_tiles[0]
    scale = precond[:, None, :]
    solution = jnp.zeros_like(rhs)
    residual = rhs
    preconditioned = scale * residual
    direction = preconditioned
    for step in range(ITERS):
        image = apply_operator(direction, diag_tiles, off_tiles, link_tile, contact_set, tables)
        parts = [
            jnp.sum(direction * image, axis=(0, 2)),
            jnp.sum(residual * preconditioned, axis=(0, 2)),
        ]
        if step < ITERS - 1:
            parts.append(jnp.sum(preconditioned * image, axis=(0, 2)))
            parts.append(jnp.sum(image * (scale * image), axis=(0, 2)))
        sums = total(jnp.stack(parts))
        curve, res_dot = sums[0], sums[1]
        alpha = res_dot / curve
        solution = solution + alpha[None, :, None] * direction
        residual = residual - alpha[None, :, None] * image
        if step < ITERS - 1:
            preconditioned = scale * residual
            next_dot = res_dot - 2.0 * alpha * sums[2] + alpha * alpha * sums[3]
            direction = preconditioned + (next_dot / res_dot)[None, :, None] * direction
    return (solution, residual)


def solution(mesh):
    in_specs = (
        P(("dom", "rep"), None, None),
        P(("dom", "rep"), None),
        P(("dom", "rep"), None, None),
        P(("dom", "rep"), None, None, None),
        P(("dom", "rep"), None),
        P(("dom", "rep"), None, None),
        P(("dom", "rep"), None, None),
        P(("dom", "rep"), None),
        P(("dom", "rep")),
        P(("dom", "rep")),
    )
    out_specs = (P(("dom", "rep"), None, None), P(("dom", "rep"), None, None))
    return jax.shard_map(body, mesh=mesh, in_specs=in_specs, out_specs=out_specs, check_vma=False)
```

```python
import jax
import jax.numpy as jnp
from jax import lax
from jax.sharding import PartitionSpec as P

B = 128
ITERS = 4
CAP = 8


def from_behind(value, axis, steps):
    count = lax.axis_size(axis)
    pairs = [(source, (source + steps) % count) for source in range(count)]
    return lax.ppermute(value, axis, pairs)


def partner(value, axis, distance):
    return lax.ppermute(value, axis, [(i, i ^ 1 << distance) for i in range(lax.axis_size(axis))])


def total(value):
    count = lax.axis_size("dom") * lax.axis_size("rep")
    spread = jnp.broadcast_to(value[None], (count,) + value.shape)
    gathered = lax.all_to_all(spread, ("dom", "rep"), 0, 0, tiled=True)
    return jnp.sum(gathered, axis=0)


def early_stiffness(rounded, diag_tiles, off_tiles, cols_onehot):
    result = jnp.einsum("nrk,nkj->nrj", rounded, diag_tiles, preferred_element_type=jnp.float32)
    picked = jnp.einsum(
        "pn,nrk->prk", cols_onehot, rounded, preferred_element_type=jnp.float32
    ).astype(jnp.bfloat16)
    picked = picked.reshape(off_tiles.shape[0], off_tiles.shape[1], rounded.shape[1], rounded.shape[2])
    return result + jnp.einsum(
        "nmrk,nmkj->nrj", picked, off_tiles, preferred_element_type=jnp.float32
    )


def mirror_stiffness(rounded, off_tiles, mirror_onehot):
    nodes = rounded.shape[0]
    chosen = mirror_onehot.reshape(nodes, off_tiles.shape[1], nodes)
    spread = chosen[:, :, :, None, None] * rounded[:, None, None, :, :]
    return jnp.einsum("nmirk,nmjk->irj", spread, off_tiles, preferred_element_type=jnp.float32)


def apply_operator(vector, diag_tiles, off_tiles, link_tile, contact_set, tables):
    cols_onehot, mirror_onehot, near_onehot, far_onehot, near_pick, far_pick = tables
    nodes = vector.shape[0]
    rounded = vector.astype(jnp.bfloat16)
    before = from_behind(rounded[nodes - 1], "rep", 1)
    other = partner(rounded, "dom", 0).astype(vector.dtype)
    near = jnp.einsum("sn,nrk->srk", near_onehot, vector, precision=lax.Precision.HIGHEST)
    far = jnp.einsum("sn,nrk->srk", far_onehot, other, precision=lax.Precision.HIGHEST)
    difference = (near - far).astype(jnp.bfloat16)
    multiplier = jnp.einsum(
        "srk,skj->srj", difference, contact_set, preferred_element_type=jnp.float32
    ).astype(jnp.bfloat16)
    spread = far_pick[:, :, None, None] * multiplier[:, None, :, :]
    far_sum = jnp.einsum("snrj,skj->nrk", spread, contact_set, preferred_element_type=jnp.float32)
    early = early_stiffness(rounded, diag_tiles, off_tiles, cols_onehot)
    far_sum, rounded, multiplier = lax.optimization_barrier(
        (far_sum.astype(jnp.bfloat16), rounded, multiplier)
    )
    far_terms = partner(far_sum, "dom", 0).astype(jnp.float32)
    back_term = lax.dot_general(
        rounded[0], link_tile, (((1,), (1,)), ((), ())), preferred_element_type=jnp.float32
    )
    after = from_behind(back_term, "rep", -1)
    result = early + mirror_stiffness(rounded, off_tiles, mirror_onehot)
    first_add = jnp.dot(before, link_tile, preferred_element_type=jnp.float32)
    ends = jnp.concatenate(
        [first_add[None], jnp.zeros((nodes - 2,) + first_add.shape, jnp.float32), after[None]]
    )
    result = result + ends
    near_spread = near_pick[:, :, None, None] * multiplier[:, None, :, :]
    result = result + jnp.einsum(
        "snrj,skj->nrk", near_spread, contact_set, preferred_element_type=jnp.float32
    )
    return result - far_terms


def body(
    rhs,
    precond,
    diag_tiles,
    off_tiles,
    off_cols,
    link_tiles,
    contact_tiles,
    contact_owner,
    contact_anode,
    contact_bnode,
):
    groups = lax.axis_size("rep")
    target = contact_owner[:, 0]
    order = jnp.arange(target.shape[0], dtype=jnp.int32)
    earlier = (target[None, :] == target[:, None]) & (order[None, :] < order[:, None])
    itself = jnp.where(order[None, :] == order[:, None], target[:, None] * CAP, 0)
    slot_of = jnp.sum(earlier.astype(jnp.int32) + itself, axis=1)
    pick = slot_of[None, :] == jnp.arange(groups * CAP, dtype=jnp.int32)[:, None]
    send_set = jnp.einsum(
        "sc,cij->sij", pick.astype(jnp.bfloat16), contact_tiles, preferred_element_type=jnp.float32
    ).astype(jnp.bfloat16).reshape(groups, CAP, B, B)
    labels = jnp.stack([contact_anode, contact_bnode], axis=1)
    send_labels = jnp.sum(
        jnp.where(pick[:, :, None], labels[None, :, :], 0), axis=1
    ).reshape(groups, CAP, 2)
    lane = lax.axis_index("rep")
    got_set = [jnp.take(send_set, lane, axis=0)]
    got_labels = [jnp.take(send_labels, lane, axis=0)]
    for shift in range(1, groups):
        ahead = (lane + shift) % groups
        got_set.append(from_behind(jnp.take(send_set, ahead, axis=0), "rep", shift))
        got_labels.append(from_behind(jnp.take(send_labels, ahead, axis=0), "rep", shift))
    got_set = jnp.stack(got_set)
    got_labels = jnp.stack(got_labels)
    slots = groups * CAP
    contact_set = got_set.reshape(slots, B, B)
    got_labels = got_labels.reshape(slots, 2)
    near_index = got_labels[:, 0]
    far_index = got_labels[:, 1]
    nodes = rhs.shape[0]
    blocks = jnp.arange(nodes, dtype=jnp.int32)[None, :]
    near_collect = (near_index[:, None] == blocks).astype(jnp.float32)
    far_collect = (far_index[:, None] == blocks).astype(jnp.float32)
    mirror_onehot = (off_cols.reshape(-1)[:, None] == blocks).astype(jnp.float32)
    tables = (
        mirror_onehot.astype(jnp.bfloat16),
        mirror_onehot.astype(jnp.bfloat16),
        near_collect,
        far_collect,
        near_collect.astype(jnp.bfloat16),
        far_collect.astype(jnp.bfloat16),
    )
    link_tile = link_tiles[0]
    scale = precond[:, None, :]
    solution = jnp.zeros_like(rhs)
    residual = rhs
    preconditioned = scale * residual
    direction = preconditioned
    for step in range(ITERS):
        image = apply_operator(direction, diag_tiles, off_tiles, link_tile, contact_set, tables)
        parts = [
            jnp.sum(direction * image, axis=(0, 2)),
            jnp.sum(residual * preconditioned, axis=(0, 2)),
        ]
        if step < ITERS - 1:
            parts.append(jnp.sum(preconditioned * image, axis=(0, 2)))
            parts.append(jnp.sum(image * (scale * image), axis=(0, 2)))
        sums = total(jnp.stack(parts))
        curve, res_dot = sums[0], sums[1]
        alpha = res_dot / curve
        solution = solution + alpha[None, :, None] * direction
        residual = residual - alpha[None, :, None] * image
        if step < ITERS - 1:
            preconditioned = scale * residual
            next_dot = res_dot - 2.0 * alpha * sums[2] + alpha * alpha * sums[3]
            direction = preconditioned + (next_dot / res_dot)[None, :, None] * direction
    return (solution, residual)


def solution(mesh):
    in_specs = (
        P(("dom", "rep"), None, None),
        P(("dom", "rep"), None),
        P(("dom", "rep"), None, None),
        P(("dom", "rep"), None, None, None),
        P(("dom", "rep"), None),
        P(("dom", "rep"), None, None),
        P(("dom", "rep"), None, None),
        P(("dom", "rep"), None),
        P(("dom", "rep")),
        P(("dom", "rep")),
    )
    out_specs = (P(("dom", "rep"), None, None), P(("dom", "rep"), None, None))
    return jax.shard_map(body, mesh=mesh, in_specs=in_specs, out_specs=out_specs, check_vma=False)
```

```python
import jax
import jax.numpy as jnp
from jax import lax
from jax.sharding import PartitionSpec as P

B = 128
ITERS = 4
CAP = 8


def from_behind(value, axis, steps):
    count = lax.axis_size(axis)
    pairs = [(source, (source + steps) % count) for source in range(count)]
    return lax.ppermute(value, axis, pairs)


def partner(value, axis, distance):
    return lax.ppermute(value, axis, [(i, i ^ 1 << distance) for i in range(lax.axis_size(axis))])


def total(value):
    count = lax.axis_size("dom") * lax.axis_size("rep")
    spread = jnp.broadcast_to(value[None], (count,) + value.shape)
    gathered = lax.all_to_all(spread, ("dom", "rep"), 0, 0, tiled=True)
    return jnp.sum(gathered, axis=0)


def local_stiffness(rounded, diag_tiles, off_tiles, cols_onehot, mirror_onehot):
    result = jnp.einsum("nrk,nkj->nrj", rounded, diag_tiles, preferred_element_type=jnp.float32)
    count = rounded.shape[0]
    chosen = cols_onehot.reshape(count, off_tiles.shape[1], count)
    picked = chosen[:, :, :, None, None] * rounded[None, None, :, :, :]
    result = result + jnp.einsum(
        "nmirk,nmkj->nrj", picked, off_tiles, preferred_element_type=jnp.float32
    )
    nodes = rounded.shape[0]
    chosen = mirror_onehot.reshape(nodes, off_tiles.shape[1], nodes)
    spread = chosen[:, :, :, None, None] * rounded[:, None, None, :, :]
    return result + jnp.einsum(
        "nmirk,nmjk->irj", spread, off_tiles, preferred_element_type=jnp.float32
    )


def apply_operator(vector, diag_tiles, off_tiles, link_tile, contact_set, tables):
    cols_onehot, mirror_onehot, near_onehot, far_onehot, near_pick, far_pick = tables
    nodes = vector.shape[0]
    rounded = vector.astype(jnp.bfloat16)
    before = from_behind(rounded[nodes - 1], "rep", 1)
    other = partner(rounded, "dom", 0).astype(vector.dtype)
    near = jnp.einsum("sn,nrk->srk", near_onehot, vector, precision=lax.Precision.HIGHEST)
    far = jnp.einsum("sn,nrk->srk", far_onehot, other, precision=lax.Precision.HIGHEST)
    difference = (near - far).astype(jnp.bfloat16)
    multiplier = jnp.einsum(
        "srk,skj->srj", difference, contact_set, preferred_element_type=jnp.float32
    ).astype(jnp.bfloat16)
    spread = far_pick[:, :, None, None] * multiplier[:, None, :, :]
    far_sum = jnp.einsum("snrj,skj->nrk", spread, contact_set, preferred_element_type=jnp.float32)
    far_sum, rounded, multiplier = lax.optimization_barrier(
        (far_sum.astype(jnp.bfloat16), rounded, multiplier)
    )
    far_terms = partner(far_sum, "dom", 0).astype(jnp.float32)
    back_term = lax.dot_general(
        rounded[0], link_tile, (((1,), (1,)), ((), ())), preferred_element_type=jnp.float32
    )
    after = from_behind(back_term, "rep", -1)
    result = local_stiffness(rounded, diag_tiles, off_tiles, cols_onehot, mirror_onehot)
    first_add = jnp.dot(before, link_tile, preferred_element_type=jnp.float32)
    ends = jnp.concatenate(
        [first_add[None], jnp.zeros((nodes - 2,) + first_add.shape, jnp.float32), after[None]]
    )
    result = result + ends
    near_spread = near_pick[:, :, None, None] * multiplier[:, None, :, :]
    result = result + jnp.einsum(
        "snrj,skj->nrk", near_spread, contact_set, preferred_element_type=jnp.float32
    )
    return result - far_terms


def body(
    rhs,
    precond,
    diag_tiles,
    off_tiles,
    off_cols,
    link_tiles,
    contact_tiles,
    contact_owner,
    contact_anode,
    contact_bnode,
):
    groups = lax.axis_size("rep")
    target = contact_owner[:, 0]
    order = jnp.arange(target.shape[0], dtype=jnp.int32)
    earlier = (target[None, :] == target[:, None]) & (order[None, :] < order[:, None])
    itself = jnp.where(order[None, :] == order[:, None], target[:, None] * CAP, 0)
    slot_of = jnp.sum(earlier.astype(jnp.int32) + itself, axis=1)
    pick = slot_of[None, :] == jnp.arange(groups * CAP, dtype=jnp.int32)[:, None]
    send_set = jnp.einsum(
        "sc,cij->sij", pick.astype(jnp.bfloat16), contact_tiles, preferred_element_type=jnp.float32
    ).astype(jnp.bfloat16).reshape(groups, CAP, B, B)
    labels = jnp.stack([contact_anode, contact_bnode], axis=1)
    send_labels = jnp.sum(
        jnp.where(pick[:, :, None], labels[None, :, :], 0), axis=1
    ).reshape(groups, CAP, 2)
    lane = lax.axis_index("rep")
    got_set = [jnp.take(send_set, lane, axis=0)]
    got_labels = [jnp.take(send_labels, lane, axis=0)]
    for shift in range(1, groups):
        ahead = (lane + shift) % groups
        got_set.append(from_behind(jnp.take(send_set, ahead, axis=0), "rep", shift))
        got_labels.append(from_behind(jnp.take(send_labels, ahead, axis=0), "rep", shift))
    got_set = jnp.stack(got_set)
    got_labels = jnp.stack(got_labels)
    slots = groups * CAP
    contact_set = got_set.reshape(slots, B, B)
    got_labels = got_labels.reshape(slots, 2)
    near_index = got_labels[:, 0]
    far_index = got_labels[:, 1]
    nodes = rhs.shape[0]
    blocks = jnp.arange(nodes, dtype=jnp.int32)[None, :]
    near_collect = (near_index[:, None] == blocks).astype(jnp.float32)
    far_collect = (far_index[:, None] == blocks).astype(jnp.float32)
    mirror_onehot = (off_cols.reshape(-1)[:, None] == blocks).astype(jnp.float32)
    tables = (
        mirror_onehot.astype(jnp.bfloat16),
        mirror_onehot.astype(jnp.bfloat16),
        near_collect,
        far_collect,
        near_collect.astype(jnp.bfloat16),
        far_collect.astype(jnp.bfloat16),
    )
    link_tile = link_tiles[0]
    scale = precond[:, None, :]
    solution = jnp.zeros_like(rhs)
    residual = rhs
    preconditioned = scale * residual
    direction = preconditioned
    for step in range(ITERS):
        image = apply_operator(direction, diag_tiles, off_tiles, link_tile, contact_set, tables)
        parts = [
            jnp.sum(direction * image, axis=(0, 2)),
            jnp.sum(residual * preconditioned, axis=(0, 2)),
        ]
        if step < ITERS - 1:
            parts.append(jnp.sum(preconditioned * image, axis=(0, 2)))
            parts.append(jnp.sum(image * (scale * image), axis=(0, 2)))
        sums = total(jnp.stack(parts))
        curve, res_dot = sums[0], sums[1]
        alpha = res_dot / curve
        solution = solution + alpha[None, :, None] * direction
        residual = residual - alpha[None, :, None] * image
        if step < ITERS - 1:
            preconditioned = scale * residual
            next_dot = res_dot - 2.0 * alpha * sums[2] + alpha * alpha * sums[3]
            direction = preconditioned + (next_dot / res_dot)[None, :, None] * direction
    return (solution, residual)


def solution(mesh):
    in_specs = (
        P(("dom", "rep"), None, None),
        P(("dom", "rep"), None),
        P(("dom", "rep"), None, None),
        P(("dom", "rep"), None, None, None),
        P(("dom", "rep"), None),
        P(("dom", "rep"), None, None),
        P(("dom", "rep"), None, None),
        P(("dom", "rep"), None),
        P(("dom", "rep")),
        P(("dom", "rep")),
    )
    out_specs = (P(("dom", "rep"), None, None), P(("dom", "rep"), None, None))
    return jax.shard_map(body, mesh=mesh, in_specs=in_specs, out_specs=out_specs, check_vma=False)
```
